32 devices in a mesh: layer: 4 (over y, x), slab: 8 (over z, core).
Axes of the slice: x: 2, y: 2, z: 4, core: 2. Of those that a mesh axis runs over, the one named last changes fastest.
Arguments:
- labels: int32 [8192, 2048], P(('layer', 'slab')), parts along dimension 0, may hold values from 0 to 3
Outputs:
- q_panel: float32 [2, 2048, 20402], P(None, ('layer', 'slab')), parts along dimension 1
The draws below stay inside these ranges and needn't reach their ends.
There are 4 independent parts, one for each index of `layer`. The reference program is written for one: setup_inputs(seed, part) draws one part's arguments, and reference() takes and returns one part's arrays. A program takes and returns all parts, laid end to end along the dimension named above; each array names one. Nothing has to cross between parts.
All inputs are finite; a program needn't handle non-finite values.
Results may differ from the reference program's by a relative error of at most 0.0003.
Values sent between devices are 32-bit elements; how exact they have to be, the bound alone decides.
No kernel may reach another device: no remote copies, remote signals or barrier semaphores. Data moves between devices by JAX's collectives and lax.ppermute only.
A program may use at most 192 MiB of HBM per device.

```python
import jax
import jax.numpy as jnp
from jax import lax

NMAP = 2048
HARM = 101
ROWS_DEV = 64
KEEP = 201
ORDERS = 10201
N_SLAB = 8


def draw_labels(key, part):
    key_rows, key_cols, key_table = jax.random.split(key, 3)
    cut_count = max(NMAP // 24, 4)
    row_cuts = jax.random.randint(key_rows, (cut_count,), 0, NMAP)
    col_cuts = jax.random.randint(key_cols, (cut_count,), 0, NMAP)
    places = jnp.arange(NMAP, dtype=jnp.int32)
    row_block = jnp.sum((places[:, None] >= row_cuts[None, :]).astype(jnp.int32), axis=1)
    col_block = jnp.sum((places[:, None] >= col_cuts[None, :]).astype(jnp.int32), axis=1)
    table = jax.random.randint(key_table, (cut_count + 1, cut_count + 1), 0, 4)
    labels = table[row_block[:, None], col_block[None, :]]
    labels = labels.at[0, 0].set(3).at[0, 1].set(0)
    return labels.astype(jnp.int32)


def setup_inputs(seed: int = 0, part: int = 0) -> dict:
    keys = jax.random.split(jax.random.key(seed), 2)
    part_keys = jax.random.split(jax.random.fold_in(keys[1], part), 2)
    return {
        "labels": draw_labels(jax.random.fold_in(jax.random.fold_in(keys[1], part), 71), part),
    }


PERMITS = (1.0, 2.1, 4.0, 12.1)

def permittivity(labels):
    total = jnp.zeros(labels.shape, jnp.float32)
    for index_value in range(4):
        total = total + jnp.where(labels == index_value, jnp.float32(PERMITS[index_value]), jnp.float32(0.0))
    return total

def smooth_all(field_in):
    return (4.0 * field_in + jnp.roll(field_in, 1, 0) + jnp.roll(field_in, -1, 0) + jnp.roll(field_in, 1, 1) + jnp.roll(field_in, -1, 1)) / 8.0

def field_stack(labels):
    permit = permittivity(labels)
    smooth = permit
    for sweep_index in range(3):
        smooth = smooth_all(smooth)
    grad_x = (jnp.roll(smooth, -1, 0) - jnp.roll(smooth, 1, 0)) / 2.0
    grad_y = (jnp.roll(smooth, -1, 1) - jnp.roll(smooth, 1, 1)) / 2.0
    scale = jnp.sqrt(grad_x * grad_x + grad_y * grad_y + 1.0)
    normal_x = grad_x / scale
    normal_y = grad_y / scale
    inverse = 1.0 / permit
    contrast = permit - inverse
    return jnp.stack([permit, contrast * normal_x * normal_x, contrast * normal_x * normal_y, contrast * normal_y * normal_y])

def build_rows(coefficients, window_rows, spacing):
    flipped = coefficients[:, :, ::-1, ::-1]
    centre = (HARM - 1) // 2
    order_count = HARM * HARM

    def one_row(row_index):
        lower_half = row_index % 2
        order_index = row_index // 2 * spacing
        first_index = order_index // HARM
        second = order_index % HARM
        zero_start = jnp.zeros((), jnp.int32)
        window = lax.dynamic_slice(flipped, (zero_start, zero_start, (HARM - 1 - first_index).astype(jnp.int32), (HARM - 1 - second).astype(jnp.int32)), (2, 4, HARM, HARM))
        toeplitz = window.reshape(2, 4, order_count)
        kx_row = 0.3 + 0.02 * (first_index - centre).astype(jnp.float32)
        ky_row = 0.2 + 0.02 * (second - centre).astype(jnp.float32)
        diag_real = (jnp.arange(order_count, dtype=jnp.int32) == order_index).astype(jnp.float32)
        diag_pair = jnp.stack([diag_real, jnp.zeros_like(diag_real)])
        top_left = kx_row * ky_row * diag_pair + toeplitz[:, 2]
        top_right = toeplitz[:, 0] - toeplitz[:, 3] - kx_row * kx_row * diag_pair
        low_left = ky_row * ky_row * diag_pair - toeplitz[:, 0] + toeplitz[:, 1]
        low_right = -toeplitz[:, 2] - kx_row * ky_row * diag_pair
        upper_row = jnp.concatenate([top_left, top_right], axis=1)
        lower_row = jnp.concatenate([low_left, low_right], axis=1)
        return jnp.where(lower_half == 1, lower_row, upper_row)
    return jax.vmap(one_row, out_axes=1)(window_rows)

def reference(labels):
    fields = field_stack(labels)
    spectra = jnp.fft.fft2(fields, axes=(1, 2))
    picks = (jnp.arange(KEEP) - (HARM - 1)) % NMAP
    picked = spectra[:, picks][:, :, picks] / float(NMAP * NMAP)
    coefficients = jnp.stack([jnp.real(picked), jnp.imag(picked)]).astype(jnp.float32)
    window_total = ROWS_DEV * N_SLAB
    spacing = ORDERS // (window_total // 2)
    all_rows = jnp.arange(window_total, dtype=jnp.int32).reshape(N_SLAB, ROWS_DEV)
    blocks = lax.map(lambda block_rows: build_rows(coefficients, block_rows, spacing), all_rows)
    return jnp.transpose(blocks, (1, 0, 2, 3)).reshape(2, window_total, 2 * ORDERS)
```

```python
import functools
import math

import jax
import jax.numpy as jnp
from jax import lax
from jax.experimental import pallas as pl
from jax.experimental.pallas import tpu as pltpu
from jax.sharding import PartitionSpec as P

HARM = 101
ROWS_DEV = 64
KEEP = 201
ORDERS = 10201
BLOCK_ROWS = 8
LANES = 128


PERMITS = (1.0, 2.1, 4.0, 12.1)


def extended_2(block, sides, width):
    for axis, dim in sides:
        count = lax.axis_size(axis)
        forward = [(i, i + 1) for i in range(count - 1)]
        forward.append((count - 1, 0))
        backward = [(target, source) for source, target in forward]
        low = lax.ppermute(
            lax.slice_in_dim(block, block.shape[dim] - width, None, axis=dim), axis, forward
        )
        high = lax.ppermute(lax.slice_in_dim(block, 0, width, axis=dim), axis, backward)
        block = jnp.concatenate([low, block, high], axis=dim)
    return block


def permittivity(labels):
    total = jnp.zeros(labels.shape, jnp.float32)
    for index_value in range(4):
        total = total + jnp.where(
            labels == index_value, jnp.float32(PERMITS[index_value]), jnp.float32(0.0)
        )
    return total


def smooth_once(extended):
    middle = extended[1:-1]
    return (
        4.0 * middle
        + extended[:-2]
        + extended[2:]
        + jnp.roll(middle, 1, 1)
        + jnp.roll(middle, -1, 1)
    ) / 8.0


def gradient(extended):
    middle = extended[1:-1]
    grad_x = (extended[2:] - extended[:-2]) / 2.0
    grad_y = (jnp.roll(middle, -1, 1) - jnp.roll(middle, 1, 1)) / 2.0
    return (grad_x, grad_y)


def rim_rows(field_in):
    return extended_2(field_in, (("slab", 0),), 1)


def row_transform(spectra_in, positions, frequency, map_width):
    phases = frequency[:, None] * positions[None, :] % map_width
    angles = phases.astype(jnp.float32) * (2.0 * math.pi / map_width)
    table = jnp.stack([jnp.cos(angles), jnp.sin(angles)])
    products = jnp.einsum("smx,kxcn->skmcn", table, spectra_in, precision=lax.Precision.HIGHEST)
    real_part = products[0, :, :, 0] + products[1, :, :, 1]
    imag_part = products[0, :, :, 1] - products[1, :, :, 0]
    return jnp.stack([real_part, imag_part])


def chunk_segments(total, half):
    chunks = []
    for start in range(0, total, LANES):
        width = min(LANES, total - start)
        runs = []
        for lane in range(width):
            flat = start + lane
            h, j = divmod(flat, half)
            u, v = divmod(j, HARM)
            if not runs or runs[-1][0] != h or runs[-1][1] != u:
                runs.append((h, u, lane, v))
        chunks.append((start, width, runs))
    return chunks


def assemble_kernel(a0_ref, b0_ref, first_ref, second_ref, dval_ref, fl_ref, o_ref, z_ref):
    s = pl.program_id(0)
    rb = pl.program_id(1)
    win = z_ref.shape[1] // BLOCK_ROWS
    span = win + BLOCK_ROWS
    row_iota = lax.broadcasted_iota(jnp.int32, (win, LANES), 0)
    lane_iota = lax.broadcasted_iota(jnp.int32, (win, LANES), 1)
    for rr in range(BLOCK_ROWS):
        row = rb * BLOCK_ROWS + rr
        a0 = a0_ref[row]
        b0 = b0_ref[row]
        first = first_ref[row]
        second = second_ref[row]
        shift = (LANES - b0) % LANES
        base = pl.multiple_of(a0 // BLOCK_ROWS * BLOCK_ROWS, BLOCK_ROWS)
        lift = (span - a0 % BLOCK_ROWS) % span
        spot = (row_iota == first) & (lane_iota == second)
        wrap = lane_iota + b0 < LANES
        for h in range(2):
            combo = 2 * (rr % 2) + h
            x_lo = fl_ref[0, combo, pl.ds(base, span), pl.ds(0, LANES)]
            x_hi = fl_ref[0, combo, pl.ds(base, span), pl.ds(LANES, LANES)]
            x_lo = pltpu.roll(x_lo, lift, 0)[:win]
            x_hi = pltpu.roll(x_hi, lift, 0)[:win]
            x = jnp.where(wrap, pltpu.roll(x_lo, shift, 1), pltpu.roll(x_hi, shift, 1))
            d = jnp.where(s == 0, dval_ref[h, row], jnp.float32(0.0))
            x = x + jnp.where(spot, d, jnp.float32(0.0))
            z_ref[h, pl.ds(rr, win, stride=BLOCK_ROWS), :] = x
    lane = lax.broadcasted_iota(jnp.int32, (BLOCK_ROWS, LANES), 1)
    for start, width, runs in chunk_segments(o_ref.shape[2], o_ref.shape[2] // 2):
        acc = None
        for h, u, l0, v0 in runs:
            src = z_ref[h, pl.ds(u * BLOCK_ROWS, BLOCK_ROWS), :]
            sh = (l0 - v0) % LANES
            if sh:
                src = pltpu.roll(src, sh, 1)
            acc = src if acc is None else jnp.where(lane >= l0, src, acc)
        if width < LANES:
            acc = acc[:, :width]
        o_ref[0, :, pl.ds(start, width)] = acc


def assemble(a0, b0, first, second, dvals, tables, rows):
    win = 104
    n_blocks = rows // BLOCK_ROWS
    total = 2 * ORDERS
    grid_spec = pltpu.PrefetchScalarGridSpec(
        num_scalar_prefetch=4,
        grid=(2, n_blocks),
        in_specs=[
            pl.BlockSpec(memory_space=pltpu.SMEM),
            pl.BlockSpec((1,) + tables.shape[1:], lambda s, rb, *_: (s, 0, 0, 0)),
        ],
        out_specs=pl.BlockSpec((1, BLOCK_ROWS, total), lambda s, rb, *_: (s, rb, 0)),
        scratch_shapes=[pltpu.VMEM((2, win * BLOCK_ROWS, LANES), jnp.float32)],
    )
    return pl.pallas_call(
        assemble_kernel,
        grid_spec=grid_spec,
        out_shape=jax.ShapeDtypeStruct((2, rows, total), jnp.float32),
        compiler_params=pltpu.CompilerParams(dimension_semantics=("arbitrary", "arbitrary")),
    )(a0, b0, first, second, dvals, tables)


def shards(labels):
    slab_rows = labels.shape[0]
    map_width = labels.shape[1]
    devices = lax.axis_size("slab")
    my_index = lax.axis_index("slab")
    permit = permittivity(labels)
    smooth = permit
    for sweep_index in range(3):
        smooth = smooth_once(rim_rows(smooth))
    grad_x, grad_y = gradient(rim_rows(smooth))
    scale = jnp.sqrt(grad_x * grad_x + grad_y * grad_y + 1.0)
    normal_x = grad_x / scale
    normal_y = grad_y / scale
    inverse = 1.0 / permit
    contrast = permit - inverse
    fields = jnp.stack(
        [
            permit,
            contrast * normal_x * normal_x,
            contrast * normal_x * normal_y,
            contrast * normal_y * normal_y,
        ]
    )
    padded_keep = -(-KEEP // devices) * devices
    frequency = (HARM - 1) - jnp.arange(padded_keep, dtype=jnp.int32)
    columns = jnp.arange(map_width, dtype=jnp.int32)
    phases = columns[:, None] * frequency[None, :] % map_width
    angles = phases.astype(jnp.float32) * (2.0 * math.pi / map_width)
    col_table = jnp.stack([jnp.cos(angles), -jnp.sin(angles)], axis=1)
    half_spectra = jnp.einsum("kxy,ycn->kxcn", fields, col_table, precision=lax.Precision.HIGHEST)
    my_positions = my_index * slab_rows + jnp.arange(slab_rows, dtype=jnp.int32)
    partial_value = row_transform(half_spectra, my_positions, frequency, map_width)
    summed = lax.psum(partial_value, "slab")
    coef = summed / float(map_width * map_width)
    tables = jnp.stack(
        [coef[:, 2], coef[:, 0] - coef[:, 3], coef[:, 1] - coef[:, 0], -coef[:, 2]], axis=1
    )
    tables = jnp.pad(tables, ((0, 0), (0, 0), (0, 0), (0, 2 * LANES - padded_keep)))
    rows = ROWS_DEV
    spacing = ORDERS // (rows * devices // 2)
    window_rows = my_index * rows + jnp.arange(rows, dtype=jnp.int32)
    order_index = window_rows // 2 * spacing
    first = order_index // HARM
    second = order_index % HARM
    centre = (HARM - 1) // 2
    kx = 0.3 + 0.02 * (first - centre).astype(jnp.float32)
    ky = 0.2 + 0.02 * (second - centre).astype(jnp.float32)
    lower = window_rows % 2 == 1
    left = jnp.where(lower, ky * ky, kx * ky)
    right = jnp.where(lower, -(kx * ky), -(kx * kx))
    dvals = jnp.stack([left, right])
    a0 = (HARM - 1) - first
    b0 = (HARM - 1) - second
    return assemble(a0, b0, first, second, dvals, tables, rows)


def solution(mesh):
    placed = (P(("layer", "slab"), None),)
    return jax.shard_map(
        shards,
        mesh=mesh,
        in_specs=placed,
        out_specs=P(None, ("layer", "slab"), None),
        check_vma=False,
    )
```

```python
import functools
import math

import jax
import jax.numpy as jnp
from jax import lax
from jax.experimental import pallas as pl
from jax.experimental.pallas import tpu as pltpu
from jax.sharding import PartitionSpec as P

HARM = 101
ROWS_DEV = 64
KEEP = 201
ORDERS = 10201
BLOCK_ROWS = 8
LANES = 128


PERMITS = (1.0, 2.1, 4.0, 12.1)


def extended_2(block, sides, width):
    for axis, dim in sides:
        count = lax.axis_size(axis)
        forward = [(i, i + 1) for i in range(count - 1)]
        forward.append((count - 1, 0))
        backward = [(target, source) for source, target in forward]
        low = lax.ppermute(
            lax.slice_in_dim(block, block.shape[dim] - width, None, axis=dim), axis, forward
        )
        high = lax.ppermute(lax.slice_in_dim(block, 0, width, axis=dim), axis, backward)
        block = jnp.concatenate([low, block, high], axis=dim)
    return block


def permittivity(labels):
    total = jnp.zeros(labels.shape, jnp.float32)
    for index_value in range(4):
        total = total + jnp.where(
            labels == index_value, jnp.float32(PERMITS[index_value]), jnp.float32(0.0)
        )
    return total


def smooth_once(extended):
    middle = extended[1:-1]
    return (
        4.0 * middle
        + extended[:-2]
        + extended[2:]
        + jnp.roll(middle, 1, 1)
        + jnp.roll(middle, -1, 1)
    ) / 8.0


def gradient(extended):
    middle = extended[1:-1]
    grad_x = (extended[2:] - extended[:-2]) / 2.0
    grad_y = (jnp.roll(middle, -1, 1) - jnp.roll(middle, 1, 1)) / 2.0
    return (grad_x, grad_y)


def rim_rows(field_in):
    return extended_2(field_in, (("slab", 0),), 1)


def row_transform(spectra_in, positions, frequency, map_width):
    phases = frequency[:, None] * positions[None, :] % map_width
    angles = phases.astype(jnp.float32) * (2.0 * math.pi / map_width)
    table = jnp.stack([jnp.cos(angles), jnp.sin(angles)])
    products = jnp.einsum("smx,kxcn->skmcn", table, spectra_in, precision=lax.Precision.HIGHEST)
    real_part = products[0, :, :, 0] + products[1, :, :, 1]
    imag_part = products[0, :, :, 1] - products[1, :, :, 0]
    return jnp.stack([real_part, imag_part])


def chunk_segments(total, half):
    chunks = []
    for start in range(0, total, LANES):
        width = min(LANES, total - start)
        runs = []
        for lane in range(width):
            flat = start + lane
            h, j = divmod(flat, half)
            u, v = divmod(j, HARM)
            if not runs or runs[-1][0] != h or runs[-1][1] != u:
                runs.append((h, u, lane, v))
        chunks.append((start, width, runs))
    return chunks


def assemble_kernel(a0_ref, b0_ref, first_ref, second_ref, dval_ref, fl_ref, o_ref, z_ref):
    s = pl.program_id(0)
    rb = pl.program_id(1)
    win = z_ref.shape[1] // BLOCK_ROWS
    span = win + BLOCK_ROWS
    row_iota = lax.broadcasted_iota(jnp.int32, (win, LANES), 0)
    lane_iota = lax.broadcasted_iota(jnp.int32, (win, LANES), 1)
    for rr in range(BLOCK_ROWS):
        row = rb * BLOCK_ROWS + rr
        a0 = a0_ref[row]
        b0 = b0_ref[row]
        first = first_ref[row]
        second = second_ref[row]
        shift = (LANES - b0) % LANES
        base = pl.multiple_of(a0 // BLOCK_ROWS * BLOCK_ROWS, BLOCK_ROWS)
        lift = (span - a0 % BLOCK_ROWS) % span
        spot = (row_iota == first) & (lane_iota == second)
        wrap = lane_iota + b0 < LANES
        for h in range(2):
            combo = 2 * (rr % 2) + h
            x_lo = fl_ref[0, combo, pl.ds(base, span), pl.ds(0, LANES)]
            x_hi = fl_ref[0, combo, pl.ds(base, span), pl.ds(LANES, LANES)]
            x_lo = pltpu.roll(x_lo, lift, 0)[:win]
            x_hi = pltpu.roll(x_hi, lift, 0)[:win]
            x = jnp.where(wrap, pltpu.roll(x_lo, shift, 1), pltpu.roll(x_hi, shift, 1))
            d = jnp.where(s == 0, dval_ref[h, row], jnp.float32(0.0))
            x = x + jnp.where(spot, d, jnp.float32(0.0))
            z_ref[h, pl.ds(rr, win, stride=BLOCK_ROWS), :] = x
    lane = lax.broadcasted_iota(jnp.int32, (BLOCK_ROWS, LANES), 1)
    for start, width, runs in chunk_segments(o_ref.shape[2], o_ref.shape[2] // 2):
        acc = None
        for h, u, l0, v0 in runs:
            src = z_ref[h, pl.ds(u * BLOCK_ROWS, BLOCK_ROWS), :]
            sh = (l0 - v0) % LANES
            if sh:
                src = pltpu.roll(src, sh, 1)
            acc = src if acc is None else jnp.where(lane >= l0, src, acc)
        if width < LANES:
            acc = acc[:, :width]
        o_ref[0, :, pl.ds(start, width)] = acc


def assemble(a0, b0, first, second, dvals, tables, rows):
    win = 104
    n_blocks = rows // BLOCK_ROWS
    total = 2 * ORDERS
    grid_spec = pltpu.PrefetchScalarGridSpec(
        num_scalar_prefetch=4,
        grid=(2, n_blocks),
        in_specs=[
            pl.BlockSpec(memory_space=pltpu.SMEM),
            pl.BlockSpec((1,) + tables.shape[1:], lambda s, rb, *_: (s, 0, 0, 0)),
        ],
        out_specs=pl.BlockSpec((1, BLOCK_ROWS, total), lambda s, rb, *_: (s, rb, 0)),
        scratch_shapes=[pltpu.VMEM((2, win * BLOCK_ROWS, LANES), jnp.float32)],
    )
    return pl.pallas_call(
        assemble_kernel,
        grid_spec=grid_spec,
        out_shape=jax.ShapeDtypeStruct((2, rows, total), jnp.float32),
        compiler_params=pltpu.CompilerParams(dimension_semantics=("arbitrary", "arbitrary")),
    )(a0, b0, first, second, dvals, tables)


def shards(labels):
    slab_rows = labels.shape[0]
    map_width = labels.shape[1]
    devices = lax.axis_size("slab")
    my_index = lax.axis_index("slab")
    permit = permittivity(labels)
    smooth = extended_2(permit, (("slab", 0),), 4)
    for sweep_index in range(3):
        smooth = smooth_once(smooth)
    grad_x, grad_y = gradient(smooth)
    scale = jnp.sqrt(grad_x * grad_x + grad_y * grad_y + 1.0)
    normal_x = grad_x / scale
    normal_y = grad_y / scale
    inverse = 1.0 / permit
    contrast = permit - inverse
    fields = jnp.stack(
        [
            permit,
            contrast * normal_x * normal_x,
            contrast * normal_x * normal_y,
            contrast * normal_y * normal_y,
        ]
    )
    padded_keep = -(-KEEP // devices) * devices
    half_keep = -(-HARM // devices) * devices
    frequency = (HARM - 1) - jnp.arange(padded_keep, dtype=jnp.int32)
    col_frequency = (HARM - 1) - jnp.arange(half_keep, dtype=jnp.int32)
    columns = jnp.arange(map_width, dtype=jnp.int32)
    phases = columns[:, None] * col_frequency[None, :] % map_width
    angles = phases.astype(jnp.float32) * (2.0 * math.pi / map_width)
    col_table = jnp.stack([jnp.cos(angles), -jnp.sin(angles)], axis=1)
    half_spectra = jnp.einsum("kxy,ycn->kxcn", fields, col_table, precision=lax.Precision.HIGHEST)
    my_positions = my_index * slab_rows + jnp.arange(slab_rows, dtype=jnp.int32)
    partial_value = row_transform(half_spectra, my_positions, frequency, map_width)
    summed = lax.psum(partial_value, "slab")
    coef = summed / float(map_width * map_width)
    a_in = jnp.arange(padded_keep, dtype=jnp.int32)
    c_in = jnp.arange(half_keep, dtype=jnp.int32)
    b_out = jnp.arange(2 * LANES, dtype=jnp.int32)
    flip_rows = (a_in[None, :] == (KEEP - 1) - a_in[:, None]).astype(jnp.float32)
    keep_cols = ((c_in[:, None] == b_out[None, :]) & (b_out[None, :] < HARM)).astype(jnp.float32)
    mirror_cols = (
        (c_in[:, None] == (KEEP - 1) - b_out[None, :]) & (b_out[None, :] >= HARM)
    ).astype(jnp.float32)
    sign = jnp.array([1.0, -1.0], jnp.float32)[:, None, None, None]
    direct = jnp.einsum("skac,cb->skab", coef, keep_cols, precision=lax.Precision.HIGHEST)
    mirrored = jnp.einsum(
        "ad,skdc,cb->skab", flip_rows, coef, mirror_cols, precision=lax.Precision.HIGHEST
    )
    full = direct + sign * mirrored
    tables = jnp.stack(
        [full[:, 2], full[:, 0] - full[:, 3], full[:, 1] - full[:, 0], -full[:, 2]], axis=1
    )
    rows = ROWS_DEV
    spacing = ORDERS // (rows * devices // 2)
    window_rows = my_index * rows + jnp.arange(rows, dtype=jnp.int32)
    order_index = window_rows // 2 * spacing
    first = order_index // HARM
    second = order_index % HARM
    centre = (HARM - 1) // 2
    kx = 0.3 + 0.02 * (first - centre).astype(jnp.float32)
    ky = 0.2 + 0.02 * (second - centre).astype(jnp.float32)
    lower = window_rows % 2 == 1
    left = jnp.where(lower, ky * ky, kx * ky)
    right = jnp.where(lower, -(kx * ky), -(kx * kx))
    dvals = jnp.stack([left, right])
    a0 = (HARM - 1) - first
    b0 = (HARM - 1) - second
    return assemble(a0, b0, first, second, dvals, tables, rows)


def solution(mesh):
    placed = (P(("layer", "slab"), None),)
    return jax.shard_map(
        shards,
        mesh=mesh,
        in_specs=placed,
        out_specs=P(None, ("layer", "slab"), None),
        check_vma=False,
    )
```

```python
import functools
import math

import jax
import jax.numpy as jnp
from jax import lax
from jax.experimental import pallas as pl
from jax.experimental.pallas import tpu as pltpu
from jax.sharding import PartitionSpec as P

HARM = 101
ROWS_DEV = 64
KEEP = 201
ORDERS = 10201
BLOCK_ROWS = 8
LANES = 128


PERMITS = (1.0, 2.1, 4.0, 12.1)


def extended_2(block, sides, width):
    for axis, dim in sides:
        count = lax.axis_size(axis)
        forward = [(i, i + 1) for i in range(count - 1)]
        forward.append((count - 1, 0))
        backward = [(target, source) for source, target in forward]
        low = lax.ppermute(
            lax.slice_in_dim(block, block.shape[dim] - width, None, axis=dim), axis, forward
        )
        high = lax.ppermute(lax.slice_in_dim(block, 0, width, axis=dim), axis, backward)
        block = jnp.concatenate([low, block, high], axis=dim)
    return block


def permittivity(labels):
    total = jnp.zeros(labels.shape, jnp.float32)
    for index_value in range(4):
        total = total + jnp.where(
            labels == index_value, jnp.float32(PERMITS[index_value]), jnp.float32(0.0)
        )
    return total


def smooth_once(extended):
    middle = extended[1:-1]
    return (
        4.0 * middle
        + extended[:-2]
        + extended[2:]
        + jnp.roll(middle, 1, 1)
        + jnp.roll(middle, -1, 1)
    ) / 8.0


def gradient(extended):
    middle = extended[1:-1]
    grad_x = (extended[2:] - extended[:-2]) / 2.0
    grad_y = (jnp.roll(middle, -1, 1) - jnp.roll(middle, 1, 1)) / 2.0
    return (grad_x, grad_y)


def rim_rows(field_in):
    return extended_2(field_in, (("slab", 0),), 1)


def row_transform(spectra_in, positions, frequency, map_width):
    phases = frequency[:, None] * positions[None, :] % map_width
    angles = phases.astype(jnp.float32) * (2.0 * math.pi / map_width)
    table = jnp.stack([jnp.cos(angles), jnp.sin(angles)])
    products = jnp.einsum("smx,kxcn->skmcn", table, spectra_in, precision=lax.Precision.HIGHEST)
    real_part = products[0, :, :, 0] + products[1, :, :, 1]
    imag_part = products[0, :, :, 1] - products[1, :, :, 0]
    return jnp.stack([real_part, imag_part])


def chunk_segments(total, half):
    chunks = []
    for start in range(0, total, LANES):
        width = min(LANES, total - start)
        runs = []
        for lane in range(width):
            flat = start + lane
            h, j = divmod(flat, half)
            u, v = divmod(j, HARM)
            if not runs or runs[-1][0] != h or runs[-1][1] != u:
                runs.append((h, u, lane, v))
        chunks.append((start, width, runs))
    return chunks


def assemble_kernel(a0_ref, b0_ref, first_ref, second_ref, dval_ref, fl_ref, o_ref, z_ref):
    s = pl.program_id(0)
    rb = pl.program_id(1)
    win = z_ref.shape[1] // BLOCK_ROWS
    span = win + BLOCK_ROWS
    row_iota = lax.broadcasted_iota(jnp.int32, (win, LANES), 0)
    lane_iota = lax.broadcasted_iota(jnp.int32, (win, LANES), 1)
    for rr in range(BLOCK_ROWS):
        row = rb * BLOCK_ROWS + rr
        a0 = a0_ref[row]
        b0 = b0_ref[row]
        first = first_ref[row]
        second = second_ref[row]
        shift = (LANES - b0) % LANES
        base = pl.multiple_of(a0 // BLOCK_ROWS * BLOCK_ROWS, BLOCK_ROWS)
        lift = (span - a0 % BLOCK_ROWS) % span
        spot = (row_iota == first) & (lane_iota == second)
        wrap = lane_iota + b0 < LANES
        for h in range(2):
            combo = 2 * (rr % 2) + h
            x_lo = fl_ref[0, combo, pl.ds(base, span), pl.ds(0, LANES)]
            x_hi = fl_ref[0, combo, pl.ds(base, span), pl.ds(LANES, LANES)]
            x_lo = pltpu.roll(x_lo, lift, 0)[:win]
            x_hi = pltpu.roll(x_hi, lift, 0)[:win]
            x = jnp.where(wrap, pltpu.roll(x_lo, shift, 1), pltpu.roll(x_hi, shift, 1))
            d = jnp.where(s == 0, dval_ref[h, row], jnp.float32(0.0))
            x = x + jnp.where(spot, d, jnp.float32(0.0))
            z_ref[h, pl.ds(rr, win, stride=BLOCK_ROWS), :] = x
    lane = lax.broadcasted_iota(jnp.int32, (BLOCK_ROWS, LANES), 1)
    for start, width, runs in chunk_segments(o_ref.shape[2], o_ref.shape[2] // 2):
        acc = None
        for h, u, l0, v0 in runs:
            src = z_ref[h, pl.ds(u * BLOCK_ROWS, BLOCK_ROWS), :]
            sh = (l0 - v0) % LANES
            if sh:
                src = pltpu.roll(src, sh, 1)
            acc = src if acc is None else jnp.where(lane >= l0, src, acc)
        if width < LANES:
            acc = acc[:, :width]
        o_ref[0, :, pl.ds(start, width)] = acc


def assemble(a0, b0, first, second, dvals, tables, rows):
    win = 104
    n_blocks = rows // BLOCK_ROWS
    total = 2 * ORDERS
    grid_spec = pltpu.PrefetchScalarGridSpec(
        num_scalar_prefetch=4,
        grid=(2, n_blocks),
        in_specs=[
            pl.BlockSpec(memory_space=pltpu.SMEM),
            pl.BlockSpec((1,) + tables.shape[1:], lambda s, rb, *_: (s, 0, 0, 0)),
        ],
        out_specs=pl.BlockSpec((1, BLOCK_ROWS, total), lambda s, rb, *_: (s, rb, 0)),
        scratch_shapes=[pltpu.VMEM((2, win * BLOCK_ROWS, LANES), jnp.float32)],
    )
    return pl.pallas_call(
        assemble_kernel,
        grid_spec=grid_spec,
        out_shape=jax.ShapeDtypeStruct((2, rows, total), jnp.float32),
        compiler_params=pltpu.CompilerParams(dimension_semantics=("arbitrary", "arbitrary")),
    )(a0, b0, first, second, dvals, tables)


def line_sum(partial_value, my_index, devices):
    core = my_index % 2
    pairs = [(i, i ^ 1) for i in range(devices)]
    keep = jnp.where(core == 0, partial_value[0], partial_value[1])
    give = jnp.where(core == 0, partial_value[1], partial_value[0])
    mine = keep + lax.ppermute(give, "slab", pairs)
    right = [(i, i + 2) for i in range(devices - 2)]
    left = [(i + 2, i) for i in range(devices - 2)]
    from_left = jnp.zeros_like(mine)
    from_right = jnp.zeros_like(mine)
    for step in range(devices // 2 - 1):
        from_left, from_right = (
            lax.ppermute(mine + from_left, "slab", right),
            lax.ppermute(mine + from_right, "slab", left),
        )
    total = mine + from_left + from_right
    other = lax.ppermute(total, "slab", pairs)
    return jnp.where(core == 0, jnp.stack([total, other]), jnp.stack([other, total]))


def shards(labels):
    slab_rows = labels.shape[0]
    map_width = labels.shape[1]
    devices = lax.axis_size("slab")
    my_index = lax.axis_index("slab")
    permit = permittivity(labels)
    smooth = extended_2(permit, (("slab", 0),), 4)
    for sweep_index in range(3):
        smooth = smooth_once(smooth)
    grad_x, grad_y = gradient(smooth)
    scale = jnp.sqrt(grad_x * grad_x + grad_y * grad_y + 1.0)
    normal_x = grad_x / scale
    normal_y = grad_y / scale
    inverse = 1.0 / permit
    contrast = permit - inverse
    fields = jnp.stack(
        [
            permit,
            contrast * normal_x * normal_x,
            contrast * normal_x * normal_y,
            contrast * normal_y * normal_y,
        ]
    )
    padded_keep = -(-KEEP // devices) * devices
    half_keep = -(-HARM // devices) * devices
    frequency = (HARM - 1) - jnp.arange(padded_keep, dtype=jnp.int32)
    col_frequency = (HARM - 1) - jnp.arange(half_keep, dtype=jnp.int32)
    columns = jnp.arange(map_width, dtype=jnp.int32)
    phases = columns[:, None] * col_frequency[None, :] % map_width
    angles = phases.astype(jnp.float32) * (2.0 * math.pi / map_width)
    col_table = jnp.stack([jnp.cos(angles), -jnp.sin(angles)], axis=1)
    half_spectra = jnp.einsum("kxy,ycn->kxcn", fields, col_table, precision=lax.Precision.HIGHEST)
    my_positions = my_index * slab_rows + jnp.arange(slab_rows, dtype=jnp.int32)
    partial_value = row_transform(half_spectra, my_positions, frequency, map_width)
    summed = line_sum(partial_value, my_index, devices)
    coef = summed / float(map_width * map_width)
    a_in = jnp.arange(padded_keep, dtype=jnp.int32)
    c_in = jnp.arange(half_keep, dtype=jnp.int32)
    b_out = jnp.arange(2 * LANES, dtype=jnp.int32)
    flip_rows = (a_in[None, :] == (KEEP - 1) - a_in[:, None]).astype(jnp.float32)
    keep_cols = ((c_in[:, None] == b_out[None, :]) & (b_out[None, :] < HARM)).astype(jnp.float32)
    mirror_cols = (
        (c_in[:, None] == (KEEP - 1) - b_out[None, :]) & (b_out[None, :] >= HARM)
    ).astype(jnp.float32)
    sign = jnp.array([1.0, -1.0], jnp.float32)[:, None, None, None]
    direct = jnp.einsum("skac,cb->skab", coef, keep_cols, precision=lax.Precision.HIGHEST)
    mirrored = jnp.einsum(
        "ad,skdc,cb->skab", flip_rows, coef, mirror_cols, precision=lax.Precision.HIGHEST
    )
    full = direct + sign * mirrored
    tables = jnp.stack(
        [full[:, 2], full[:, 0] - full[:, 3], full[:, 1] - full[:, 0], -full[:, 2]], axis=1
    )
    rows = ROWS_DEV
    spacing = ORDERS // (rows * devices // 2)
    window_rows = my_index * rows + jnp.arange(rows, dtype=jnp.int32)
    order_index = window_rows // 2 * spacing
    first = order_index // HARM
    second = order_index % HARM
    centre = (HARM - 1) // 2
    kx = 0.3 + 0.02 * (first - centre).astype(jnp.float32)
    ky = 0.2 + 0.02 * (second - centre).astype(jnp.float32)
    lower = window_rows % 2 == 1
    left = jnp.where(lower, ky * ky, kx * ky)
    right = jnp.where(lower, -(kx * ky), -(kx * kx))
    dvals = jnp.stack([left, right])
    a0 = (HARM - 1) - first
    b0 = (HARM - 1) - second
    return assemble(a0, b0, first, second, dvals, tables, rows)


def solution(mesh):
    placed = (P(("layer", "slab"), None),)
    return jax.shard_map(
        shards,
        mesh=mesh,
        in_specs=placed,
        out_specs=P(None, ("layer", "slab"), None),
        check_vma=False,
    )
```

```python
import functools
import math

import jax
import jax.numpy as jnp
from jax import lax
from jax.experimental import pallas as pl
from jax.experimental.pallas import tpu as pltpu
from jax.sharding import PartitionSpec as P

HARM = 101
ROWS_DEV = 64
KEEP = 201
ORDERS = 10201
BLOCK_ROWS = 8
LANES = 128


PERMITS = (1.0, 2.1, 4.0, 12.1)


def extended_2(block, sides, width):
    for axis, dim in sides:
        count = lax.axis_size(axis)
        forward = [(i, i + 1) for i in range(count - 1)]
        forward.append((count - 1, 0))
        backward = [(target, source) for source, target in forward]
        low = lax.ppermute(
            lax.slice_in_dim(block, block.shape[dim] - width, None, axis=dim), axis, forward
        )
        high = lax.ppermute(lax.slice_in_dim(block, 0, width, axis=dim), axis, backward)
        block = jnp.concatenate([low, block, high], axis=dim)
    return block


def permittivity(labels):
    total = jnp.zeros(labels.shape, jnp.float32)
    for index_value in range(4):
        total = total + jnp.where(
            labels == index_value, jnp.float32(PERMITS[index_value]), jnp.float32(0.0)
        )
    return total


def smooth_once(extended):
    middle = extended[1:-1]
    return (
        4.0 * middle
        + extended[:-2]
        + extended[2:]
        + jnp.roll(middle, 1, 1)
        + jnp.roll(middle, -1, 1)
    ) / 8.0


def gradient(extended):
    middle = extended[1:-1]
    grad_x = (extended[2:] - extended[:-2]) / 2.0
    grad_y = (jnp.roll(middle, -1, 1) - jnp.roll(middle, 1, 1)) / 2.0
    return (grad_x, grad_y)


def rim_rows(field_in):
    return extended_2(field_in, (("slab", 0),), 1)


def row_transform(spectra_in, positions, frequency, map_width):
    phases = frequency[:, None] * positions[None, :] % map_width
    angles = phases.astype(jnp.float32) * (2.0 * math.pi / map_width)
    table = jnp.stack([jnp.cos(angles), jnp.sin(angles)])
    products = jnp.einsum("smx,kxcn->skmcn", table, spectra_in, precision=lax.Precision.HIGH)
    real_part = products[0, :, :, 0] + products[1, :, :, 1]
    imag_part = products[0, :, :, 1] - products[1, :, :, 0]
    return jnp.stack([real_part, imag_part])


def chunk_segments(total, half):
    chunks = []
    for start in range(0, total, LANES):
        width = min(LANES, total - start)
        runs = []
        for lane in range(width):
            flat = start + lane
            h, j = divmod(flat, half)
            u, v = divmod(j, HARM)
            if not runs or runs[-1][0] != h or runs[-1][1] != u:
                runs.append((h, u, lane, v))
        chunks.append((start, width, runs))
    return chunks


def assemble_kernel(a0_ref, b0_ref, first_ref, second_ref, dval_ref, fl_ref, o_ref, z_ref):
    s = pl.program_id(0)
    rb = pl.program_id(1)
    win = z_ref.shape[1] // BLOCK_ROWS
    span = win + BLOCK_ROWS
    row_iota = lax.broadcasted_iota(jnp.int32, (win, LANES), 0)
    lane_iota = lax.broadcasted_iota(jnp.int32, (win, LANES), 1)
    for rr in range(BLOCK_ROWS):
        row = rb * BLOCK_ROWS + rr
        a0 = a0_ref[row]
        b0 = b0_ref[row]
        first = first_ref[row]
        second = second_ref[row]
        shift = (LANES - b0) % LANES
        base = pl.multiple_of(a0 // BLOCK_ROWS * BLOCK_ROWS, BLOCK_ROWS)
        lift = (span - a0 % BLOCK_ROWS) % span
        spot = (row_iota == first) & (lane_iota == second)
        wrap = lane_iota + b0 < LANES
        for h in range(2):
            combo = 2 * (rr % 2) + h
            x_lo = fl_ref[0, combo, pl.ds(base, span), pl.ds(0, LANES)]
            x_hi = fl_ref[0, combo, pl.ds(base, span), pl.ds(LANES, LANES)]
            x_lo = pltpu.roll(x_lo, lift, 0)[:win]
            x_hi = pltpu.roll(x_hi, lift, 0)[:win]
            x = jnp.where(wrap, pltpu.roll(x_lo, shift, 1), pltpu.roll(x_hi, shift, 1))
            d = jnp.where(s == 0, dval_ref[h, row], jnp.float32(0.0))
            x = x + jnp.where(spot, d, jnp.float32(0.0))
            z_ref[h, pl.ds(rr, win, stride=BLOCK_ROWS), :] = x
    lane = lax.broadcasted_iota(jnp.int32, (BLOCK_ROWS, LANES), 1)
    for start, width, runs in chunk_segments(o_ref.shape[2], o_ref.shape[2] // 2):
        acc = None
        for h, u, l0, v0 in runs:
            src = z_ref[h, pl.ds(u * BLOCK_ROWS, BLOCK_ROWS), :]
            sh = (l0 - v0) % LANES
            if sh:
                src = pltpu.roll(src, sh, 1)
            acc = src if acc is None else jnp.where(lane >= l0, src, acc)
        if width < LANES:
            acc = acc[:, :width]
        o_ref[0, :, pl.ds(start, width)] = acc


def assemble(a0, b0, first, second, dvals, tables, rows):
    win = 104
    n_blocks = rows // BLOCK_ROWS
    total = 2 * ORDERS
    grid_spec = pltpu.PrefetchScalarGridSpec(
        num_scalar_prefetch=4,
        grid=(2, n_blocks),
        in_specs=[
            pl.BlockSpec(memory_space=pltpu.SMEM),
            pl.BlockSpec((1,) + tables.shape[1:], lambda s, rb, *_: (s, 0, 0, 0)),
        ],
        out_specs=pl.BlockSpec((1, BLOCK_ROWS, total), lambda s, rb, *_: (s, rb, 0)),
        scratch_shapes=[pltpu.VMEM((2, win * BLOCK_ROWS, LANES), jnp.float32)],
    )
    return pl.pallas_call(
        assemble_kernel,
        grid_spec=grid_spec,
        out_shape=jax.ShapeDtypeStruct((2, rows, total), jnp.float32),
        compiler_params=pltpu.CompilerParams(dimension_semantics=("arbitrary", "arbitrary")),
    )(a0, b0, first, second, dvals, tables)


def line_sum(partial_value, my_index, devices):
    core = my_index % 2
    pairs = [(i, i ^ 1) for i in range(devices)]
    keep = jnp.where(core == 0, partial_value[0], partial_value[1])
    give = jnp.where(core == 0, partial_value[1], partial_value[0])
    mine = keep + lax.ppermute(give, "slab", pairs)
    right = [(i, i + 2) for i in range(devices - 2)]
    left = [(i + 2, i) for i in range(devices - 2)]
    from_left = jnp.zeros_like(mine)
    from_right = jnp.zeros_like(mine)
    for step in range(devices // 2 - 1):
        from_left, from_right = (
            lax.ppermute(mine + from_left, "slab", right),
            lax.ppermute(mine + from_right, "slab", left),
        )
    total = mine + from_left + from_right
    other = lax.ppermute(total, "slab", pairs)
    return jnp.where(core == 0, jnp.stack([total, other]), jnp.stack([other, total]))


def shards(labels):
    slab_rows = labels.shape[0]
    map_width = labels.shape[1]
    devices = lax.axis_size("slab")
    my_index = lax.axis_index("slab")
    permit = permittivity(labels)
    smooth = extended_2(permit, (("slab", 0),), 4)
    for sweep_index in range(3):
        smooth = smooth_once(smooth)
    grad_x, grad_y = gradient(smooth)
    scale = jnp.sqrt(grad_x * grad_x + grad_y * grad_y + 1.0)
    normal_x = grad_x / scale
    normal_y = grad_y / scale
    inverse = 1.0 / permit
    contrast = permit - inverse
    fields = jnp.stack(
        [
            permit,
            contrast * normal_x * normal_x,
            contrast * normal_x * normal_y,
            contrast * normal_y * normal_y,
        ]
    )
    padded_keep = -(-KEEP // devices) * devices
    half_keep = -(-HARM // devices) * devices
    frequency = (HARM - 1) - jnp.arange(padded_keep, dtype=jnp.int32)
    col_frequency = (HARM - 1) - jnp.arange(half_keep, dtype=jnp.int32)
    columns = jnp.arange(map_width, dtype=jnp.int32)
    phases = columns[:, None] * col_frequency[None, :] % map_width
    angles = phases.astype(jnp.float32) * (2.0 * math.pi / map_width)
    col_table = jnp.stack([jnp.cos(angles), -jnp.sin(angles)], axis=1)
    half_spectra = jnp.einsum("kxy,ycn->kxcn", fields, col_table, precision=lax.Precision.HIGH)
    my_positions = my_index * slab_rows + jnp.arange(slab_rows, dtype=jnp.int32)
    partial_value = row_transform(half_spectra, my_positions, frequency, map_width)
    summed = line_sum(partial_value, my_index, devices)
    coef = summed / float(map_width * map_width)
    a_in = jnp.arange(padded_keep, dtype=jnp.int32)
    c_in = jnp.arange(half_keep, dtype=jnp.int32)
    b_out = jnp.arange(2 * LANES, dtype=jnp.int32)
    flip_rows = (a_in[None, :] == (KEEP - 1) - a_in[:, None]).astype(jnp.float32)
    keep_cols = ((c_in[:, None] == b_out[None, :]) & (b_out[None, :] < HARM)).astype(jnp.float32)
    mirror_cols = (
        (c_in[:, None] == (KEEP - 1) - b_out[None, :]) & (b_out[None, :] >= HARM)
    ).astype(jnp.float32)
    sign = jnp.array([1.0, -1.0], jnp.float32)[:, None, None, None]
    direct = jnp.einsum("skac,cb->skab", coef, keep_cols, precision=lax.Precision.HIGHEST)
    mirrored = jnp.einsum(
        "ad,skdc,cb->skab", flip_rows, coef, mirror_cols, precision=lax.Precision.HIGHEST
    )
    full = direct + sign * mirrored
    tables = jnp.stack(
        [full[:, 2], full[:, 0] - full[:, 3], full[:, 1] - full[:, 0], -full[:, 2]], axis=1
    )
    rows = ROWS_DEV
    spacing = ORDERS // (rows * devices // 2)
    window_rows = my_index * rows + jnp.arange(rows, dtype=jnp.int32)
    order_index = window_rows // 2 * spacing
    first = order_index // HARM
    second = order_index % HARM
    centre = (HARM - 1) // 2
    kx = 0.3 + 0.02 * (first - centre).astype(jnp.float32)
    ky = 0.2 + 0.02 * (second - centre).astype(jnp.float32)
    lower = window_rows % 2 == 1
    left = jnp.where(lower, ky * ky, kx * ky)
    right = jnp.where(lower, -(kx * ky), -(kx * kx))
    dvals = jnp.stack([left, right])
    a0 = (HARM - 1) - first
    b0 = (HARM - 1) - second
    return assemble(a0, b0, first, second, dvals, tables, rows)


def solution(mesh):
    placed = (P(("layer", "slab"), None),)
    return jax.shard_map(
        shards,
        mesh=mesh,
        in_specs=placed,
        out_specs=P(None, ("layer", "slab"), None),
        check_vma=False,
    )
```

```python
import functools
import math

import jax
import jax.numpy as jnp
from jax import lax
from jax.experimental import pallas as pl
from jax.experimental.pallas import tpu as pltpu
from jax.sharding import PartitionSpec as P

HARM = 101
ROWS_DEV = 64
KEEP = 201
ORDERS = 10201
BLOCK_ROWS = 8
LANES = 128


PERMITS = (1.0, 2.1, 4.0, 12.1)


def extended_2(block, sides, width):
    for axis, dim in sides:
        count = lax.axis_size(axis)
        forward = [(i, i + 1) for i in range(count - 1)]
        forward.append((count - 1, 0))
        backward = [(target, source) for source, target in forward]
        low = lax.ppermute(
            lax.slice_in_dim(block, block.shape[dim] - width, None, axis=dim), axis, forward
        )
        high = lax.ppermute(lax.slice_in_dim(block, 0, width, axis=dim), axis, backward)
        block = jnp.concatenate([low, block, high], axis=dim)
    return block


def permittivity(labels):
    total = jnp.zeros(labels.shape, jnp.float32)
    for index_value in range(4):
        total = total + jnp.where(
            labels == index_value, jnp.float32(PERMITS[index_value]), jnp.float32(0.0)
        )
    return total


def smooth_once(extended):
    middle = extended[1:-1]
    return (
        4.0 * middle
        + extended[:-2]
        + extended[2:]
        + jnp.roll(middle, 1, 1)
        + jnp.roll(middle, -1, 1)
    ) / 8.0


def gradient(extended):
    middle = extended[1:-1]
    grad_x = (extended[2:] - extended[:-2]) / 2.0
    grad_y = (jnp.roll(middle, -1, 1) - jnp.roll(middle, 1, 1)) / 2.0
    return (grad_x, grad_y)


def rim_rows(field_in):
    return extended_2(field_in, (("slab", 0),), 1)


def row_transform(spectra_in, positions, frequency, map_width):
    phases = frequency[:, None] * positions[None, :] % map_width
    angles = phases.astype(jnp.float32) * (2.0 * math.pi / map_width)
    table = jnp.stack([jnp.cos(angles), jnp.sin(angles)])
    products = jnp.einsum("smx,kxcn->skmcn", table, spectra_in, precision=lax.Precision.HIGH)
    real_part = products[0, :, :, 0] + products[1, :, :, 1]
    imag_part = products[0, :, :, 1] - products[1, :, :, 0]
    return jnp.stack([real_part, imag_part])


def chunk_segments(total, half):
    chunks = []
    for start in range(0, total, LANES):
        width = min(LANES, total - start)
        runs = []
        for lane in range(width):
            flat = start + lane
            h, j = divmod(flat, half)
            u, v = divmod(j, HARM)
            if not runs or runs[-1][0] != h or runs[-1][1] != u:
                runs.append((h, u, lane, v))
        chunks.append((start, width, runs))
    return chunks


def assemble_kernel(a0_ref, b0_ref, first_ref, second_ref, dval_ref, fl_ref, o_ref, z_ref):
    s = pl.program_id(0)
    rb = pl.program_id(1)
    span = z_ref.shape[1] // BLOCK_ROWS - BLOCK_ROWS
    lane_iota = lax.broadcasted_iota(jnp.int32, (span, LANES), 1)
    sub = lax.broadcasted_iota(jnp.int32, (BLOCK_ROWS, LANES), 0)
    lane = lax.broadcasted_iota(jnp.int32, (BLOCK_ROWS, LANES), 1)
    for rr in range(BLOCK_ROWS):
        row = rb * BLOCK_ROWS + rr
        a0 = a0_ref[row]
        b0 = b0_ref[row]
        first = first_ref[row]
        second = second_ref[row]
        shift = (LANES - b0) % LANES
        base = pl.multiple_of(a0 // BLOCK_ROWS * BLOCK_ROWS, BLOCK_ROWS)
        off = a0 % BLOCK_ROWS
        dest = pl.multiple_of((BLOCK_ROWS - off) * BLOCK_ROWS, BLOCK_ROWS) + rr
        spot_tile = pl.multiple_of((first + BLOCK_ROWS) * BLOCK_ROWS, BLOCK_ROWS)
        wrap = lane_iota + b0 < LANES
        spot = (sub == rr) & (lane == second)
        for h in range(2):
            combo = 2 * (rr % 2) + h
            x_lo = fl_ref[0, combo, pl.ds(base, span), pl.ds(0, LANES)]
            x_hi = fl_ref[0, combo, pl.ds(base, span), pl.ds(LANES, LANES)]
            x = jnp.where(wrap, pltpu.roll(x_lo, shift, 1), pltpu.roll(x_hi, shift, 1))
            z_ref[h, pl.ds(dest, span, stride=BLOCK_ROWS), :] = x
            d = jnp.where(s == 0, dval_ref[h, row], jnp.float32(0.0))
            tile = z_ref[h, pl.ds(spot_tile, BLOCK_ROWS), :]
            z_ref[h, pl.ds(spot_tile, BLOCK_ROWS), :] = tile + jnp.where(spot, d, jnp.float32(0.0))
    for start, width, runs in chunk_segments(o_ref.shape[2], o_ref.shape[2] // 2):
        acc = None
        for h, u, l0, v0 in runs:
            src = z_ref[h, pl.ds((u + BLOCK_ROWS) * BLOCK_ROWS, BLOCK_ROWS), :]
            sh = (l0 - v0) % LANES
            if sh:
                src = pltpu.roll(src, sh, 1)
            acc = src if acc is None else jnp.where(lane >= l0, src, acc)
        if width < LANES:
            acc = acc[:, :width]
        o_ref[0, :, pl.ds(start, width)] = acc


def assemble(a0, b0, first, second, dvals, tables, rows):
    span = 112
    n_blocks = rows // BLOCK_ROWS
    total = 2 * ORDERS
    grid_spec = pltpu.PrefetchScalarGridSpec(
        num_scalar_prefetch=4,
        grid=(2, n_blocks),
        in_specs=[
            pl.BlockSpec(memory_space=pltpu.SMEM),
            pl.BlockSpec((1,) + tables.shape[1:], lambda s, rb, *_: (s, 0, 0, 0)),
        ],
        out_specs=pl.BlockSpec((1, BLOCK_ROWS, total), lambda s, rb, *_: (s, rb, 0)),
        scratch_shapes=[pltpu.VMEM((2, (span + BLOCK_ROWS) * BLOCK_ROWS, LANES), jnp.float32)],
    )
    return pl.pallas_call(
        assemble_kernel,
        grid_spec=grid_spec,
        out_shape=jax.ShapeDtypeStruct((2, rows, total), jnp.float32),
        compiler_params=pltpu.CompilerParams(dimension_semantics=("arbitrary", "arbitrary")),
    )(a0, b0, first, second, dvals, tables)


def line_sum(partial_value, my_index, devices):
    core = my_index % 2
    pairs = [(i, i ^ 1) for i in range(devices)]
    keep = jnp.where(core == 0, partial_value[0], partial_value[1])
    give = jnp.where(core == 0, partial_value[1], partial_value[0])
    mine = keep + lax.ppermute(give, "slab", pairs)
    right = [(i, i + 2) for i in range(devices - 2)]
    left = [(i + 2, i) for i in range(devices - 2)]
    from_left = jnp.zeros_like(mine)
    from_right = jnp.zeros_like(mine)
    for step in range(devices // 2 - 1):
        from_left, from_right = (
            lax.ppermute(mine + from_left, "slab", right),
            lax.ppermute(mine + from_right, "slab", left),
        )
    total = mine + from_left + from_right
    other = lax.ppermute(total, "slab", pairs)
    return jnp.where(core == 0, jnp.stack([total, other]), jnp.stack([other, total]))


def shards(labels):
    slab_rows = labels.shape[0]
    map_width = labels.shape[1]
    devices = lax.axis_size("slab")
    my_index = lax.axis_index("slab")
    permit = permittivity(labels)
    smooth = extended_2(permit, (("slab", 0),), 4)
    for sweep_index in range(3):
        smooth = smooth_once(smooth)
    grad_x, grad_y = gradient(smooth)
    scale = jnp.sqrt(grad_x * grad_x + grad_y * grad_y + 1.0)
    normal_x = grad_x / scale
    normal_y = grad_y / scale
    inverse = 1.0 / permit
    contrast = permit - inverse
    fields = jnp.stack(
        [
            permit,
            contrast * normal_x * normal_x,
            contrast * normal_x * normal_y,
            contrast * normal_y * normal_y,
        ]
    )
    padded_keep = -(-KEEP // devices) * devices
    half_keep = -(-HARM // devices) * devices
    frequency = (HARM - 1) - jnp.arange(padded_keep, dtype=jnp.int32)
    col_frequency = (HARM - 1) - jnp.arange(half_keep, dtype=jnp.int32)
    columns = jnp.arange(map_width, dtype=jnp.int32)
    phases = columns[:, None] * col_frequency[None, :] % map_width
    angles = phases.astype(jnp.float32) * (2.0 * math.pi / map_width)
    col_table = jnp.stack([jnp.cos(angles), -jnp.sin(angles)], axis=1)
    half_spectra = jnp.einsum("kxy,ycn->kxcn", fields, col_table, precision=lax.Precision.HIGH)
    my_positions = my_index * slab_rows + jnp.arange(slab_rows, dtype=jnp.int32)
    partial_value = row_transform(half_spectra, my_positions, frequency, map_width)
    summed = line_sum(partial_value, my_index, devices)
    coef = summed / float(map_width * map_width)
    a_in = jnp.arange(padded_keep, dtype=jnp.int32)
    c_in = jnp.arange(half_keep, dtype=jnp.int32)
    b_out = jnp.arange(2 * LANES, dtype=jnp.int32)
    flip_rows = (a_in[None, :] == (KEEP - 1) - a_in[:, None]).astype(jnp.float32)
    keep_cols = ((c_in[:, None] == b_out[None, :]) & (b_out[None, :] < HARM)).astype(jnp.float32)
    mirror_cols = (
        (c_in[:, None] == (KEEP - 1) - b_out[None, :]) & (b_out[None, :] >= HARM)
    ).astype(jnp.float32)
    sign = jnp.array([1.0, -1.0], jnp.float32)[:, None, None, None]
    direct = jnp.einsum("skac,cb->skab", coef, keep_cols, precision=lax.Precision.HIGHEST)
    mirrored = jnp.einsum(
        "ad,skdc,cb->skab", flip_rows, coef, mirror_cols, precision=lax.Precision.HIGHEST
    )
    full = direct + sign * mirrored
    tables = jnp.stack(
        [full[:, 2], full[:, 0] - full[:, 3], full[:, 1] - full[:, 0], -full[:, 2]], axis=1
    )
    rows = ROWS_DEV
    spacing = ORDERS // (rows * devices // 2)
    window_rows = my_index * rows + jnp.arange(rows, dtype=jnp.int32)
    order_index = window_rows // 2 * spacing
    first = order_index // HARM
    second = order_index % HARM
    centre = (HARM - 1) // 2
    kx = 0.3 + 0.02 * (first - centre).astype(jnp.float32)
    ky = 0.2 + 0.02 * (second - centre).astype(jnp.float32)
    lower = window_rows % 2 == 1
    left = jnp.where(lower, ky * ky, kx * ky)
    right = jnp.where(lower, -(kx * ky), -(kx * kx))
    dvals = jnp.stack([left, right])
    a0 = (HARM - 1) - first
    b0 = (HARM - 1) - second
    return assemble(a0, b0, first, second, dvals, tables, rows)


def solution(mesh):
    placed = (P(("layer", "slab"), None),)
    return jax.shard_map(
        shards,
        mesh=mesh,
        in_specs=placed,
        out_specs=P(None, ("layer", "slab"), None),
        check_vma=False,
    )
```

```python
import functools
import math

import jax
import jax.numpy as jnp
from jax import lax
from jax.experimental import pallas as pl
from jax.experimental.pallas import tpu as pltpu
from jax.sharding import PartitionSpec as P

HARM = 101
ROWS_DEV = 64
KEEP = 201
ORDERS = 10201
BLOCK_ROWS = 8
LANES = 128


PERMITS = (1.0, 2.1, 4.0, 12.1)


def extended_2(block, sides, width):
    for axis, dim in sides:
        count = lax.axis_size(axis)
        forward = [(i, i + 1) for i in range(count - 1)]
        forward.append((count - 1, 0))
        backward = [(target, source) for source, target in forward]
        low = lax.ppermute(
            lax.slice_in_dim(block, block.shape[dim] - width, None, axis=dim), axis, forward
        )
        high = lax.ppermute(lax.slice_in_dim(block, 0, width, axis=dim), axis, backward)
        block = jnp.concatenate([low, block, high], axis=dim)
    return block


def permittivity(labels):
    total = jnp.zeros(labels.shape, jnp.float32)
    for index_value in range(4):
        total = total + jnp.where(
            labels == index_value, jnp.float32(PERMITS[index_value]), jnp.float32(0.0)
        )
    return total


def smooth_once(extended):
    middle = extended[1:-1]
    return (
        4.0 * middle
        + extended[:-2]
        + extended[2:]
        + jnp.roll(middle, 1, 1)
        + jnp.roll(middle, -1, 1)
    ) / 8.0


def gradient(extended):
    middle = extended[1:-1]
    grad_x = (extended[2:] - extended[:-2]) / 2.0
    grad_y = (jnp.roll(middle, -1, 1) - jnp.roll(middle, 1, 1)) / 2.0
    return (grad_x, grad_y)


def rim_rows(field_in):
    return extended_2(field_in, (("slab", 0),), 1)


def row_transform(spectra_in, positions, frequency, map_width):
    phases = frequency[:, None] * positions[None, :] % map_width
    angles = phases.astype(jnp.float32) * (2.0 * math.pi / map_width)
    table = jnp.stack([jnp.cos(angles), jnp.sin(angles)])
    products = jnp.einsum("smx,kxcn->skmcn", table, spectra_in, precision=lax.Precision.HIGH)
    real_part = products[0, :, :, 0] + products[1, :, :, 1]
    imag_part = products[0, :, :, 1] - products[1, :, :, 0]
    return jnp.stack([real_part, imag_part])


def chunk_segments(total, half):
    chunks = []
    for start in range(0, total, LANES):
        width = min(LANES, total - start)
        runs = []
        for lane in range(width):
            flat = start + lane
            h, j = divmod(flat, half)
            u, v = divmod(j, HARM)
            if not runs or runs[-1][0] != h or runs[-1][1] != u:
                runs.append((h, u, lane, v))
        chunks.append((start, width, runs))
    return chunks


def assemble_kernel(a0_ref, b0_ref, first_ref, second_ref, dval_ref, fl_ref, o_ref, z_ref):
    s = pl.program_id(0)
    rb = pl.program_id(1)
    span = z_ref.shape[1] // BLOCK_ROWS - BLOCK_ROWS
    lane_iota = lax.broadcasted_iota(jnp.int32, (span, LANES), 1)
    sub = lax.broadcasted_iota(jnp.int32, (BLOCK_ROWS, LANES), 0)
    lane = lax.broadcasted_iota(jnp.int32, (BLOCK_ROWS, LANES), 1)
    for rr in range(BLOCK_ROWS):
        row = rb * BLOCK_ROWS + rr
        a0 = a0_ref[row]
        b0 = b0_ref[row]
        first = first_ref[row]
        second = second_ref[row]
        shift = (LANES - b0) % LANES
        base = pl.multiple_of(a0 // BLOCK_ROWS * BLOCK_ROWS, BLOCK_ROWS)
        off = a0 % BLOCK_ROWS
        dest = pl.multiple_of((BLOCK_ROWS - off) * BLOCK_ROWS, BLOCK_ROWS) + rr
        spot_tile = pl.multiple_of((first + BLOCK_ROWS) * BLOCK_ROWS, BLOCK_ROWS)
        wrap = lane_iota + b0 < LANES
        spot = (sub == rr) & (lane == second)
        for h in range(2):
            combo = 2 * (rr % 2) + h
            x_lo = fl_ref[0, combo, pl.ds(base, span), pl.ds(0, LANES)]
            x_hi = fl_ref[0, combo, pl.ds(base, span), pl.ds(LANES, LANES)]
            x = jnp.where(wrap, pltpu.roll(x_lo, shift, 1), pltpu.roll(x_hi, shift, 1))
            z_ref[h, pl.ds(dest, span, stride=BLOCK_ROWS), :] = x
            d = jnp.where(s == 0, dval_ref[h, row], jnp.float32(0.0))
            tile = z_ref[h, pl.ds(spot_tile, BLOCK_ROWS), :]
            z_ref[h, pl.ds(spot_tile, BLOCK_ROWS), :] = tile + jnp.where(spot, d, jnp.float32(0.0))
    placed = {}
    for start, width, runs in chunk_segments(o_ref.shape[2], o_ref.shape[2] // 2):
        acc = None
        for h, u, l0, v0 in runs:
            if (h, u) not in placed:
                src = z_ref[h, pl.ds((u + BLOCK_ROWS) * BLOCK_ROWS, BLOCK_ROWS), :]
                sh = (l0 - v0) % LANES
                placed[(h, u)] = pltpu.roll(src, sh, 1) if sh else src
            src = placed[(h, u)]
            acc = src if acc is None else jnp.where(lane >= l0, src, acc)
        if width < LANES:
            acc = acc[:, :width]
        o_ref[0, :, pl.ds(start, width)] = acc


def assemble(a0, b0, first, second, dvals, tables, rows):
    span = 112
    n_blocks = rows // BLOCK_ROWS
    total = 2 * ORDERS
    grid_spec = pltpu.PrefetchScalarGridSpec(
        num_scalar_prefetch=4,
        grid=(2, n_blocks),
        in_specs=[
            pl.BlockSpec(memory_space=pltpu.SMEM),
            pl.BlockSpec((1,) + tables.shape[1:], lambda s, rb, *_: (s, 0, 0, 0)),
        ],
        out_specs=pl.BlockSpec((1, BLOCK_ROWS, total), lambda s, rb, *_: (s, rb, 0)),
        scratch_shapes=[pltpu.VMEM((2, (span + BLOCK_ROWS) * BLOCK_ROWS, LANES), jnp.float32)],
    )
    return pl.pallas_call(
        assemble_kernel,
        grid_spec=grid_spec,
        out_shape=jax.ShapeDtypeStruct((2, rows, total), jnp.float32),
        compiler_params=pltpu.CompilerParams(dimension_semantics=("arbitrary", "arbitrary")),
    )(a0, b0, first, second, dvals, tables)


def line_sum(partial_value, my_index, devices):
    core = my_index % 2
    pairs = [(i, i ^ 1) for i in range(devices)]
    keep = jnp.where(core == 0, partial_value[0], partial_value[1])
    give = jnp.where(core == 0, partial_value[1], partial_value[0])
    mine = keep + lax.ppermute(give, "slab", pairs)
    right = [(i, i + 2) for i in range(devices - 2)]
    left = [(i + 2, i) for i in range(devices - 2)]
    from_left = jnp.zeros_like(mine)
    from_right = jnp.zeros_like(mine)
    for step in range(devices // 2 - 1):
        from_left, from_right = (
            lax.ppermute(mine + from_left, "slab", right),
            lax.ppermute(mine + from_right, "slab", left),
        )
    total = mine + from_left + from_right
    other = lax.ppermute(total, "slab", pairs)
    return jnp.where(core == 0, jnp.stack([total, other]), jnp.stack([other, total]))


def shards(labels):
    slab_rows = labels.shape[0]
    map_width = labels.shape[1]
    devices = lax.axis_size("slab")
    my_index = lax.axis_index("slab")
    permit = permittivity(labels)
    smooth = extended_2(permit, (("slab", 0),), 4)
    for sweep_index in range(3):
        smooth = smooth_once(smooth)
    grad_x, grad_y = gradient(smooth)
    scale = jnp.sqrt(grad_x * grad_x + grad_y * grad_y + 1.0)
    normal_x = grad_x / scale
    normal_y = grad_y / scale
    inverse = 1.0 / permit
    contrast = permit - inverse
    fields = jnp.stack(
        [
            permit,
            contrast * normal_x * normal_x,
            contrast * normal_x * normal_y,
            contrast * normal_y * normal_y,
        ]
    )
    padded_keep = -(-KEEP // devices) * devices
    half_keep = -(-HARM // devices) * devices
    frequency = (HARM - 1) - jnp.arange(padded_keep, dtype=jnp.int32)
    col_frequency = (HARM - 1) - jnp.arange(half_keep, dtype=jnp.int32)
    columns = jnp.arange(map_width, dtype=jnp.int32)
    phases = columns[:, None] * col_frequency[None, :] % map_width
    angles = phases.astype(jnp.float32) * (2.0 * math.pi / map_width)
    col_table = jnp.stack([jnp.cos(angles), -jnp.sin(angles)], axis=1)
    half_spectra = jnp.einsum("kxy,ycn->kxcn", fields, col_table, precision=lax.Precision.HIGH)
    my_positions = my_index * slab_rows + jnp.arange(slab_rows, dtype=jnp.int32)
    partial_value = row_transform(half_spectra, my_positions, frequency, map_width)
    summed = line_sum(partial_value, my_index, devices)
    coef = summed / float(map_width * map_width)
    a_in = jnp.arange(padded_keep, dtype=jnp.int32)
    c_in = jnp.arange(half_keep, dtype=jnp.int32)
    b_out = jnp.arange(2 * LANES, dtype=jnp.int32)
    flip_rows = (a_in[None, :] == (KEEP - 1) - a_in[:, None]).astype(jnp.float32)
    keep_cols = ((c_in[:, None] == b_out[None, :]) & (b_out[None, :] < HARM)).astype(jnp.float32)
    mirror_cols = (
        (c_in[:, None] == (KEEP - 1) - b_out[None, :]) & (b_out[None, :] >= HARM)
    ).astype(jnp.float32)
    sign = jnp.array([1.0, -1.0], jnp.float32)[:, None, None, None]
    direct = jnp.einsum("skac,cb->skab", coef, keep_cols, precision=lax.Precision.HIGHEST)
    mirrored = jnp.einsum(
        "ad,skdc,cb->skab", flip_rows, coef, mirror_cols, precision=lax.Precision.HIGHEST
    )
    full = direct + sign * mirrored
    tables = jnp.stack(
        [full[:, 2], full[:, 0] - full[:, 3], full[:, 1] - full[:, 0], -full[:, 2]], axis=1
    )
    rows = ROWS_DEV
    spacing = ORDERS // (rows * devices // 2)
    window_rows = my_index * rows + jnp.arange(rows, dtype=jnp.int32)
    order_index = window_rows // 2 * spacing
    first = order_index // HARM
    second = order_index % HARM
    centre = (HARM - 1) // 2
    kx = 0.3 + 0.02 * (first - centre).astype(jnp.float32)
    ky = 0.2 + 0.02 * (second - centre).astype(jnp.float32)
    lower = window_rows % 2 == 1
    left = jnp.where(lower, ky * ky, kx * ky)
    right = jnp.where(lower, -(kx * ky), -(kx * kx))
    dvals = jnp.stack([left, right])
    a0 = (HARM - 1) - first
    b0 = (HARM - 1) - second
    return assemble(a0, b0, first, second, dvals, tables, rows)


def solution(mesh):
    placed = (P(("layer", "slab"), None),)
    return jax.shard_map(
        shards,
        mesh=mesh,
        in_specs=placed,
        out_specs=P(None, ("layer", "slab"), None),
        check_vma=False,
    )
```

```python
import functools
import math

import jax
import jax.numpy as jnp
from jax import lax
from jax.experimental import pallas as pl
from jax.experimental.pallas import tpu as pltpu
from jax.sharding import PartitionSpec as P

HARM = 101
ROWS_DEV = 64
KEEP = 201
ORDERS = 10201
BLOCK_ROWS = 8
LANES = 128


PERMITS = (1.0, 2.1, 4.0, 12.1)


def extended_2(block, sides, width):
    for axis, dim in sides:
        count = lax.axis_size(axis)
        forward = [(i, i + 1) for i in range(count - 1)]
        forward.append((count - 1, 0))
        backward = [(target, source) for source, target in forward]
        low = lax.ppermute(
            lax.slice_in_dim(block, block.shape[dim] - width, None, axis=dim), axis, forward
        )
        high = lax.ppermute(lax.slice_in_dim(block, 0, width, axis=dim), axis, backward)
        block = jnp.concatenate([low, block, high], axis=dim)
    return block


def permittivity(labels):
    total = jnp.zeros(labels.shape, jnp.float32)
    for index_value in range(4):
        total = total + jnp.where(
            labels == index_value, jnp.float32(PERMITS[index_value]), jnp.float32(0.0)
        )
    return total


def smooth_once(extended):
    middle = extended[1:-1]
    return (
        4.0 * middle
        + extended[:-2]
        + extended[2:]
        + jnp.roll(middle, 1, 1)
        + jnp.roll(middle, -1, 1)
    ) / 8.0


def gradient(extended):
    middle = extended[1:-1]
    grad_x = (extended[2:] - extended[:-2]) / 2.0
    grad_y = (jnp.roll(middle, -1, 1) - jnp.roll(middle, 1, 1)) / 2.0
    return (grad_x, grad_y)


def rim_rows(field_in):
    return extended_2(field_in, (("slab", 0),), 1)


def row_transform(spectra_in, positions, frequency, map_width):
    phases = frequency[:, None] * positions[None, :] % map_width
    angles = phases.astype(jnp.float32) * (2.0 * math.pi / map_width)
    table = jnp.stack([jnp.cos(angles), jnp.sin(angles)])
    products = jnp.einsum("smx,kxcn->skmcn", table, spectra_in, precision=lax.Precision.HIGH)
    real_part = products[0, :, :, 0] + products[1, :, :, 1]
    imag_part = products[0, :, :, 1] - products[1, :, :, 0]
    return jnp.stack([real_part, imag_part])


def chunk_segments(total, half):
    chunks = []
    for start in range(0, total, LANES):
        width = min(LANES, total - start)
        runs = []
        for lane in range(width):
            flat = start + lane
            h, j = divmod(flat, half)
            u, v = divmod(j, HARM)
            if not runs or runs[-1][0] != h or runs[-1][1] != u:
                runs.append((h, u, lane, v))
        chunks.append((start, width, runs))
    return chunks


def assemble_kernel(a0_ref, b0_ref, first_ref, second_ref, dval_ref, fl_ref, o_ref, z_ref):
    s = pl.program_id(0)
    rb = pl.program_id(1)
    span = z_ref.shape[1] // BLOCK_ROWS - BLOCK_ROWS
    lane_iota = lax.broadcasted_iota(jnp.int32, (span, LANES), 1)
    sub = lax.broadcasted_iota(jnp.int32, (BLOCK_ROWS, LANES), 0)
    lane = lax.broadcasted_iota(jnp.int32, (BLOCK_ROWS, LANES), 1)
    for rr in range(BLOCK_ROWS):
        row = rb * BLOCK_ROWS + rr
        a0 = a0_ref[row]
        b0 = b0_ref[row]
        first = first_ref[row]
        second = second_ref[row]
        shift = (LANES - b0) % LANES
        base = pl.multiple_of(a0 // BLOCK_ROWS * BLOCK_ROWS, BLOCK_ROWS)
        off = a0 % BLOCK_ROWS
        dest = pl.multiple_of((BLOCK_ROWS - off) * BLOCK_ROWS, BLOCK_ROWS) + rr
        spot_tile = pl.multiple_of((first + BLOCK_ROWS) * BLOCK_ROWS, BLOCK_ROWS)
        wrap = lane_iota + b0 < LANES
        spot = (sub == rr) & (lane == second)
        for h in range(2):
            combo = 2 * (rr % 2) + h
            x_lo = fl_ref[0, combo, pl.ds(base, span), pl.ds(0, LANES)]
            x_hi = fl_ref[0, combo, pl.ds(base, span), pl.ds(LANES, LANES)]
            x = jnp.where(wrap, pltpu.roll(x_lo, shift, 1), pltpu.roll(x_hi, shift, 1))
            z_ref[h, pl.ds(dest, span, stride=BLOCK_ROWS), :] = x
            d = jnp.where(s == 0, dval_ref[h, row], jnp.float32(0.0))
            tile = z_ref[h, pl.ds(spot_tile, BLOCK_ROWS), :]
            z_ref[h, pl.ds(spot_tile, BLOCK_ROWS), :] = tile + jnp.where(spot, d, jnp.float32(0.0))
    placed = {}
    for start, width, runs in chunk_segments(o_ref.shape[2], o_ref.shape[2] // 2):
        acc = None
        for h, u, l0, v0 in runs:
            if (h, u) not in placed:
                src = z_ref[h, pl.ds((u + BLOCK_ROWS) * BLOCK_ROWS, BLOCK_ROWS), :]
                sh = (l0 - v0) % LANES
                placed[(h, u)] = pltpu.roll(src, sh, 1) if sh else src
            src = placed[(h, u)]
            acc = src if acc is None else jnp.where(lane >= l0, src, acc)
        if width < LANES:
            acc = acc[:, :width]
        o_ref[0, :, pl.ds(start, width)] = acc


def assemble(a0, b0, first, second, dvals, tables, rows):
    span = 112
    n_blocks = rows // BLOCK_ROWS
    total = 2 * ORDERS
    grid_spec = pltpu.PrefetchScalarGridSpec(
        num_scalar_prefetch=4,
        grid=(2, n_blocks),
        in_specs=[
            pl.BlockSpec(memory_space=pltpu.SMEM),
            pl.BlockSpec((1,) + tables.shape[1:], lambda s, rb, *_: (s, 0, 0, 0)),
        ],
        out_specs=pl.BlockSpec((1, BLOCK_ROWS, total), lambda s, rb, *_: (s, rb, 0)),
        scratch_shapes=[pltpu.VMEM((2, (span + BLOCK_ROWS) * BLOCK_ROWS, LANES), jnp.float32)],
    )
    return pl.pallas_call(
        assemble_kernel,
        grid_spec=grid_spec,
        out_shape=jax.ShapeDtypeStruct((2, rows, total), jnp.float32),
        compiler_params=pltpu.CompilerParams(dimension_semantics=("arbitrary", "arbitrary")),
    )(a0, b0, first, second, dvals, tables)


def line_sum(partial_value, my_index, devices):
    core = my_index % 2
    pairs = [(i, i ^ 1) for i in range(devices)]
    half_shape = partial_value.shape[1:]
    dense = (-1, LANES) if math.prod(half_shape) % LANES == 0 else half_shape
    keep = jnp.where(core == 0, partial_value[0], partial_value[1]).reshape(dense)
    give = jnp.where(core == 0, partial_value[1], partial_value[0]).reshape(dense)
    mine = keep + lax.ppermute(give, "slab", pairs)
    right = [(i, i + 2) for i in range(devices - 2)]
    left = [(i + 2, i) for i in range(devices - 2)]
    from_left = jnp.zeros_like(mine)
    from_right = jnp.zeros_like(mine)
    for step in range(devices // 2 - 1):
        from_left, from_right = (
            lax.ppermute(mine + from_left, "slab", right),
            lax.ppermute(mine + from_right, "slab", left),
        )
    total = mine + from_left + from_right
    other = lax.ppermute(total, "slab", pairs).reshape(half_shape)
    total = total.reshape(half_shape)
    return jnp.where(core == 0, jnp.stack([total, other]), jnp.stack([other, total]))


def shards(labels):
    slab_rows = labels.shape[0]
    map_width = labels.shape[1]
    devices = lax.axis_size("slab")
    my_index = lax.axis_index("slab")
    permit = permittivity(labels)
    smooth = extended_2(permit, (("slab", 0),), 4)
    for sweep_index in range(3):
        smooth = smooth_once(smooth)
    grad_x, grad_y = gradient(smooth)
    scale = jnp.sqrt(grad_x * grad_x + grad_y * grad_y + 1.0)
    normal_x = grad_x / scale
    normal_y = grad_y / scale
    inverse = 1.0 / permit
    contrast = permit - inverse
    fields = jnp.stack(
        [
            permit,
            contrast * normal_x * normal_x,
            contrast * normal_x * normal_y,
            contrast * normal_y * normal_y,
        ]
    )
    padded_keep = -(-KEEP // devices) * devices
    half_keep = -(-HARM // devices) * devices
    frequency = (HARM - 1) - jnp.arange(padded_keep, dtype=jnp.int32)
    col_frequency = (HARM - 1) - jnp.arange(half_keep, dtype=jnp.int32)
    columns = jnp.arange(map_width, dtype=jnp.int32)
    phases = columns[:, None] * col_frequency[None, :] % map_width
    angles = phases.astype(jnp.float32) * (2.0 * math.pi / map_width)
    col_table = jnp.stack([jnp.cos(angles), -jnp.sin(angles)], axis=1)
    half_spectra = jnp.einsum("kxy,ycn->kxcn", fields, col_table, precision=lax.Precision.HIGH)
    my_positions = my_index * slab_rows + jnp.arange(slab_rows, dtype=jnp.int32)
    partial_value = row_transform(half_spectra, my_positions, frequency, map_width)
    summed = line_sum(partial_value, my_index, devices)
    coef = summed / float(map_width * map_width)
    a_in = jnp.arange(padded_keep, dtype=jnp.int32)
    c_in = jnp.arange(half_keep, dtype=jnp.int32)
    b_out = jnp.arange(2 * LANES, dtype=jnp.int32)
    flip_rows = (a_in[None, :] == (KEEP - 1) - a_in[:, None]).astype(jnp.float32)
    keep_cols = ((c_in[:, None] == b_out[None, :]) & (b_out[None, :] < HARM)).astype(jnp.float32)
    mirror_cols = (
        (c_in[:, None] == (KEEP - 1) - b_out[None, :]) & (b_out[None, :] >= HARM)
    ).astype(jnp.float32)
    sign = jnp.array([1.0, -1.0], jnp.float32)[:, None, None, None]
    direct = jnp.einsum("skac,cb->skab", coef, keep_cols, precision=lax.Precision.HIGHEST)
    mirrored = jnp.einsum(
        "ad,skdc,cb->skab", flip_rows, coef, mirror_cols, precision=lax.Precision.HIGHEST
    )
    full = direct + sign * mirrored
    tables = jnp.stack(
        [full[:, 2], full[:, 0] - full[:, 3], full[:, 1] - full[:, 0], -full[:, 2]], axis=1
    )
    rows = ROWS_DEV
    spacing = ORDERS // (rows * devices // 2)
    window_rows = my_index * rows + jnp.arange(rows, dtype=jnp.int32)
    order_index = window_rows // 2 * spacing
    first = order_index // HARM
    second = order_index % HARM
    centre = (HARM - 1) // 2
    kx = 0.3 + 0.02 * (first - centre).astype(jnp.float32)
    ky = 0.2 + 0.02 * (second - centre).astype(jnp.float32)
    lower = window_rows % 2 == 1
    left = jnp.where(lower, ky * ky, kx * ky)
    right = jnp.where(lower, -(kx * ky), -(kx * kx))
    dvals = jnp.stack([left, right])
    a0 = (HARM - 1) - first
    b0 = (HARM - 1) - second
    return assemble(a0, b0, first, second, dvals, tables, rows)


def solution(mesh):
    placed = (P(("layer", "slab"), None),)
    return jax.shard_map(
        shards,
        mesh=mesh,
        in_specs=placed,
        out_specs=P(None, ("layer", "slab"), None),
        check_vma=False,
    )
```

```python
import functools
import math

import jax
import jax.numpy as jnp
from jax import lax
from jax.experimental import pallas as pl
from jax.experimental.pallas import tpu as pltpu
from jax.sharding import PartitionSpec as P

HARM = 101
ROWS_DEV = 64
KEEP = 201
ORDERS = 10201
BLOCK_ROWS = 8
LANES = 128


PERMITS = (1.0, 2.1, 4.0, 12.1)


def extended_2(block, sides, width):
    for axis, dim in sides:
        count = lax.axis_size(axis)
        forward = [(i, i + 1) for i in range(count - 1)]
        forward.append((count - 1, 0))
        backward = [(target, source) for source, target in forward]
        low = lax.ppermute(
            lax.slice_in_dim(block, block.shape[dim] - width, None, axis=dim), axis, forward
        )
        high = lax.ppermute(lax.slice_in_dim(block, 0, width, axis=dim), axis, backward)
        block = jnp.concatenate([low, block, high], axis=dim)
    return block


def permittivity(labels):
    total = jnp.zeros(labels.shape, jnp.float32)
    for index_value in range(4):
        total = total + jnp.where(
            labels == index_value, jnp.float32(PERMITS[index_value]), jnp.float32(0.0)
        )
    return total


def smooth_once(extended):
    middle = extended[1:-1]
    return (
        4.0 * middle
        + extended[:-2]
        + extended[2:]
        + jnp.roll(middle, 1, 1)
        + jnp.roll(middle, -1, 1)
    ) / 8.0


def gradient(extended):
    middle = extended[1:-1]
    grad_x = (extended[2:] - extended[:-2]) / 2.0
    grad_y = (jnp.roll(middle, -1, 1) - jnp.roll(middle, 1, 1)) / 2.0
    return (grad_x, grad_y)


def rim_rows(field_in):
    return extended_2(field_in, (("slab", 0),), 1)


def row_transform(spectra_in, positions, frequency, map_width):
    phases = frequency[:, None] * positions[None, :] % map_width
    angles = phases.astype(jnp.float32) * (2.0 * math.pi / map_width)
    table = jnp.stack([jnp.cos(angles), jnp.sin(angles)])
    products = jnp.einsum("smx,kxcn->skmcn", table, spectra_in, precision=lax.Precision.HIGH)
    real_part = products[0, :, :, 0] + products[1, :, :, 1]
    imag_part = products[0, :, :, 1] - products[1, :, :, 0]
    return jnp.stack([real_part, imag_part])


def chunk_segments(total, half):
    chunks = []
    for start in range(0, total, LANES):
        width = min(LANES, total - start)
        runs = []
        for lane in range(width):
            flat = start + lane
            h, j = divmod(flat, half)
            u, v = divmod(j, HARM)
            if not runs or runs[-1][0] != h or runs[-1][1] != u:
                runs.append((h, u, lane, v))
        chunks.append((start, width, runs))
    return chunks


def assemble_kernel(a0_ref, b0_ref, first_ref, second_ref, dval_ref, fl_ref, o_ref, z_ref):
    s = pl.program_id(0)
    rb = pl.program_id(1)
    span = z_ref.shape[1] // BLOCK_ROWS - BLOCK_ROWS
    lane_iota = lax.broadcasted_iota(jnp.int32, (span, LANES), 1)
    sub = lax.broadcasted_iota(jnp.int32, (BLOCK_ROWS, LANES), 0)
    lane = lax.broadcasted_iota(jnp.int32, (BLOCK_ROWS, LANES), 1)
    for rr in range(BLOCK_ROWS):
        row = rb * BLOCK_ROWS + rr
        a0 = a0_ref[row]
        b0 = b0_ref[row]
        first = first_ref[row]
        second = second_ref[row]
        shift = (LANES - b0) % LANES
        base = pl.multiple_of(a0 // BLOCK_ROWS * BLOCK_ROWS, BLOCK_ROWS)
        off = a0 % BLOCK_ROWS
        dest = pl.multiple_of((BLOCK_ROWS - off) * BLOCK_ROWS, BLOCK_ROWS) + rr
        spot_tile = pl.multiple_of((first + BLOCK_ROWS) * BLOCK_ROWS, BLOCK_ROWS)
        wrap = lane_iota + b0 < LANES
        spot = (sub == rr) & (lane == second)
        for h in range(2):
            combo = 2 * (rr % 2) + h
            x_lo = fl_ref[0, combo, pl.ds(base, span), pl.ds(0, LANES)]
            x_hi = fl_ref[0, combo, pl.ds(base, span), pl.ds(LANES, LANES)]
            x = jnp.where(wrap, pltpu.roll(x_lo, shift, 1), pltpu.roll(x_hi, shift, 1))
            z_ref[h, pl.ds(dest, span, stride=BLOCK_ROWS), :] = x
            d = jnp.where(s == 0, dval_ref[h, row], jnp.float32(0.0))
            tile = z_ref[h, pl.ds(spot_tile, BLOCK_ROWS), :]
            z_ref[h, pl.ds(spot_tile, BLOCK_ROWS), :] = tile + jnp.where(spot, d, jnp.float32(0.0))
    placed = {}
    for start, width, runs in chunk_segments(o_ref.shape[2], o_ref.shape[2] // 2):
        acc = None
        for h, u, l0, v0 in runs:
            if (h, u) not in placed:
                src = z_ref[h, pl.ds((u + BLOCK_ROWS) * BLOCK_ROWS, BLOCK_ROWS), :]
                sh = (l0 - v0) % LANES
                placed[(h, u)] = pltpu.roll(src, sh, 1) if sh else src
            src = placed[(h, u)]
            acc = src if acc is None else jnp.where(lane >= l0, src, acc)
        if width < LANES:
            acc = acc[:, :width]
        o_ref[0, :, pl.ds(start, width)] = acc


def assemble(a0, b0, first, second, dvals, tables, rows):
    span = 112
    n_blocks = rows // BLOCK_ROWS
    total = 2 * ORDERS
    grid_spec = pltpu.PrefetchScalarGridSpec(
        num_scalar_prefetch=4,
        grid=(2, n_blocks),
        in_specs=[
            pl.BlockSpec(memory_space=pltpu.SMEM),
            pl.BlockSpec((1,) + tables.shape[1:], lambda s, rb, *_: (s, 0, 0, 0)),
        ],
        out_specs=pl.BlockSpec((1, BLOCK_ROWS, total), lambda s, rb, *_: (s, rb, 0)),
        scratch_shapes=[pltpu.VMEM((2, (span + BLOCK_ROWS) * BLOCK_ROWS, LANES), jnp.float32)],
    )
    return pl.pallas_call(
        assemble_kernel,
        grid_spec=grid_spec,
        out_shape=jax.ShapeDtypeStruct((2, rows, total), jnp.float32),
        compiler_params=pltpu.CompilerParams(dimension_semantics=("arbitrary", "arbitrary")),
    )(a0, b0, first, second, dvals, tables)


def line_sum(partial_value, my_index, devices):
    core = my_index % 2
    pairs = [(i, i ^ 1) for i in range(devices)]
    half_shape = partial_value.shape[1:]
    dense = (-1, LANES) if math.prod(half_shape) % LANES == 0 else half_shape
    keep = jnp.where(core == 0, partial_value[0], partial_value[1]).reshape(dense)
    give = jnp.where(core == 0, partial_value[1], partial_value[0]).reshape(dense)
    mine = keep + lax.ppermute(give, "slab", pairs)
    chips = devices // 2
    if chips & (chips - 1) == 0:
        total = mine
        bit = 2
        while bit < devices:
            total = total + lax.ppermute(total, "slab", [(i, i ^ bit) for i in range(devices)])
            bit *= 2
    else:
        right = [(i, i + 2) for i in range(devices - 2)]
        left = [(i + 2, i) for i in range(devices - 2)]
        from_left = jnp.zeros_like(mine)
        from_right = jnp.zeros_like(mine)
        for step in range(chips - 1):
            from_left, from_right = (
                lax.ppermute(mine + from_left, "slab", right),
                lax.ppermute(mine + from_right, "slab", left),
            )
        total = mine + from_left + from_right
    other = lax.ppermute(total, "slab", pairs).reshape(half_shape)
    total = total.reshape(half_shape)
    return jnp.where(core == 0, jnp.stack([total, other]), jnp.stack([other, total]))


def shards(labels):
    slab_rows = labels.shape[0]
    map_width = labels.shape[1]
    devices = lax.axis_size("slab")
    my_index = lax.axis_index("slab")
    permit = permittivity(labels)
    smooth = extended_2(permit, (("slab", 0),), 4)
    for sweep_index in range(3):
        smooth = smooth_once(smooth)
    grad_x, grad_y = gradient(smooth)
    scale = jnp.sqrt(grad_x * grad_x + grad_y * grad_y + 1.0)
    normal_x = grad_x / scale
    normal_y = grad_y / scale
    inverse = 1.0 / permit
    contrast = permit - inverse
    fields = jnp.stack(
        [
            permit,
            contrast * normal_x * normal_x,
            contrast * normal_x * normal_y,
            contrast * normal_y * normal_y,
        ]
    )
    padded_keep = -(-KEEP // devices) * devices
    half_keep = -(-HARM // devices) * devices
    frequency = (HARM - 1) - jnp.arange(padded_keep, dtype=jnp.int32)
    col_frequency = (HARM - 1) - jnp.arange(half_keep, dtype=jnp.int32)
    columns = jnp.arange(map_width, dtype=jnp.int32)
    phases = columns[:, None] * col_frequency[None, :] % map_width
    angles = phases.astype(jnp.float32) * (2.0 * math.pi / map_width)
    col_table = jnp.stack([jnp.cos(angles), -jnp.sin(angles)], axis=1)
    half_spectra = jnp.einsum("kxy,ycn->kxcn", fields, col_table, precision=lax.Precision.HIGH)
    my_positions = my_index * slab_rows + jnp.arange(slab_rows, dtype=jnp.int32)
    partial_value = row_transform(half_spectra, my_positions, frequency, map_width)
    summed = line_sum(partial_value, my_index, devices)
    coef = summed / float(map_width * map_width)
    a_in = jnp.arange(padded_keep, dtype=jnp.int32)
    c_in = jnp.arange(half_keep, dtype=jnp.int32)
    b_out = jnp.arange(2 * LANES, dtype=jnp.int32)
    flip_rows = (a_in[None, :] == (KEEP - 1) - a_in[:, None]).astype(jnp.float32)
    keep_cols = ((c_in[:, None] == b_out[None, :]) & (b_out[None, :] < HARM)).astype(jnp.float32)
    mirror_cols = (
        (c_in[:, None] == (KEEP - 1) - b_out[None, :]) & (b_out[None, :] >= HARM)
    ).astype(jnp.float32)
    sign = jnp.array([1.0, -1.0], jnp.float32)[:, None, None, None]
    direct = jnp.einsum("skac,cb->skab", coef, keep_cols, precision=lax.Precision.HIGHEST)
    mirrored = jnp.einsum(
        "ad,skdc,cb->skab", flip_rows, coef, mirror_cols, precision=lax.Precision.HIGHEST
    )
    full = direct + sign * mirrored
    tables = jnp.stack(
        [full[:, 2], full[:, 0] - full[:, 3], full[:, 1] - full[:, 0], -full[:, 2]], axis=1
    )
    rows = ROWS_DEV
    spacing = ORDERS // (rows * devices // 2)
    window_rows = my_index * rows + jnp.arange(rows, dtype=jnp.int32)
    order_index = window_rows // 2 * spacing
    first = order_index // HARM
    second = order_index % HARM
    centre = (HARM - 1) // 2
    kx = 0.3 + 0.02 * (first - centre).astype(jnp.float32)
    ky = 0.2 + 0.02 * (second - centre).astype(jnp.float32)
    lower = window_rows % 2 == 1
    left = jnp.where(lower, ky * ky, kx * ky)
    right = jnp.where(lower, -(kx * ky), -(kx * kx))
    dvals = jnp.stack([left, right])
    a0 = (HARM - 1) - first
    b0 = (HARM - 1) - second
    return assemble(a0, b0, first, second, dvals, tables, rows)


def solution(mesh):
    placed = (P(("layer", "slab"), None),)
    return jax.shard_map(
        shards,
        mesh=mesh,
        in_specs=placed,
        out_specs=P(None, ("layer", "slab"), None),
        check_vma=False,
    )
```

```python
import functools
import math

import jax
import jax.numpy as jnp
from jax import lax
from jax.experimental import pallas as pl
from jax.experimental.pallas import tpu as pltpu
from jax.sharding import PartitionSpec as P

HARM = 101
ROWS_DEV = 64
KEEP = 201
ORDERS = 10201
BLOCK_ROWS = 8
LANES = 128


PERMITS = (1.0, 2.1, 4.0, 12.1)


def extended_2(block, sides, width):
    for axis, dim in sides:
        count = lax.axis_size(axis)
        forward = [(i, i + 1) for i in range(count - 1)]
        forward.append((count - 1, 0))
        backward = [(target, source) for source, target in forward]
        low = lax.ppermute(
            lax.slice_in_dim(block, block.shape[dim] - width, None, axis=dim), axis, forward
        )
        high = lax.ppermute(lax.slice_in_dim(block, 0, width, axis=dim), axis, backward)
        block = jnp.concatenate([low, block, high], axis=dim)
    return block


def permittivity(labels):
    total = jnp.zeros(labels.shape, jnp.float32)
    for index_value in range(4):
        total = total + jnp.where(
            labels == index_value, jnp.float32(PERMITS[index_value]), jnp.float32(0.0)
        )
    return total


def smooth_once(extended):
    middle = extended[1:-1]
    return (
        4.0 * middle
        + extended[:-2]
        + extended[2:]
        + jnp.roll(middle, 1, 1)
        + jnp.roll(middle, -1, 1)
    ) / 8.0


def gradient(extended):
    middle = extended[1:-1]
    grad_x = (extended[2:] - extended[:-2]) / 2.0
    grad_y = (jnp.roll(middle, -1, 1) - jnp.roll(middle, 1, 1)) / 2.0
    return (grad_x, grad_y)


def rim_rows(field_in):
    return extended_2(field_in, (("slab", 0),), 1)


def row_transform(spectra_in, positions, frequency, map_width):
    phases = frequency[:, None] * positions[None, :] % map_width
    angles = phases.astype(jnp.float32) * (2.0 * math.pi / map_width)
    table = jnp.stack([jnp.cos(angles), jnp.sin(angles)])
    products = jnp.einsum("smx,kxcn->skmcn", table, spectra_in, precision=lax.Precision.HIGH)
    real_part = products[0, :, :, 0] + products[1, :, :, 1]
    imag_part = products[0, :, :, 1] - products[1, :, :, 0]
    return jnp.stack([real_part, imag_part])


FIELD_ROWS = 32
RIM = 4


def field_kernel(ext_ref, o_ref, work_ref):
    i = pl.program_id(0)
    start = pl.multiple_of(i * FIELD_ROWS, 8)
    count = FIELD_ROWS + 2 * RIM
    work_ref[pl.ds(0, count), :] = ext_ref[pl.ds(start, count), :]
    width = work_ref.shape[1]
    permit = work_ref[pl.ds(RIM, FIELD_ROWS), :]
    for sweep_index in range(3):
        count -= 2
        middle = work_ref[pl.ds(1, count), :]
        smooth = (
            4.0 * middle
            + work_ref[pl.ds(0, count), :]
            + work_ref[pl.ds(2, count), :]
            + pltpu.roll(middle, 1, 1)
            + pltpu.roll(middle, width - 1, 1)
        ) / 8.0
        work_ref[pl.ds(0, count), :] = smooth
    count -= 2
    middle = work_ref[pl.ds(1, count), :]
    grad_x = (work_ref[pl.ds(2, count), :] - work_ref[pl.ds(0, count), :]) / 2.0
    grad_y = (pltpu.roll(middle, width - 1, 1) - pltpu.roll(middle, 1, 1)) / 2.0
    scale = jnp.sqrt(grad_x * grad_x + grad_y * grad_y + 1.0)
    normal_x = grad_x / scale
    normal_y = grad_y / scale
    inverse = 1.0 / permit
    contrast = permit - inverse
    o_ref[0] = permit
    o_ref[1] = contrast * normal_x * normal_x
    o_ref[2] = contrast * normal_x * normal_y
    o_ref[3] = contrast * normal_y * normal_y


def field_stack(extended):
    rows = extended.shape[0] - 2 * RIM
    width = extended.shape[1]
    return pl.pallas_call(
        field_kernel,
        grid=(rows // FIELD_ROWS,),
        in_specs=[pl.BlockSpec(extended.shape, lambda i: (0, 0))],
        out_specs=pl.BlockSpec((4, FIELD_ROWS, width), lambda i: (0, i, 0)),
        out_shape=jax.ShapeDtypeStruct((4, rows, width), jnp.float32),
        scratch_shapes=[pltpu.VMEM((FIELD_ROWS + 2 * RIM, width), jnp.float32)],
    )(extended)


def chunk_segments(total, half):
    chunks = []
    for start in range(0, total, LANES):
        width = min(LANES, total - start)
        runs = []
        for lane in range(width):
            flat = start + lane
            h, j = divmod(flat, half)
            u, v = divmod(j, HARM)
            if not runs or runs[-1][0] != h or runs[-1][1] != u:
                runs.append((h, u, lane, v))
        chunks.append((start, width, runs))
    return chunks


def assemble_kernel(a0_ref, b0_ref, first_ref, second_ref, dval_ref, fl_ref, o_ref, z_ref):
    s = pl.program_id(0)
    rb = pl.program_id(1)
    span = z_ref.shape[1] // BLOCK_ROWS - BLOCK_ROWS
    lane_iota = lax.broadcasted_iota(jnp.int32, (span, LANES), 1)
    sub = lax.broadcasted_iota(jnp.int32, (BLOCK_ROWS, LANES), 0)
    lane = lax.broadcasted_iota(jnp.int32, (BLOCK_ROWS, LANES), 1)
    for rr in range(BLOCK_ROWS):
        row = rb * BLOCK_ROWS + rr
        a0 = a0_ref[row]
        b0 = b0_ref[row]
        first = first_ref[row]
        second = second_ref[row]
        shift = (LANES - b0) % LANES
        base = pl.multiple_of(a0 // BLOCK_ROWS * BLOCK_ROWS, BLOCK_ROWS)
        off = a0 % BLOCK_ROWS
        dest = pl.multiple_of((BLOCK_ROWS - off) * BLOCK_ROWS, BLOCK_ROWS) + rr
        spot_tile = pl.multiple_of((first + BLOCK_ROWS) * BLOCK_ROWS, BLOCK_ROWS)
        wrap = lane_iota + b0 < LANES
        spot = (sub == rr) & (lane == second)
        for h in range(2):
            combo = 2 * (rr % 2) + h
            x_lo = fl_ref[0, combo, pl.ds(base, span), pl.ds(0, LANES)]
            x_hi = fl_ref[0, combo, pl.ds(base, span), pl.ds(LANES, LANES)]
            x = jnp.where(wrap, pltpu.roll(x_lo, shift, 1), pltpu.roll(x_hi, shift, 1))
            z_ref[h, pl.ds(dest, span, stride=BLOCK_ROWS), :] = x
            d = jnp.where(s == 0, dval_ref[h, row], jnp.float32(0.0))
            tile = z_ref[h, pl.ds(spot_tile, BLOCK_ROWS), :]
            z_ref[h, pl.ds(spot_tile, BLOCK_ROWS), :] = tile + jnp.where(spot, d, jnp.float32(0.0))
    placed = {}
    for start, width, runs in chunk_segments(o_ref.shape[2], o_ref.shape[2] // 2):
        acc = None
        for h, u, l0, v0 in runs:
            if (h, u) not in placed:
                src = z_ref[h, pl.ds((u + BLOCK_ROWS) * BLOCK_ROWS, BLOCK_ROWS), :]
                sh = (l0 - v0) % LANES
                placed[(h, u)] = pltpu.roll(src, sh, 1) if sh else src
            src = placed[(h, u)]
            acc = src if acc is None else jnp.where(lane >= l0, src, acc)
        if width < LANES:
            acc = acc[:, :width]
        o_ref[0, :, pl.ds(start, width)] = acc


def assemble(a0, b0, first, second, dvals, tables, rows):
    span = 112
    n_blocks = rows // BLOCK_ROWS
    total = 2 * ORDERS
    grid_spec = pltpu.PrefetchScalarGridSpec(
        num_scalar_prefetch=4,
        grid=(2, n_blocks),
        in_specs=[
            pl.BlockSpec(memory_space=pltpu.SMEM),
            pl.BlockSpec((1,) + tables.shape[1:], lambda s, rb, *_: (s, 0, 0, 0)),
        ],
        out_specs=pl.BlockSpec((1, BLOCK_ROWS, total), lambda s, rb, *_: (s, rb, 0)),
        scratch_shapes=[pltpu.VMEM((2, (span + BLOCK_ROWS) * BLOCK_ROWS, LANES), jnp.float32)],
    )
    return pl.pallas_call(
        assemble_kernel,
        grid_spec=grid_spec,
        out_shape=jax.ShapeDtypeStruct((2, rows, total), jnp.float32),
        compiler_params=pltpu.CompilerParams(dimension_semantics=("arbitrary", "arbitrary")),
    )(a0, b0, first, second, dvals, tables)


def line_sum(partial_value, my_index, devices):
    core = my_index % 2
    pairs = [(i, i ^ 1) for i in range(devices)]
    half_shape = partial_value.shape[1:]
    dense = (-1, LANES) if math.prod(half_shape) % LANES == 0 else half_shape
    keep = jnp.where(core == 0, partial_value[0], partial_value[1]).reshape(dense)
    give = jnp.where(core == 0, partial_value[1], partial_value[0]).reshape(dense)
    mine = keep + lax.ppermute(give, "slab", pairs)
    chips = devices // 2
    if chips & (chips - 1) == 0:
        total = mine
        bit = 2
        while bit < devices:
            total = total + lax.ppermute(total, "slab", [(i, i ^ bit) for i in range(devices)])
            bit *= 2
    else:
        right = [(i, i + 2) for i in range(devices - 2)]
        left = [(i + 2, i) for i in range(devices - 2)]
        from_left = jnp.zeros_like(mine)
        from_right = jnp.zeros_like(mine)
        for step in range(chips - 1):
            from_left, from_right = (
                lax.ppermute(mine + from_left, "slab", right),
                lax.ppermute(mine + from_right, "slab", left),
            )
        total = mine + from_left + from_right
    other = lax.ppermute(total, "slab", pairs).reshape(half_shape)
    total = total.reshape(half_shape)
    return jnp.where(core == 0, jnp.stack([total, other]), jnp.stack([other, total]))


def shards(labels):
    slab_rows = labels.shape[0]
    map_width = labels.shape[1]
    devices = lax.axis_size("slab")
    my_index = lax.axis_index("slab")
    permit = permittivity(labels)
    fields = field_stack(extended_2(permit, (("slab", 0),), RIM))
    padded_keep = -(-KEEP // devices) * devices
    half_keep = -(-HARM // devices) * devices
    frequency = (HARM - 1) - jnp.arange(padded_keep, dtype=jnp.int32)
    col_frequency = (HARM - 1) - jnp.arange(half_keep, dtype=jnp.int32)
    columns = jnp.arange(map_width, dtype=jnp.int32)
    phases = columns[:, None] * col_frequency[None, :] % map_width
    angles = phases.astype(jnp.float32) * (2.0 * math.pi / map_width)
    col_table = jnp.stack([jnp.cos(angles), -jnp.sin(angles)], axis=1)
    half_spectra = jnp.einsum("kxy,ycn->kxcn", fields, col_table, precision=lax.Precision.HIGH)
    my_positions = my_index * slab_rows + jnp.arange(slab_rows, dtype=jnp.int32)
    partial_value = row_transform(half_spectra, my_positions, frequency, map_width)
    summed = line_sum(partial_value, my_index, devices)
    coef = summed / float(map_width * map_width)
    a_in = jnp.arange(padded_keep, dtype=jnp.int32)
    c_in = jnp.arange(half_keep, dtype=jnp.int32)
    b_out = jnp.arange(2 * LANES, dtype=jnp.int32)
    flip_rows = (a_in[None, :] == (KEEP - 1) - a_in[:, None]).astype(jnp.float32)
    keep_cols = ((c_in[:, None] == b_out[None, :]) & (b_out[None, :] < HARM)).astype(jnp.float32)
    mirror_cols = (
        (c_in[:, None] == (KEEP - 1) - b_out[None, :]) & (b_out[None, :] >= HARM)
    ).astype(jnp.float32)
    sign = jnp.array([1.0, -1.0], jnp.float32)[:, None, None, None]
    direct = jnp.einsum("skac,cb->skab", coef, keep_cols, precision=lax.Precision.HIGHEST)
    mirrored = jnp.einsum(
        "ad,skdc,cb->skab", flip_rows, coef, mirror_cols, precision=lax.Precision.HIGHEST
    )
    full = direct + sign * mirrored
    tables = jnp.stack(
        [full[:, 2], full[:, 0] - full[:, 3], full[:, 1] - full[:, 0], -full[:, 2]], axis=1
    )
    rows = ROWS_DEV
    spacing = ORDERS // (rows * devices // 2)
    window_rows = my_index * rows + jnp.arange(rows, dtype=jnp.int32)
    order_index = window_rows // 2 * spacing
    first = order_index // HARM
    second = order_index % HARM
    centre = (HARM - 1) // 2
    kx = 0.3 + 0.02 * (first - centre).astype(jnp.float32)
    ky = 0.2 + 0.02 * (second - centre).astype(jnp.float32)
    lower = window_rows % 2 == 1
    left = jnp.where(lower, ky * ky, kx * ky)
    right = jnp.where(lower, -(kx * ky), -(kx * kx))
    dvals = jnp.stack([left, right])
    a0 = (HARM - 1) - first
    b0 = (HARM - 1) - second
    return assemble(a0, b0, first, second, dvals, tables, rows)


def solution(mesh):
    placed = (P(("layer", "slab"), None),)
    return jax.shard_map(
        shards,
        mesh=mesh,
        in_specs=placed,
        out_specs=P(None, ("layer", "slab"), None),
        check_vma=False,
    )
```

```python
import functools
import math

import jax
import jax.numpy as jnp
from jax import lax
from jax.experimental import pallas as pl
from jax.experimental.pallas import tpu as pltpu
from jax.sharding import PartitionSpec as P

HARM = 101
ROWS_DEV = 64
KEEP = 201
ORDERS = 10201
BLOCK_ROWS = 8
LANES = 128


PERMITS = (1.0, 2.1, 4.0, 12.1)


def extended_2(block, sides, width):
    for axis, dim in sides:
        count = lax.axis_size(axis)
        forward = [(i, i + 1) for i in range(count - 1)]
        forward.append((count - 1, 0))
        backward = [(target, source) for source, target in forward]
        low = lax.ppermute(
            lax.slice_in_dim(block, block.shape[dim] - width, None, axis=dim), axis, forward
        )
        high = lax.ppermute(lax.slice_in_dim(block, 0, width, axis=dim), axis, backward)
        block = jnp.concatenate([low, block, high], axis=dim)
    return block


def permittivity(labels):
    total = jnp.zeros(labels.shape, jnp.float32)
    for index_value in range(4):
        total = total + jnp.where(
            labels == index_value, jnp.float32(PERMITS[index_value]), jnp.float32(0.0)
        )
    return total


def smooth_once(extended):
    middle = extended[1:-1]
    return (
        4.0 * middle
        + extended[:-2]
        + extended[2:]
        + jnp.roll(middle, 1, 1)
        + jnp.roll(middle, -1, 1)
    ) / 8.0


def gradient(extended):
    middle = extended[1:-1]
    grad_x = (extended[2:] - extended[:-2]) / 2.0
    grad_y = (jnp.roll(middle, -1, 1) - jnp.roll(middle, 1, 1)) / 2.0
    return (grad_x, grad_y)


def rim_rows(field_in):
    return extended_2(field_in, (("slab", 0),), 1)


def row_transform(spectra_in, positions, frequency, map_width):
    phases = frequency[:, None] * positions[None, :] % map_width
    angles = phases.astype(jnp.float32) * (2.0 * math.pi / map_width)
    table = jnp.stack([jnp.cos(angles), jnp.sin(angles)])
    products = jnp.einsum("smx,kxcn->skmcn", table, spectra_in, precision=lax.Precision.HIGH)
    real_part = products[0, :, :, 0] + products[1, :, :, 1]
    imag_part = products[0, :, :, 1] - products[1, :, :, 0]
    return jnp.stack([real_part, imag_part])


def chunk_segments(total, half):
    chunks = []
    for start in range(0, total, LANES):
        width = min(LANES, total - start)
        runs = []
        for lane in range(width):
            flat = start + lane
            h, j = divmod(flat, half)
            u, v = divmod(j, HARM)
            if not runs or runs[-1][0] != h or runs[-1][1] != u:
                runs.append((h, u, lane, v))
        chunks.append((start, width, runs))
    return chunks


def assemble_kernel(a0_ref, b0_ref, first_ref, second_ref, dval_ref, fl_ref, o_ref, z_ref):
    s = pl.program_id(0)
    rb = pl.program_id(1)
    span = z_ref.shape[1] // BLOCK_ROWS - BLOCK_ROWS
    lane_iota = lax.broadcasted_iota(jnp.int32, (span, LANES), 1)
    sub = lax.broadcasted_iota(jnp.int32, (BLOCK_ROWS, LANES), 0)
    lane = lax.broadcasted_iota(jnp.int32, (BLOCK_ROWS, LANES), 1)
    for rr in range(BLOCK_ROWS):
        row = rb * BLOCK_ROWS + rr
        a0 = a0_ref[row]
        b0 = b0_ref[row]
        first = first_ref[row]
        second = second_ref[row]
        shift = (LANES - b0) % LANES
        base = pl.multiple_of(a0 // BLOCK_ROWS * BLOCK_ROWS, BLOCK_ROWS)
        off = a0 % BLOCK_ROWS
        dest = pl.multiple_of((BLOCK_ROWS - off) * BLOCK_ROWS, BLOCK_ROWS) + rr
        spot_tile = pl.multiple_of((first + BLOCK_ROWS) * BLOCK_ROWS, BLOCK_ROWS)
        wrap = lane_iota + b0 < LANES
        spot = (sub == rr) & (lane == second)
        for h in range(2):
            combo = 2 * (rr % 2) + h
            x_lo = fl_ref[0, combo, pl.ds(base, span), pl.ds(0, LANES)]
            x_hi = fl_ref[0, combo, pl.ds(base, span), pl.ds(LANES, LANES)]
            x = jnp.where(wrap, pltpu.roll(x_lo, shift, 1), pltpu.roll(x_hi, shift, 1))
            z_ref[h, pl.ds(dest, span, stride=BLOCK_ROWS), :] = x
            d = jnp.where(s == 0, dval_ref[h, row], jnp.float32(0.0))
            tile = z_ref[h, pl.ds(spot_tile, BLOCK_ROWS), :]
            z_ref[h, pl.ds(spot_tile, BLOCK_ROWS), :] = tile + jnp.where(spot, d, jnp.float32(0.0))
    placed = {}
    for start, width, runs in chunk_segments(o_ref.shape[2], o_ref.shape[2] // 2):
        acc = None
        for h, u, l0, v0 in runs:
            if (h, u) not in placed:
                src = z_ref[h, pl.ds((u + BLOCK_ROWS) * BLOCK_ROWS, BLOCK_ROWS), :]
                sh = (l0 - v0) % LANES
                placed[(h, u)] = pltpu.roll(src, sh, 1) if sh else src
            src = placed[(h, u)]
            acc = src if acc is None else jnp.where(lane >= l0, src, acc)
        if width < LANES:
            acc = acc[:, :width]
        o_ref[0, :, pl.ds(start, width)] = acc


def assemble(a0, b0, first, second, dvals, tables, rows):
    span = 112
    n_blocks = rows // BLOCK_ROWS
    total = 2 * ORDERS
    grid_spec = pltpu.PrefetchScalarGridSpec(
        num_scalar_prefetch=4,
        grid=(2, n_blocks),
        in_specs=[
            pl.BlockSpec(memory_space=pltpu.SMEM),
            pl.BlockSpec((1,) + tables.shape[1:], lambda s, rb, *_: (s, 0, 0, 0)),
        ],
        out_specs=pl.BlockSpec((1, BLOCK_ROWS, total), lambda s, rb, *_: (s, rb, 0)),
        scratch_shapes=[pltpu.VMEM((2, (span + BLOCK_ROWS) * BLOCK_ROWS, LANES), jnp.float32)],
    )
    return pl.pallas_call(
        assemble_kernel,
        grid_spec=grid_spec,
        out_shape=jax.ShapeDtypeStruct((2, rows, total), jnp.float32),
        compiler_params=pltpu.CompilerParams(dimension_semantics=("arbitrary", "arbitrary")),
    )(a0, b0, first, second, dvals, tables)


def line_sum(partial_value, my_index, devices):
    core = my_index % 2
    pairs = [(i, i ^ 1) for i in range(devices)]
    half_shape = partial_value.shape[1:]
    dense = (-1, LANES) if math.prod(half_shape) % LANES == 0 else half_shape
    keep = jnp.where(core == 0, partial_value[0], partial_value[1]).reshape(dense)
    give = jnp.where(core == 0, partial_value[1], partial_value[0]).reshape(dense)
    mine = keep + lax.ppermute(give, "slab", pairs)
    chips = devices // 2
    if chips & (chips - 1) == 0 and chips > 1 and len(dense) == 2:
        rows = mine.shape[0]
        padded = -(-rows // 16) * 16
        grown = jnp.pad(mine, ((0, padded - rows), (0, 0)))
        upper = (my_index // 2) % 2
        halves = (grown[: padded // 2], grown[padded // 2 :])
        pair = [(i, i ^ 2) for i in range(devices)]
        kept = jnp.where(upper == 0, halves[0], halves[1])
        sent = jnp.where(upper == 0, halves[1], halves[0])
        kept = kept + lax.ppermute(sent, "slab", pair)
        bit = 4
        while bit < devices:
            kept = kept + lax.ppermute(kept, "slab", [(i, i ^ bit) for i in range(devices)])
            bit *= 2
        back = lax.ppermute(kept, "slab", pair)
        total = jnp.where(
            upper == 0, jnp.concatenate([kept, back]), jnp.concatenate([back, kept])
        )[:rows]
    else:
        right = [(i, i + 2) for i in range(devices - 2)]
        left = [(i + 2, i) for i in range(devices - 2)]
        from_left = jnp.zeros_like(mine)
        from_right = jnp.zeros_like(mine)
        for step in range(chips - 1):
            from_left, from_right = (
                lax.ppermute(mine + from_left, "slab", right),
                lax.ppermute(mine + from_right, "slab", left),
            )
        total = mine + from_left + from_right
    other = lax.ppermute(total, "slab", pairs).reshape(half_shape)
    total = total.reshape(half_shape)
    return jnp.where(core == 0, jnp.stack([total, other]), jnp.stack([other, total]))


def shards(labels):
    slab_rows = labels.shape[0]
    map_width = labels.shape[1]
    devices = lax.axis_size("slab")
    my_index = lax.axis_index("slab")
    permit = permittivity(labels)
    smooth = extended_2(permit, (("slab", 0),), 4)
    for sweep_index in range(3):
        smooth = smooth_once(smooth)
    grad_x, grad_y = gradient(smooth)
    scale = jnp.sqrt(grad_x * grad_x + grad_y * grad_y + 1.0)
    normal_x = grad_x / scale
    normal_y = grad_y / scale
    inverse = 1.0 / permit
    contrast = permit - inverse
    fields = jnp.stack(
        [
            permit,
            contrast * normal_x * normal_x,
            contrast * normal_x * normal_y,
            contrast * normal_y * normal_y,
        ]
    )
    padded_keep = -(-KEEP // devices) * devices
    half_keep = -(-HARM // devices) * devices
    frequency = (HARM - 1) - jnp.arange(padded_keep, dtype=jnp.int32)
    col_frequency = (HARM - 1) - jnp.arange(half_keep, dtype=jnp.int32)
    columns = jnp.arange(map_width, dtype=jnp.int32)
    phases = columns[:, None] * col_frequency[None, :] % map_width
    angles = phases.astype(jnp.float32) * (2.0 * math.pi / map_width)
    col_table = jnp.stack([jnp.cos(angles), -jnp.sin(angles)], axis=1)
    half_spectra = jnp.einsum("kxy,ycn->kxcn", fields, col_table, precision=lax.Precision.HIGH)
    my_positions = my_index * slab_rows + jnp.arange(slab_rows, dtype=jnp.int32)
    partial_value = row_transform(half_spectra, my_positions, frequency, map_width)
    summed = line_sum(partial_value, my_index, devices)
    coef = summed / float(map_width * map_width)
    a_in = jnp.arange(padded_keep, dtype=jnp.int32)
    c_in = jnp.arange(half_keep, dtype=jnp.int32)
    b_out = jnp.arange(2 * LANES, dtype=jnp.int32)
    flip_rows = (a_in[None, :] == (KEEP - 1) - a_in[:, None]).astype(jnp.float32)
    keep_cols = ((c_in[:, None] == b_out[None, :]) & (b_out[None, :] < HARM)).astype(jnp.float32)
    mirror_cols = (
        (c_in[:, None] == (KEEP - 1) - b_out[None, :]) & (b_out[None, :] >= HARM)
    ).astype(jnp.float32)
    sign = jnp.array([1.0, -1.0], jnp.float32)[:, None, None, None]
    direct = jnp.einsum("skac,cb->skab", coef, keep_cols, precision=lax.Precision.HIGHEST)
    mirrored = jnp.einsum(
        "ad,skdc,cb->skab", flip_rows, coef, mirror_cols, precision=lax.Precision.HIGHEST
    )
    full = direct + sign * mirrored
    tables = jnp.stack(
        [full[:, 2], full[:, 0] - full[:, 3], full[:, 1] - full[:, 0], -full[:, 2]], axis=1
    )
    rows = ROWS_DEV
    spacing = ORDERS // (rows * devices // 2)
    window_rows = my_index * rows + jnp.arange(rows, dtype=jnp.int32)
    order_index = window_rows // 2 * spacing
    first = order_index // HARM
    second = order_index % HARM
    centre = (HARM - 1) // 2
    kx = 0.3 + 0.02 * (first - centre).astype(jnp.float32)
    ky = 0.2 + 0.02 * (second - centre).astype(jnp.float32)
    lower = window_rows % 2 == 1
    left = jnp.where(lower, ky * ky, kx * ky)
    right = jnp.where(lower, -(kx * ky), -(kx * kx))
    dvals = jnp.stack([left, right])
    a0 = (HARM - 1) - first
    b0 = (HARM - 1) - second
    return assemble(a0, b0, first, second, dvals, tables, rows)


def solution(mesh):
    placed = (P(("layer", "slab"), None),)
    return jax.shard_map(
        shards,
        mesh=mesh,
        in_specs=placed,
        out_specs=P(None, ("layer", "slab"), None),
        check_vma=False,
    )
```

```python
import functools
import math

import jax
import jax.numpy as jnp
from jax import lax
from jax.experimental import pallas as pl
from jax.experimental.pallas import tpu as pltpu
from jax.sharding import PartitionSpec as P

HARM = 101
ROWS_DEV = 64
KEEP = 201
ORDERS = 10201
BLOCK_ROWS = 8
LANES = 128


PERMITS = (1.0, 2.1, 4.0, 12.1)


def extended_2(block, sides, width):
    for axis, dim in sides:
        count = lax.axis_size(axis)
        forward = [(i, i + 1) for i in range(count - 1)]
        forward.append((count - 1, 0))
        backward = [(target, source) for source, target in forward]
        low = lax.ppermute(
            lax.slice_in_dim(block, block.shape[dim] - width, None, axis=dim), axis, forward
        )
        high = lax.ppermute(lax.slice_in_dim(block, 0, width, axis=dim), axis, backward)
        block = jnp.concatenate([low, block, high], axis=dim)
    return block


def permittivity(labels):
    total = jnp.zeros(labels.shape, jnp.float32)
    for index_value in range(4):
        total = total + jnp.where(
            labels == index_value, jnp.float32(PERMITS[index_value]), jnp.float32(0.0)
        )
    return total


def smooth_once(extended):
    middle = extended[1:-1]
    return (
        4.0 * middle
        + extended[:-2]
        + extended[2:]
        + jnp.roll(middle, 1, 1)
        + jnp.roll(middle, -1, 1)
    ) / 8.0


def gradient(extended):
    middle = extended[1:-1]
    grad_x = (extended[2:] - extended[:-2]) / 2.0
    grad_y = (jnp.roll(middle, -1, 1) - jnp.roll(middle, 1, 1)) / 2.0
    return (grad_x, grad_y)


def rim_rows(field_in):
    return extended_2(field_in, (("slab", 0),), 1)


def row_transform(spectra_in, positions, frequency, map_width):
    phases = frequency[:, None] * positions[None, :] % map_width
    angles = phases.astype(jnp.float32) * (2.0 * math.pi / map_width)
    table = jnp.stack([jnp.cos(angles), jnp.sin(angles)])
    products = jnp.einsum("smx,kxcn->skmcn", table, spectra_in, precision=lax.Precision.HIGH)
    real_part = products[0, :, :, 0] + products[1, :, :, 1]
    imag_part = products[0, :, :, 1] - products[1, :, :, 0]
    return jnp.stack([real_part, imag_part])


def chunk_segments(total, half):
    chunks = []
    for start in range(0, total, LANES):
        width = min(LANES, total - start)
        runs = []
        for lane in range(width):
            flat = start + lane
            h, j = divmod(flat, half)
            u, v = divmod(j, HARM)
            if not runs or runs[-1][0] != h or runs[-1][1] != u:
                runs.append((h, u, lane, v))
        chunks.append((start, width, runs))
    return chunks


def assemble_kernel(a0_ref, b0_ref, first_ref, second_ref, dval_ref, fl_ref, o_ref, z_ref):
    s = pl.program_id(0)
    rb = pl.program_id(1)
    span = z_ref.shape[1] // BLOCK_ROWS - BLOCK_ROWS
    lane_iota = lax.broadcasted_iota(jnp.int32, (span, LANES), 1)
    sub = lax.broadcasted_iota(jnp.int32, (BLOCK_ROWS, LANES), 0)
    lane = lax.broadcasted_iota(jnp.int32, (BLOCK_ROWS, LANES), 1)
    for rr in range(BLOCK_ROWS):
        row = rb * BLOCK_ROWS + rr
        a0 = a0_ref[row]
        b0 = b0_ref[row]
        first = first_ref[row]
        second = second_ref[row]
        shift = (LANES - b0) % LANES
        base = pl.multiple_of(a0 // BLOCK_ROWS * BLOCK_ROWS, BLOCK_ROWS)
        off = a0 % BLOCK_ROWS
        dest = pl.multiple_of((BLOCK_ROWS - off) * BLOCK_ROWS, BLOCK_ROWS) + rr
        spot_tile = pl.multiple_of((first + BLOCK_ROWS) * BLOCK_ROWS, BLOCK_ROWS)
        wrap = lane_iota + b0 < LANES
        spot = (sub == rr) & (lane == second)
        for h in range(2):
            combo = 2 * (rr % 2) + h
            x_lo = fl_ref[0, combo, pl.ds(base, span), pl.ds(0, LANES)]
            x_hi = fl_ref[0, combo, pl.ds(base, span), pl.ds(LANES, LANES)]
            x = jnp.where(wrap, pltpu.roll(x_lo, shift, 1), pltpu.roll(x_hi, shift, 1))
            z_ref[h, pl.ds(dest, span, stride=BLOCK_ROWS), :] = x
            d = jnp.where(s == 0, dval_ref[h, row], jnp.float32(0.0))
            tile = z_ref[h, pl.ds(spot_tile, BLOCK_ROWS), :]
            z_ref[h, pl.ds(spot_tile, BLOCK_ROWS), :] = tile + jnp.where(spot, d, jnp.float32(0.0))
    placed = {}
    for start, width, runs in chunk_segments(o_ref.shape[2], o_ref.shape[2] // 2):
        acc = None
        for h, u, l0, v0 in runs:
            if (h, u) not in placed:
                src = z_ref[h, pl.ds((u + BLOCK_ROWS) * BLOCK_ROWS, BLOCK_ROWS), :]
                sh = (l0 - v0) % LANES
                placed[(h, u)] = pltpu.roll(src, sh, 1) if sh else src
            src = placed[(h, u)]
            acc = src if acc is None else jnp.where(lane >= l0, src, acc)
        if width < LANES:
            acc = acc[:, :width]
        o_ref[0, :, pl.ds(start, width)] = acc


def assemble(a0, b0, first, second, dvals, tables, rows):
    span = 112
    n_blocks = rows // BLOCK_ROWS
    total = 2 * ORDERS
    grid_spec = pltpu.PrefetchScalarGridSpec(
        num_scalar_prefetch=4,
        grid=(2, n_blocks),
        in_specs=[
            pl.BlockSpec(memory_space=pltpu.SMEM),
            pl.BlockSpec((1,) + tables.shape[1:], lambda s, rb, *_: (s, 0, 0, 0)),
        ],
        out_specs=pl.BlockSpec((1, BLOCK_ROWS, total), lambda s, rb, *_: (s, rb, 0)),
        scratch_shapes=[pltpu.VMEM((2, (span + BLOCK_ROWS) * BLOCK_ROWS, LANES), jnp.float32)],
    )
    return pl.pallas_call(
        assemble_kernel,
        grid_spec=grid_spec,
        out_shape=jax.ShapeDtypeStruct((2, rows, total), jnp.float32),
        compiler_params=pltpu.CompilerParams(dimension_semantics=("arbitrary", "arbitrary")),
    )(a0, b0, first, second, dvals, tables)


def line_sum(partial_value, my_index, devices):
    core = my_index % 2
    pairs = [(i, i ^ 1) for i in range(devices)]
    half_shape = partial_value.shape[1:]
    dense = (-1, LANES) if math.prod(half_shape) % LANES == 0 else half_shape
    keep = jnp.where(core == 0, partial_value[0], partial_value[1]).reshape(dense)
    give = jnp.where(core == 0, partial_value[1], partial_value[0]).reshape(dense)
    mine = keep + lax.ppermute(give, "slab", pairs)
    chips = devices // 2
    if chips & (chips - 1) == 0 and chips > 1 and len(dense) == 2:
        rows = mine.shape[0]
        padded = -(-rows // 16) * 16
        grown = jnp.pad(mine, ((0, padded - rows), (0, 0)))
        upper = (my_index // 2) % 2
        halves = (grown[: padded // 2], grown[padded // 2 :])
        pair = [(i, i ^ 2) for i in range(devices)]
        kept = jnp.where(upper == 0, halves[0], halves[1])
        sent = jnp.where(upper == 0, halves[1], halves[0])
        kept = kept + lax.ppermute(sent, "slab", pair)
        bit = 4
        while bit < devices:
            kept = kept + lax.ppermute(kept, "slab", [(i, i ^ bit) for i in range(devices)])
            bit *= 2
        back = lax.ppermute(kept, "slab", pair)
        total = jnp.where(
            upper == 0, jnp.concatenate([kept, back]), jnp.concatenate([back, kept])
        )[:rows]
    else:
        right = [(i, i + 2) for i in range(devices - 2)]
        left = [(i + 2, i) for i in range(devices - 2)]
        from_left = jnp.zeros_like(mine)
        from_right = jnp.zeros_like(mine)
        for step in range(chips - 1):
            from_left, from_right = (
                lax.ppermute(mine + from_left, "slab", right),
                lax.ppermute(mine + from_right, "slab", left),
            )
        total = mine + from_left + from_right
    other = lax.ppermute(total, "slab", pairs).reshape(half_shape)
    total = total.reshape(half_shape)
    return jnp.where(core == 0, jnp.stack([total, other]), jnp.stack([other, total]))


def shards(labels):
    slab_rows = labels.shape[0]
    map_width = labels.shape[1]
    devices = lax.axis_size("slab")
    my_index = lax.axis_index("slab")
    permit = permittivity(labels)
    padded_keep = -(-KEEP // devices) * devices
    half_keep = -(-HARM // devices) * devices
    frequency = (HARM - 1) - jnp.arange(padded_keep, dtype=jnp.int32)
    col_frequency = (HARM - 1) - jnp.arange(half_keep, dtype=jnp.int32)
    columns = jnp.arange(map_width, dtype=jnp.int32)
    phases = columns[:, None] * col_frequency[None, :] % map_width
    angles = phases.astype(jnp.float32) * (2.0 * math.pi / map_width)
    col_table = jnp.stack([jnp.cos(angles), -jnp.sin(angles)], axis=1)
    col_table, permit = lax.optimization_barrier((col_table, permit))
    smooth = extended_2(permit, (("slab", 0),), 4)
    for sweep_index in range(3):
        smooth = smooth_once(smooth)
    grad_x, grad_y = gradient(smooth)
    scale = jnp.sqrt(grad_x * grad_x + grad_y * grad_y + 1.0)
    normal_x = grad_x / scale
    normal_y = grad_y / scale
    inverse = 1.0 / permit
    contrast = permit - inverse
    fields = jnp.stack(
        [
            permit,
            contrast * normal_x * normal_x,
            contrast * normal_x * normal_y,
            contrast * normal_y * normal_y,
        ]
    )
    half_spectra = jnp.einsum("kxy,ycn->kxcn", fields, col_table, precision=lax.Precision.HIGH)
    my_positions = my_index * slab_rows + jnp.arange(slab_rows, dtype=jnp.int32)
    partial_value = row_transform(half_spectra, my_positions, frequency, map_width)
    summed = line_sum(partial_value, my_index, devices)
    coef = summed / float(map_width * map_width)
    a_in = jnp.arange(padded_keep, dtype=jnp.int32)
    c_in = jnp.arange(half_keep, dtype=jnp.int32)
    b_out = jnp.arange(2 * LANES, dtype=jnp.int32)
    flip_rows = (a_in[None, :] == (KEEP - 1) - a_in[:, None]).astype(jnp.float32)
    keep_cols = ((c_in[:, None] == b_out[None, :]) & (b_out[None, :] < HARM)).astype(jnp.float32)
    mirror_cols = (
        (c_in[:, None] == (KEEP - 1) - b_out[None, :]) & (b_out[None, :] >= HARM)
    ).astype(jnp.float32)
    sign = jnp.array([1.0, -1.0], jnp.float32)[:, None, None, None]
    direct = jnp.einsum("skac,cb->skab", coef, keep_cols, precision=lax.Precision.HIGHEST)
    mirrored = jnp.einsum(
        "ad,skdc,cb->skab", flip_rows, coef, mirror_cols, precision=lax.Precision.HIGHEST
    )
    full = direct + sign * mirrored
    tables = jnp.stack(
        [full[:, 2], full[:, 0] - full[:, 3], full[:, 1] - full[:, 0], -full[:, 2]], axis=1
    )
    rows = ROWS_DEV
    spacing = ORDERS // (rows * devices // 2)
    window_rows = my_index * rows + jnp.arange(rows, dtype=jnp.int32)
    order_index = window_rows // 2 * spacing
    first = order_index // HARM
    second = order_index % HARM
    centre = (HARM - 1) // 2
    kx = 0.3 + 0.02 * (first - centre).astype(jnp.float32)
    ky = 0.2 + 0.02 * (second - centre).astype(jnp.float32)
    lower = window_rows % 2 == 1
    left = jnp.where(lower, ky * ky, kx * ky)
    right = jnp.where(lower, -(kx * ky), -(kx * kx))
    dvals = jnp.stack([left, right])
    a0 = (HARM - 1) - first
    b0 = (HARM - 1) - second
    return assemble(a0, b0, first, second, dvals, tables, rows)


def solution(mesh):
    placed = (P(("layer", "slab"), None),)
    return jax.shard_map(
        shards,
        mesh=mesh,
        in_specs=placed,
        out_specs=P(None, ("layer", "slab"), None),
        check_vma=False,
    )
```

```python
import functools
import math

import jax
import jax.numpy as jnp
from jax import lax
from jax.experimental import pallas as pl
from jax.experimental.pallas import tpu as pltpu
from jax.sharding import PartitionSpec as P

HARM = 101
ROWS_DEV = 64
KEEP = 201
ORDERS = 10201
BLOCK_ROWS = 8
COPIES = 4
COPY_STEP = 28
LANES = 128


PERMITS = (1.0, 2.1, 4.0, 12.1)


def extended_2(block, sides, width):
    for axis, dim in sides:
        count = lax.axis_size(axis)
        forward = [(i, i + 1) for i in range(count - 1)]
        forward.append((count - 1, 0))
        backward = [(target, source) for source, target in forward]
        low = lax.ppermute(
            lax.slice_in_dim(block, block.shape[dim] - width, None, axis=dim), axis, forward
        )
        high = lax.ppermute(lax.slice_in_dim(block, 0, width, axis=dim), axis, backward)
        block = jnp.concatenate([low, block, high], axis=dim)
    return block


def permittivity(labels):
    total = jnp.zeros(labels.shape, jnp.float32)
    for index_value in range(4):
        total = total + jnp.where(
            labels == index_value, jnp.float32(PERMITS[index_value]), jnp.float32(0.0)
        )
    return total


def smooth_once(extended):
    middle = extended[1:-1]
    return (
        4.0 * middle
        + extended[:-2]
        + extended[2:]
        + jnp.roll(middle, 1, 1)
        + jnp.roll(middle, -1, 1)
    ) / 8.0


def gradient(extended):
    middle = extended[1:-1]
    grad_x = (extended[2:] - extended[:-2]) / 2.0
    grad_y = (jnp.roll(middle, -1, 1) - jnp.roll(middle, 1, 1)) / 2.0
    return (grad_x, grad_y)


def rim_rows(field_in):
    return extended_2(field_in, (("slab", 0),), 1)


def row_transform(spectra_in, positions, frequency, map_width):
    phases = frequency[:, None] * positions[None, :] % map_width
    angles = phases.astype(jnp.float32) * (2.0 * math.pi / map_width)
    table = jnp.stack([jnp.cos(angles), jnp.sin(angles)])
    products = jnp.einsum("smx,kxcn->skmcn", table, spectra_in, precision=lax.Precision.HIGH)
    real_part = products[0, :, :, 0] + products[1, :, :, 1]
    imag_part = products[0, :, :, 1] - products[1, :, :, 0]
    return jnp.stack([real_part, imag_part])


def chunk_segments(total, half):
    chunks = []
    for start in range(0, total, LANES):
        width = min(LANES, total - start)
        runs = []
        for lane in range(width):
            flat = start + lane
            h, j = divmod(flat, half)
            u, v = divmod(j, HARM)
            if not runs or runs[-1][0] != h or runs[-1][1] != u:
                runs.append((h, u, lane, v))
        chunks.append((start, width, runs))
    return chunks


def assemble_kernel(a0_ref, b0_ref, first_ref, second_ref, dval_ref, fl_ref, o_ref, z_ref):
    s = pl.program_id(0)
    rb = pl.program_id(1)
    span = z_ref.shape[1] // BLOCK_ROWS - BLOCK_ROWS
    lane_iota = lax.broadcasted_iota(jnp.int32, (span, LANES), 1)
    sub = lax.broadcasted_iota(jnp.int32, (BLOCK_ROWS, LANES), 0)
    lane = lax.broadcasted_iota(jnp.int32, (BLOCK_ROWS, LANES), 1)
    for rr in range(BLOCK_ROWS):
        row = rb * BLOCK_ROWS + rr
        a0 = a0_ref[row]
        b0 = b0_ref[row]
        first = first_ref[row]
        second = second_ref[row]
        copy = jnp.minimum(b0 // COPY_STEP, COPIES - 1)
        shift = (LANES - (b0 - COPY_STEP * copy)) % LANES
        base = pl.multiple_of(a0 // BLOCK_ROWS * BLOCK_ROWS, BLOCK_ROWS)
        off = a0 % BLOCK_ROWS
        dest = pl.multiple_of((BLOCK_ROWS - off) * BLOCK_ROWS, BLOCK_ROWS) + rr
        spot_tile = pl.multiple_of((first + BLOCK_ROWS) * BLOCK_ROWS, BLOCK_ROWS)
        spot = (sub == rr) & (lane == second)
        for h in range(2):
            combo = 2 * (rr % 2) + h
            x = fl_ref[0, copy, combo, pl.ds(base, span), :]
            x = pltpu.roll(x, shift, 1)
            z_ref[h, pl.ds(dest, span, stride=BLOCK_ROWS), :] = x
            d = jnp.where(s == 0, dval_ref[h, row], jnp.float32(0.0))
            tile = z_ref[h, pl.ds(spot_tile, BLOCK_ROWS), :]
            z_ref[h, pl.ds(spot_tile, BLOCK_ROWS), :] = tile + jnp.where(spot, d, jnp.float32(0.0))
    placed = {}
    for start, width, runs in chunk_segments(o_ref.shape[2], o_ref.shape[2] // 2):
        acc = None
        for h, u, l0, v0 in runs:
            if (h, u) not in placed:
                src = z_ref[h, pl.ds((u + BLOCK_ROWS) * BLOCK_ROWS, BLOCK_ROWS), :]
                sh = (l0 - v0) % LANES
                placed[(h, u)] = pltpu.roll(src, sh, 1) if sh else src
            src = placed[(h, u)]
            acc = src if acc is None else jnp.where(lane >= l0, src, acc)
        if width < LANES:
            acc = acc[:, :width]
        o_ref[0, :, pl.ds(start, width)] = acc


def assemble(a0, b0, first, second, dvals, tables, rows):
    span = 112
    n_blocks = rows // BLOCK_ROWS
    total = 2 * ORDERS
    grid_spec = pltpu.PrefetchScalarGridSpec(
        num_scalar_prefetch=4,
        grid=(2, n_blocks),
        in_specs=[
            pl.BlockSpec(memory_space=pltpu.SMEM),
            pl.BlockSpec((1,) + tables.shape[1:], lambda s, rb, *_: (s, 0, 0, 0, 0)),
        ],
        out_specs=pl.BlockSpec((1, BLOCK_ROWS, total), lambda s, rb, *_: (s, rb, 0)),
        scratch_shapes=[pltpu.VMEM((2, (span + BLOCK_ROWS) * BLOCK_ROWS, LANES), jnp.float32)],
    )
    return pl.pallas_call(
        assemble_kernel,
        grid_spec=grid_spec,
        out_shape=jax.ShapeDtypeStruct((2, rows, total), jnp.float32),
        compiler_params=pltpu.CompilerParams(dimension_semantics=("arbitrary", "arbitrary")),
    )(a0, b0, first, second, dvals, tables)


def line_sum(partial_value, my_index, devices):
    core = my_index % 2
    pairs = [(i, i ^ 1) for i in range(devices)]
    half_shape = partial_value.shape[1:]
    dense = (-1, LANES) if math.prod(half_shape) % LANES == 0 else half_shape
    keep = jnp.where(core == 0, partial_value[0], partial_value[1]).reshape(dense)
    give = jnp.where(core == 0, partial_value[1], partial_value[0]).reshape(dense)
    mine = keep + lax.ppermute(give, "slab", pairs)
    chips = devices // 2
    if chips & (chips - 1) == 0 and chips > 1 and len(dense) == 2:
        rows = mine.shape[0]
        padded = -(-rows // 16) * 16
        grown = jnp.pad(mine, ((0, padded - rows), (0, 0)))
        upper = (my_index // 2) % 2
        halves = (grown[: padded // 2], grown[padded // 2 :])
        pair = [(i, i ^ 2) for i in range(devices)]
        kept = jnp.where(upper == 0, halves[0], halves[1])
        sent = jnp.where(upper == 0, halves[1], halves[0])
        kept = kept + lax.ppermute(sent, "slab", pair)
        bit = 4
        while bit < devices:
            kept = kept + lax.ppermute(kept, "slab", [(i, i ^ bit) for i in range(devices)])
            bit *= 2
        back = lax.ppermute(kept, "slab", pair)
        total = jnp.where(
            upper == 0, jnp.concatenate([kept, back]), jnp.concatenate([back, kept])
        )[:rows]
    else:
        right = [(i, i + 2) for i in range(devices - 2)]
        left = [(i + 2, i) for i in range(devices - 2)]
        from_left = jnp.zeros_like(mine)
        from_right = jnp.zeros_like(mine)
        for step in range(chips - 1):
            from_left, from_right = (
                lax.ppermute(mine + from_left, "slab", right),
                lax.ppermute(mine + from_right, "slab", left),
            )
        total = mine + from_left + from_right
    other = lax.ppermute(total, "slab", pairs).reshape(half_shape)
    total = total.reshape(half_shape)
    return jnp.where(core == 0, jnp.stack([total, other]), jnp.stack([other, total]))


def shards(labels):
    slab_rows = labels.shape[0]
    map_width = labels.shape[1]
    devices = lax.axis_size("slab")
    my_index = lax.axis_index("slab")
    permit = permittivity(labels)
    padded_keep = -(-KEEP // devices) * devices
    half_keep = -(-HARM // devices) * devices
    frequency = (HARM - 1) - jnp.arange(padded_keep, dtype=jnp.int32)
    col_frequency = (HARM - 1) - jnp.arange(half_keep, dtype=jnp.int32)
    columns = jnp.arange(map_width, dtype=jnp.int32)
    phases = columns[:, None] * col_frequency[None, :] % map_width
    angles = phases.astype(jnp.float32) * (2.0 * math.pi / map_width)
    col_table = jnp.stack([jnp.cos(angles), -jnp.sin(angles)], axis=1)
    col_table, permit = lax.optimization_barrier((col_table, permit))
    smooth = extended_2(permit, (("slab", 0),), 4)
    for sweep_index in range(3):
        smooth = smooth_once(smooth)
    grad_x, grad_y = gradient(smooth)
    scale = jnp.sqrt(grad_x * grad_x + grad_y * grad_y + 1.0)
    normal_x = grad_x / scale
    normal_y = grad_y / scale
    inverse = 1.0 / permit
    contrast = permit - inverse
    fields = jnp.stack(
        [
            permit,
            contrast * normal_x * normal_x,
            contrast * normal_x * normal_y,
            contrast * normal_y * normal_y,
        ]
    )
    half_spectra = jnp.einsum("kxy,ycn->kxcn", fields, col_table, precision=lax.Precision.HIGH)
    my_positions = my_index * slab_rows + jnp.arange(slab_rows, dtype=jnp.int32)
    partial_value = row_transform(half_spectra, my_positions, frequency, map_width)
    summed = line_sum(partial_value, my_index, devices)
    coef = summed / float(map_width * map_width)
    a_in = jnp.arange(padded_keep, dtype=jnp.int32)
    c_in = jnp.arange(half_keep, dtype=jnp.int32)
    b_out = jnp.arange(2 * LANES, dtype=jnp.int32)
    flip_rows = (a_in[None, :] == (KEEP - 1) - a_in[:, None]).astype(jnp.float32)
    keep_cols = ((c_in[:, None] == b_out[None, :]) & (b_out[None, :] < HARM)).astype(jnp.float32)
    mirror_cols = (
        (c_in[:, None] == (KEEP - 1) - b_out[None, :]) & (b_out[None, :] >= HARM)
    ).astype(jnp.float32)
    sign = jnp.array([1.0, -1.0], jnp.float32)[:, None, None, None]
    direct = jnp.einsum("skac,cb->skab", coef, keep_cols, precision=lax.Precision.HIGHEST)
    mirrored = jnp.einsum(
        "ad,skdc,cb->skab", flip_rows, coef, mirror_cols, precision=lax.Precision.HIGHEST
    )
    full = direct + sign * mirrored
    tables = jnp.stack(
        [full[:, 2], full[:, 0] - full[:, 3], full[:, 1] - full[:, 0], -full[:, 2]], axis=1
    )
    tables = jnp.stack(
        [tables[..., COPY_STEP * c : COPY_STEP * c + LANES] for c in range(COPIES)], axis=1
    )
    rows = ROWS_DEV
    spacing = ORDERS // (rows * devices // 2)
    window_rows = my_index * rows + jnp.arange(rows, dtype=jnp.int32)
    order_index = window_rows // 2 * spacing
    first = order_index // HARM
    second = order_index % HARM
    centre = (HARM - 1) // 2
    kx = 0.3 + 0.02 * (first - centre).astype(jnp.float32)
    ky = 0.2 + 0.02 * (second - centre).astype(jnp.float32)
    lower = window_rows % 2 == 1
    left = jnp.where(lower, ky * ky, kx * ky)
    right = jnp.where(lower, -(kx * ky), -(kx * kx))
    dvals = jnp.stack([left, right])
    a0 = (HARM - 1) - first
    b0 = (HARM - 1) - second
    return assemble(a0, b0, first, second, dvals, tables, rows)


def solution(mesh):
    placed = (P(("layer", "slab"), None),)
    return jax.shard_map(
        shards,
        mesh=mesh,
        in_specs=placed,
        out_specs=P(None, ("layer", "slab"), None),
        check_vma=False,
    )
```

```python
import functools
import math

import jax
import jax.numpy as jnp
from jax import lax
from jax.experimental import pallas as pl
from jax.experimental.pallas import tpu as pltpu
from jax.sharding import PartitionSpec as P

HARM = 101
ROWS_DEV = 64
KEEP = 201
ORDERS = 10201
BLOCK_ROWS = 8
COPIES = 4
COPY_STEP = 28
LANES = 128


PERMITS = (1.0, 2.1, 4.0, 12.1)


def extended_2(block, sides, width):
    for axis, dim in sides:
        count = lax.axis_size(axis)
        forward = [(i, i + 1) for i in range(count - 1)]
        forward.append((count - 1, 0))
        backward = [(target, source) for source, target in forward]
        low = lax.ppermute(
            lax.slice_in_dim(block, block.shape[dim] - width, None, axis=dim), axis, forward
        )
        high = lax.ppermute(lax.slice_in_dim(block, 0, width, axis=dim), axis, backward)
        block = jnp.concatenate([low, block, high], axis=dim)
    return block


def permittivity(labels):
    total = jnp.zeros(labels.shape, jnp.float32)
    for index_value in range(4):
        total = total + jnp.where(
            labels == index_value, jnp.float32(PERMITS[index_value]), jnp.float32(0.0)
        )
    return total


def smooth_once(extended):
    middle = extended[1:-1]
    return (
        4.0 * middle
        + extended[:-2]
        + extended[2:]
        + jnp.roll(middle, 1, 1)
        + jnp.roll(middle, -1, 1)
    ) / 8.0


def gradient(extended):
    middle = extended[1:-1]
    grad_x = (extended[2:] - extended[:-2]) / 2.0
    grad_y = (jnp.roll(middle, -1, 1) - jnp.roll(middle, 1, 1)) / 2.0
    return (grad_x, grad_y)


def rim_rows(field_in):
    return extended_2(field_in, (("slab", 0),), 1)


def row_transform(spectra_in, positions, frequency, map_width):
    phases = frequency[:, None] * positions[None, :] % map_width
    angles = phases.astype(jnp.float32) * (2.0 * math.pi / map_width)
    table = jnp.stack([jnp.cos(angles), jnp.sin(angles)])
    products = jnp.einsum("smx,kxcn->skmcn", table, spectra_in, precision=lax.Precision.HIGH)
    real_part = products[0, :, :, 0] + products[1, :, :, 1]
    imag_part = products[0, :, :, 1] - products[1, :, :, 0]
    return jnp.stack([real_part, imag_part])


def chunk_segments(total, half):
    chunks = []
    for start in range(0, total, LANES):
        width = min(LANES, total - start)
        runs = []
        for lane in range(width):
            flat = start + lane
            h, j = divmod(flat, half)
            u, v = divmod(j, HARM)
            if not runs or runs[-1][0] != h or runs[-1][1] != u:
                runs.append((h, u, lane, v))
        chunks.append((start, width, runs))
    return chunks


def assemble_kernel(a0_ref, b0_ref, first_ref, second_ref, dval_ref, fl_ref, o_ref, z_ref, zt_ref, sems):
    s = pl.program_id(0)
    rb = pl.program_id(1)
    span = zt_ref.shape[1]
    sub = lax.broadcasted_iota(jnp.int32, (BLOCK_ROWS, LANES), 0)
    lane = lax.broadcasted_iota(jnp.int32, (BLOCK_ROWS, LANES), 1)
    copies = []
    spots = []
    for rr in range(BLOCK_ROWS):
        row = rb * BLOCK_ROWS + rr
        a0 = a0_ref[row]
        b0 = b0_ref[row]
        first = first_ref[row]
        second = second_ref[row]
        copy = jnp.minimum(b0 // COPY_STEP, COPIES - 1)
        shift = (LANES - (b0 - COPY_STEP * copy)) % LANES
        base = pl.multiple_of(a0 // BLOCK_ROWS * BLOCK_ROWS, BLOCK_ROWS)
        off = a0 % BLOCK_ROWS
        for h in range(2):
            combo = 2 * (rr % 2) + h
            slot = 2 * rr + h
            x = fl_ref[0, copy, combo, pl.ds(base, span), :]
            zt_ref[slot] = pltpu.roll(x, shift, 1)
            move = pltpu.make_async_copy(
                zt_ref.at[slot], z_ref.at[h, pl.ds(BLOCK_ROWS - off, span), rr], sems.at[slot]
            )
            move.start()
            copies.append(move)
            d = jnp.where(s == 0, dval_ref[h, row], jnp.float32(0.0))
            spots.append((h, rr, first + BLOCK_ROWS, second, d))
    for move in copies:
        move.wait()
    for h, rr, tile_index, second, d in spots:
        spot = (sub == rr) & (lane == second)
        z_ref[h, tile_index] = z_ref[h, tile_index] + jnp.where(spot, d, jnp.float32(0.0))
    placed = {}
    for start, width, runs in chunk_segments(o_ref.shape[2], o_ref.shape[2] // 2):
        acc = None
        for h, u, l0, v0 in runs:
            if (h, u) not in placed:
                src = z_ref[h, u + BLOCK_ROWS]
                sh = (l0 - v0) % LANES
                placed[(h, u)] = pltpu.roll(src, sh, 1) if sh else src
            src = placed[(h, u)]
            acc = src if acc is None else jnp.where(lane >= l0, src, acc)
        if width < LANES:
            acc = acc[:, :width]
        o_ref[0, :, pl.ds(start, width)] = acc


def assemble(a0, b0, first, second, dvals, tables, rows):
    span = 112
    n_blocks = rows // BLOCK_ROWS
    total = 2 * ORDERS
    grid_spec = pltpu.PrefetchScalarGridSpec(
        num_scalar_prefetch=4,
        grid=(2, n_blocks),
        in_specs=[
            pl.BlockSpec(memory_space=pltpu.SMEM),
            pl.BlockSpec((1,) + tables.shape[1:], lambda s, rb, *_: (s, 0, 0, 0, 0)),
        ],
        out_specs=pl.BlockSpec((1, BLOCK_ROWS, total), lambda s, rb, *_: (s, rb, 0)),
        scratch_shapes=[
            pltpu.VMEM((2, span + BLOCK_ROWS, BLOCK_ROWS, LANES), jnp.float32),
            pltpu.VMEM((2 * BLOCK_ROWS, span, LANES), jnp.float32),
            pltpu.SemaphoreType.DMA((2 * BLOCK_ROWS,)),
        ],
    )
    return pl.pallas_call(
        assemble_kernel,
        grid_spec=grid_spec,
        out_shape=jax.ShapeDtypeStruct((2, rows, total), jnp.float32),
        compiler_params=pltpu.CompilerParams(dimension_semantics=("arbitrary", "arbitrary")),
    )(a0, b0, first, second, dvals, tables)


def line_sum(partial_value, my_index, devices):
    core = my_index % 2
    pairs = [(i, i ^ 1) for i in range(devices)]
    half_shape = partial_value.shape[1:]
    dense = (-1, LANES) if math.prod(half_shape) % LANES == 0 else half_shape
    keep = jnp.where(core == 0, partial_value[0], partial_value[1]).reshape(dense)
    give = jnp.where(core == 0, partial_value[1], partial_value[0]).reshape(dense)
    mine = keep + lax.ppermute(give, "slab", pairs)
    chips = devices // 2
    if chips & (chips - 1) == 0 and chips > 1 and len(dense) == 2:
        rows = mine.shape[0]
        padded = -(-rows // 16) * 16
        grown = jnp.pad(mine, ((0, padded - rows), (0, 0)))
        upper = (my_index // 2) % 2
        halves = (grown[: padded // 2], grown[padded // 2 :])
        pair = [(i, i ^ 2) for i in range(devices)]
        kept = jnp.where(upper == 0, halves[0], halves[1])
        sent = jnp.where(upper == 0, halves[1], halves[0])
        kept = kept + lax.ppermute(sent, "slab", pair)
        bit = 4
        while bit < devices:
            kept = kept + lax.ppermute(kept, "slab", [(i, i ^ bit) for i in range(devices)])
            bit *= 2
        back = lax.ppermute(kept, "slab", pair)
        total = jnp.where(
            upper == 0, jnp.concatenate([kept, back]), jnp.concatenate([back, kept])
        )[:rows]
    else:
        right = [(i, i + 2) for i in range(devices - 2)]
        left = [(i + 2, i) for i in range(devices - 2)]
        from_left = jnp.zeros_like(mine)
        from_right = jnp.zeros_like(mine)
        for step in range(chips - 1):
            from_left, from_right = (
                lax.ppermute(mine + from_left, "slab", right),
                lax.ppermute(mine + from_right, "slab", left),
            )
        total = mine + from_left + from_right
    other = lax.ppermute(total, "slab", pairs).reshape(half_shape)
    total = total.reshape(half_shape)
    return jnp.where(core == 0, jnp.stack([total, other]), jnp.stack([other, total]))


def shards(labels):
    slab_rows = labels.shape[0]
    map_width = labels.shape[1]
    devices = lax.axis_size("slab")
    my_index = lax.axis_index("slab")
    permit = permittivity(labels)
    padded_keep = -(-KEEP // devices) * devices
    half_keep = -(-HARM // devices) * devices
    frequency = (HARM - 1) - jnp.arange(padded_keep, dtype=jnp.int32)
    col_frequency = (HARM - 1) - jnp.arange(half_keep, dtype=jnp.int32)
    columns = jnp.arange(map_width, dtype=jnp.int32)
    phases = columns[:, None] * col_frequency[None, :] % map_width
    angles = phases.astype(jnp.float32) * (2.0 * math.pi / map_width)
    col_table = jnp.stack([jnp.cos(angles), -jnp.sin(angles)], axis=1)
    col_table, permit = lax.optimization_barrier((col_table, permit))
    smooth = extended_2(permit, (("slab", 0),), 4)
    for sweep_index in range(3):
        smooth = smooth_once(smooth)
    grad_x, grad_y = gradient(smooth)
    scale = jnp.sqrt(grad_x * grad_x + grad_y * grad_y + 1.0)
    normal_x = grad_x / scale
    normal_y = grad_y / scale
    inverse = 1.0 / permit
    contrast = permit - inverse
    fields = jnp.stack(
        [
            permit,
            contrast * normal_x * normal_x,
            contrast * normal_x * normal_y,
            contrast * normal_y * normal_y,
        ]
    )
    half_spectra = jnp.einsum("kxy,ycn->kxcn", fields, col_table, precision=lax.Precision.HIGH)
    my_positions = my_index * slab_rows + jnp.arange(slab_rows, dtype=jnp.int32)
    partial_value = row_transform(half_spectra, my_positions, frequency, map_width)
    summed = line_sum(partial_value, my_index, devices)
    coef = summed / float(map_width * map_width)
    a_in = jnp.arange(padded_keep, dtype=jnp.int32)
    c_in = jnp.arange(half_keep, dtype=jnp.int32)
    b_out = jnp.arange(2 * LANES, dtype=jnp.int32)
    flip_rows = (a_in[None, :] == (KEEP - 1) - a_in[:, None]).astype(jnp.float32)
    keep_cols = ((c_in[:, None] == b_out[None, :]) & (b_out[None, :] < HARM)).astype(jnp.float32)
    mirror_cols = (
        (c_in[:, None] == (KEEP - 1) - b_out[None, :]) & (b_out[None, :] >= HARM)
    ).astype(jnp.float32)
    sign = jnp.array([1.0, -1.0], jnp.float32)[:, None, None, None]
    direct = jnp.einsum("skac,cb->skab", coef, keep_cols, precision=lax.Precision.HIGHEST)
    mirrored = jnp.einsum(
        "ad,skdc,cb->skab", flip_rows, coef, mirror_cols, precision=lax.Precision.HIGHEST
    )
    full = direct + sign * mirrored
    tables = jnp.stack(
        [full[:, 2], full[:, 0] - full[:, 3], full[:, 1] - full[:, 0], -full[:, 2]], axis=1
    )
    tables = jnp.stack(
        [tables[..., COPY_STEP * c : COPY_STEP * c + LANES] for c in range(COPIES)], axis=1
    )
    rows = ROWS_DEV
    spacing = ORDERS // (rows * devices // 2)
    window_rows = my_index * rows + jnp.arange(rows, dtype=jnp.int32)
    order_index = window_rows // 2 * spacing
    first = order_index // HARM
    second = order_index % HARM
    centre = (HARM - 1) // 2
    kx = 0.3 + 0.02 * (first - centre).astype(jnp.float32)
    ky = 0.2 + 0.02 * (second - centre).astype(jnp.float32)
    lower = window_rows % 2 == 1
    left = jnp.where(lower, ky * ky, kx * ky)
    right = jnp.where(lower, -(kx * ky), -(kx * kx))
    dvals = jnp.stack([left, right])
    a0 = (HARM - 1) - first
    b0 = (HARM - 1) - second
    return assemble(a0, b0, first, second, dvals, tables, rows)


def solution(mesh):
    placed = (P(("layer", "slab"), None),)
    return jax.shard_map(
        shards,
        mesh=mesh,
        in_specs=placed,
        out_specs=P(None, ("layer", "slab"), None),
        check_vma=False,
    )
```

```python
import functools
import math

import jax
import jax.numpy as jnp
from jax import lax
from jax.experimental import pallas as pl
from jax.experimental.pallas import tpu as pltpu
from jax.sharding import PartitionSpec as P

HARM = 101
ROWS_DEV = 64
KEEP = 201
ORDERS = 10201
BLOCK_ROWS = 8
COPIES = 4
COPY_STEP = 28
LANES = 128


PERMITS = (1.0, 2.1, 4.0, 12.1)


def extended_2(block, sides, width):
    for axis, dim in sides:
        count = lax.axis_size(axis)
        forward = [(i, i + 1) for i in range(count - 1)]
        forward.append((count - 1, 0))
        backward = [(target, source) for source, target in forward]
        low = lax.ppermute(
            lax.slice_in_dim(block, block.shape[dim] - width, None, axis=dim), axis, forward
        )
        high = lax.ppermute(lax.slice_in_dim(block, 0, width, axis=dim), axis, backward)
        block = jnp.concatenate([low, block, high], axis=dim)
    return block


def permittivity(labels):
    total = jnp.zeros(labels.shape, jnp.float32)
    for index_value in range(4):
        total = total + jnp.where(
            labels == index_value, jnp.float32(PERMITS[index_value]), jnp.float32(0.0)
        )
    return total


def smooth_once(extended):
    middle = extended[1:-1]
    return (
        4.0 * middle
        + extended[:-2]
        + extended[2:]
        + jnp.roll(middle, 1, 1)
        + jnp.roll(middle, -1, 1)
    ) / 8.0


def gradient(extended):
    middle = extended[1:-1]
    grad_x = (extended[2:] - extended[:-2]) / 2.0
    grad_y = (jnp.roll(middle, -1, 1) - jnp.roll(middle, 1, 1)) / 2.0
    return (grad_x, grad_y)


def rim_rows(field_in):
    return extended_2(field_in, (("slab", 0),), 1)


def row_transform(spectra_in, positions, frequency, map_width):
    phases = frequency[:, None] * positions[None, :] % map_width
    angles = phases.astype(jnp.float32) * (2.0 * math.pi / map_width)
    table = jnp.stack([jnp.cos(angles), jnp.sin(angles)])
    products = jnp.einsum("smx,kxcn->skmcn", table, spectra_in, precision=lax.Precision.HIGH)
    real_part = products[0, :, :, 0] + products[1, :, :, 1]
    imag_part = products[0, :, :, 1] - products[1, :, :, 0]
    return jnp.stack([real_part, imag_part])


def chunk_segments(total, half):
    chunks = []
    for start in range(0, total, LANES):
        width = min(LANES, total - start)
        runs = []
        for lane in range(width):
            flat = start + lane
            h, j = divmod(flat, half)
            u, v = divmod(j, HARM)
            if not runs or runs[-1][0] != h or runs[-1][1] != u:
                runs.append((h, u, lane, v))
        chunks.append((start, width, runs))
    return chunks


def assemble_kernel(index_ref, fl_ref, o_ref, z_ref):
    s = pl.program_id(0)
    rb = pl.program_id(1)
    rows = o_ref.shape[1] * pl.num_programs(1)
    spacing = ORDERS // (rows * index_ref[1] // 2)
    centre = (HARM - 1) // 2
    span = z_ref.shape[1] // BLOCK_ROWS - BLOCK_ROWS
    lane_iota = lax.broadcasted_iota(jnp.int32, (span, LANES), 1)
    sub = lax.broadcasted_iota(jnp.int32, (BLOCK_ROWS, LANES), 0)
    lane = lax.broadcasted_iota(jnp.int32, (BLOCK_ROWS, LANES), 1)
    for rr in range(BLOCK_ROWS):
        row = rb * BLOCK_ROWS + rr
        order_index = (index_ref[0] * rows + row) // 2 * spacing
        first = order_index // HARM
        second = order_index % HARM
        a0 = (HARM - 1) - first
        b0 = (HARM - 1) - second
        kx = 0.3 + 0.02 * (first - centre).astype(jnp.float32)
        ky = 0.2 + 0.02 * (second - centre).astype(jnp.float32)
        if rr % 2:
            diagonal = (ky * ky, -(kx * ky))
        else:
            diagonal = (kx * ky, -(kx * kx))
        copy = jnp.minimum(b0 // COPY_STEP, COPIES - 1)
        shift = (LANES - (b0 - COPY_STEP * copy)) % LANES
        base = pl.multiple_of(a0 // BLOCK_ROWS * BLOCK_ROWS, BLOCK_ROWS)
        off = a0 % BLOCK_ROWS
        dest = pl.multiple_of((BLOCK_ROWS - off) * BLOCK_ROWS, BLOCK_ROWS) + rr
        spot_tile = pl.multiple_of((first + BLOCK_ROWS) * BLOCK_ROWS, BLOCK_ROWS)
        spot = (sub == rr) & (lane == second)
        for h in range(2):
            combo = 2 * (rr % 2) + h
            x = fl_ref[0, copy, combo, pl.ds(base, span), :]
            x = pltpu.roll(x, shift, 1)
            z_ref[h, pl.ds(dest, span, stride=BLOCK_ROWS), :] = x
            d = jnp.where(s == 0, diagonal[h], jnp.float32(0.0))
            tile = z_ref[h, pl.ds(spot_tile, BLOCK_ROWS), :]
            z_ref[h, pl.ds(spot_tile, BLOCK_ROWS), :] = tile + jnp.where(spot, d, jnp.float32(0.0))
    placed = {}
    for start, width, runs in chunk_segments(o_ref.shape[2], o_ref.shape[2] // 2):
        acc = None
        for h, u, l0, v0 in runs:
            if (h, u) not in placed:
                src = z_ref[h, pl.ds((u + BLOCK_ROWS) * BLOCK_ROWS, BLOCK_ROWS), :]
                sh = (l0 - v0) % LANES
                placed[(h, u)] = pltpu.roll(src, sh, 1) if sh else src
            src = placed[(h, u)]
            acc = src if acc is None else jnp.where(lane >= l0, src, acc)
        if width < LANES:
            acc = acc[:, :width]
        o_ref[0, :, pl.ds(start, width)] = acc


def assemble(index, tables, rows):
    span = 112
    n_blocks = rows // BLOCK_ROWS
    total = 2 * ORDERS
    grid_spec = pltpu.PrefetchScalarGridSpec(
        num_scalar_prefetch=1,
        grid=(2, n_blocks),
        in_specs=[
            pl.BlockSpec((1,) + tables.shape[1:], lambda s, rb, *_: (s, 0, 0, 0, 0)),
        ],
        out_specs=pl.BlockSpec((1, BLOCK_ROWS, total), lambda s, rb, *_: (s, rb, 0)),
        scratch_shapes=[pltpu.VMEM((2, (span + BLOCK_ROWS) * BLOCK_ROWS, LANES), jnp.float32)],
    )
    return pl.pallas_call(
        assemble_kernel,
        grid_spec=grid_spec,
        out_shape=jax.ShapeDtypeStruct((2, rows, total), jnp.float32),
        compiler_params=pltpu.CompilerParams(dimension_semantics=("arbitrary", "arbitrary")),
    )(index, tables)


def line_sum(partial_value, my_index, devices):
    core = my_index % 2
    pairs = [(i, i ^ 1) for i in range(devices)]
    half_shape = partial_value.shape[1:]
    dense = (-1, LANES) if math.prod(half_shape) % LANES == 0 else half_shape
    keep = jnp.where(core == 0, partial_value[0], partial_value[1]).reshape(dense)
    give = jnp.where(core == 0, partial_value[1], partial_value[0]).reshape(dense)
    mine = keep + lax.ppermute(give, "slab", pairs)
    chips = devices // 2
    if chips & (chips - 1) == 0 and chips > 1 and len(dense) == 2:
        rows = mine.shape[0]
        padded = -(-rows // 16) * 16
        grown = jnp.pad(mine, ((0, padded - rows), (0, 0)))
        upper = (my_index // 2) % 2
        halves = (grown[: padded // 2], grown[padded // 2 :])
        pair = [(i, i ^ 2) for i in range(devices)]
        kept = jnp.where(upper == 0, halves[0], halves[1])
        sent = jnp.where(upper == 0, halves[1], halves[0])
        kept = kept + lax.ppermute(sent, "slab", pair)
        bit = 4
        while bit < devices:
            kept = kept + lax.ppermute(kept, "slab", [(i, i ^ bit) for i in range(devices)])
            bit *= 2
        back = lax.ppermute(kept, "slab", pair)
        total = jnp.where(
            upper == 0, jnp.concatenate([kept, back]), jnp.concatenate([back, kept])
        )[:rows]
    else:
        right = [(i, i + 2) for i in range(devices - 2)]
        left = [(i + 2, i) for i in range(devices - 2)]
        from_left = jnp.zeros_like(mine)
        from_right = jnp.zeros_like(mine)
        for step in range(chips - 1):
            from_left, from_right = (
                lax.ppermute(mine + from_left, "slab", right),
                lax.ppermute(mine + from_right, "slab", left),
            )
        total = mine + from_left + from_right
    other = lax.ppermute(total, "slab", pairs).reshape(half_shape)
    total = total.reshape(half_shape)
    return jnp.where(core == 0, jnp.stack([total, other]), jnp.stack([other, total]))


def shards(labels):
    slab_rows = labels.shape[0]
    map_width = labels.shape[1]
    devices = lax.axis_size("slab")
    my_index = lax.axis_index("slab")
    permit = permittivity(labels)
    padded_keep = -(-KEEP // devices) * devices
    half_keep = -(-HARM // devices) * devices
    frequency = (HARM - 1) - jnp.arange(padded_keep, dtype=jnp.int32)
    col_frequency = (HARM - 1) - jnp.arange(half_keep, dtype=jnp.int32)
    columns = jnp.arange(map_width, dtype=jnp.int32)
    phases = columns[:, None] * col_frequency[None, :] % map_width
    angles = phases.astype(jnp.float32) * (2.0 * math.pi / map_width)
    col_table = jnp.stack([jnp.cos(angles), -jnp.sin(angles)], axis=1)
    col_table, permit = lax.optimization_barrier((col_table, permit))
    smooth = extended_2(permit, (("slab", 0),), 4)
    for sweep_index in range(3):
        smooth = smooth_once(smooth)
    grad_x, grad_y = gradient(smooth)
    scale = jnp.sqrt(grad_x * grad_x + grad_y * grad_y + 1.0)
    normal_x = grad_x / scale
    normal_y = grad_y / scale
    inverse = 1.0 / permit
    contrast = permit - inverse
    fields = jnp.stack(
        [
            permit,
            contrast * normal_x * normal_x,
            contrast * normal_x * normal_y,
            contrast * normal_y * normal_y,
        ]
    )
    half_spectra = jnp.einsum("kxy,ycn->kxcn", fields, col_table, precision=lax.Precision.HIGH)
    my_positions = my_index * slab_rows + jnp.arange(slab_rows, dtype=jnp.int32)
    partial_value = row_transform(half_spectra, my_positions, frequency, map_width)
    summed = line_sum(partial_value, my_index, devices)
    coef = summed / float(map_width * map_width)
    a_in = jnp.arange(padded_keep, dtype=jnp.int32)
    c_in = jnp.arange(half_keep, dtype=jnp.int32)
    b_out = jnp.arange(2 * LANES, dtype=jnp.int32)
    flip_rows = (a_in[None, :] == (KEEP - 1) - a_in[:, None]).astype(jnp.float32)
    keep_cols = ((c_in[:, None] == b_out[None, :]) & (b_out[None, :] < HARM)).astype(jnp.float32)
    mirror_cols = (
        (c_in[:, None] == (KEEP - 1) - b_out[None, :]) & (b_out[None, :] >= HARM)
    ).astype(jnp.float32)
    sign = jnp.array([1.0, -1.0], jnp.float32)[:, None, None, None]
    direct = jnp.einsum("skac,cb->skab", coef, keep_cols, precision=lax.Precision.HIGHEST)
    mirrored = jnp.einsum(
        "ad,skdc,cb->skab", flip_rows, coef, mirror_cols, precision=lax.Precision.HIGHEST
    )
    full = direct + sign * mirrored
    tables = jnp.stack(
        [full[:, 2], full[:, 0] - full[:, 3], full[:, 1] - full[:, 0], -full[:, 2]], axis=1
    )
    tables = jnp.stack(
        [tables[..., COPY_STEP * c : COPY_STEP * c + LANES] for c in range(COPIES)], axis=1
    )
    index = jnp.stack([my_index, devices]).astype(jnp.int32)
    return assemble(index, tables, ROWS_DEV)


def solution(mesh):
    placed = (P(("layer", "slab"), None),)
    return jax.shard_map(
        shards,
        mesh=mesh,
        in_specs=placed,
        out_specs=P(None, ("layer", "slab"), None),
        check_vma=False,
    )
```

```python
import functools
import math

import jax
import jax.numpy as jnp
from jax import lax
from jax.experimental import pallas as pl
from jax.experimental.pallas import tpu as pltpu
from jax.sharding import PartitionSpec as P

HARM = 101
ROWS_DEV = 64
KEEP = 201
ORDERS = 10201
BLOCK_ROWS = 8
COPIES = 4
COPY_STEP = 28
LANES = 128


PERMITS = (1.0, 2.1, 4.0, 12.1)


def extended_2(block, sides, width):
    for axis, dim in sides:
        count = lax.axis_size(axis)
        forward = [(i, i + 1) for i in range(count - 1)]
        forward.append((count - 1, 0))
        backward = [(target, source) for source, target in forward]
        low = lax.ppermute(
            lax.slice_in_dim(block, block.shape[dim] - width, None, axis=dim), axis, forward
        )
        high = lax.ppermute(lax.slice_in_dim(block, 0, width, axis=dim), axis, backward)
        block = jnp.concatenate([low, block, high], axis=dim)
    return block


def permittivity(labels):
    total = jnp.zeros(labels.shape, jnp.float32)
    for index_value in range(4):
        total = total + jnp.where(
            labels == index_value, jnp.float32(PERMITS[index_value]), jnp.float32(0.0)
        )
    return total


def smooth_once(extended):
    middle = extended[1:-1]
    return (
        4.0 * middle
        + extended[:-2]
        + extended[2:]
        + jnp.roll(middle, 1, 1)
        + jnp.roll(middle, -1, 1)
    ) / 8.0


def gradient(extended):
    middle = extended[1:-1]
    grad_x = (extended[2:] - extended[:-2]) / 2.0
    grad_y = (jnp.roll(middle, -1, 1) - jnp.roll(middle, 1, 1)) / 2.0
    return (grad_x, grad_y)


def rim_rows(field_in):
    return extended_2(field_in, (("slab", 0),), 1)


def row_transform(spectra_in, positions, frequency, map_width):
    phases = frequency[:, None] * positions[None, :] % map_width
    angles = phases.astype(jnp.float32) * (2.0 * math.pi / map_width)
    table = jnp.stack([jnp.cos(angles), jnp.sin(angles)])
    products = jnp.einsum("smx,kxcn->skmcn", table, spectra_in, precision=lax.Precision.HIGH)
    real_part = products[0, :, :, 0] + products[1, :, :, 1]
    imag_part = products[0, :, :, 1] - products[1, :, :, 0]
    return jnp.stack([real_part, imag_part])


def chunk_segments(total, half):
    chunks = []
    for start in range(0, total, LANES):
        width = min(LANES, total - start)
        runs = []
        for lane in range(width):
            flat = start + lane
            h, j = divmod(flat, half)
            u, v = divmod(j, HARM)
            if not runs or runs[-1][0] != h or runs[-1][1] != u:
                runs.append((h, u, lane, v))
        chunks.append((start, width, runs))
    return chunks


def assemble_kernel(index_ref, fl_ref, o_ref, z_ref):
    s = pl.program_id(0)
    rb = pl.program_id(1)
    rows = o_ref.shape[1] * pl.num_programs(1)
    spacing = ORDERS // (rows * index_ref[1] // 2)
    centre = (HARM - 1) // 2
    span = z_ref.shape[1] // BLOCK_ROWS - BLOCK_ROWS
    lane_iota = lax.broadcasted_iota(jnp.int32, (span, LANES), 1)
    sub = lax.broadcasted_iota(jnp.int32, (BLOCK_ROWS, LANES), 0)
    lane = lax.broadcasted_iota(jnp.int32, (BLOCK_ROWS, LANES), 1)
    for rr in range(BLOCK_ROWS):
        row = rb * BLOCK_ROWS + rr
        order_index = (index_ref[0] * rows + row) // 2 * spacing
        first = order_index // HARM
        second = order_index % HARM
        a0 = (HARM - 1) - first
        b0 = (HARM - 1) - second
        kx = 0.3 + 0.02 * (first - centre).astype(jnp.float32)
        ky = 0.2 + 0.02 * (second - centre).astype(jnp.float32)
        if rr % 2:
            diagonal = (ky * ky, -(kx * ky))
        else:
            diagonal = (kx * ky, -(kx * kx))
        copy = jnp.minimum(b0 // COPY_STEP, COPIES - 1)
        shift = (LANES - (b0 - COPY_STEP * copy)) % LANES
        base = pl.multiple_of(a0 // BLOCK_ROWS * BLOCK_ROWS, BLOCK_ROWS)
        off = a0 % BLOCK_ROWS
        dest = pl.multiple_of((BLOCK_ROWS - off) * BLOCK_ROWS, BLOCK_ROWS) + rr
        spot_tile = pl.multiple_of((first + BLOCK_ROWS) * BLOCK_ROWS, BLOCK_ROWS)
        spot = (sub == rr) & (lane == second)
        for h in range(2):
            combo = 2 * (rr % 2) + h
            x = fl_ref[0, copy, combo, pl.ds(base, span), :]
            x = pltpu.roll(x, shift, 1)
            z_ref[h, pl.ds(dest, span, stride=BLOCK_ROWS), :] = x
            d = jnp.where(s == 0, diagonal[h], jnp.float32(0.0))
            tile = z_ref[h, pl.ds(spot_tile, BLOCK_ROWS), :]
            z_ref[h, pl.ds(spot_tile, BLOCK_ROWS), :] = tile + jnp.where(spot, d, jnp.float32(0.0))
    placed = {}
    for start, width, runs in chunk_segments(o_ref.shape[2], o_ref.shape[2] // 2):
        acc = None
        for h, u, l0, v0 in runs:
            if (h, u) not in placed:
                src = z_ref[h, pl.ds((u + BLOCK_ROWS) * BLOCK_ROWS, BLOCK_ROWS), :]
                sh = (l0 - v0) % LANES
                placed[(h, u)] = pltpu.roll(src, sh, 1) if sh else src
            src = placed[(h, u)]
            acc = src if acc is None else jnp.where(lane >= l0, src, acc)
        if width < LANES:
            acc = acc[:, :width]
        o_ref[0, :, pl.ds(start, width)] = acc


def assemble(index, tables, rows):
    span = 112
    n_blocks = rows // BLOCK_ROWS
    total = 2 * ORDERS
    grid_spec = pltpu.PrefetchScalarGridSpec(
        num_scalar_prefetch=1,
        grid=(2, n_blocks),
        in_specs=[
            pl.BlockSpec((1,) + tables.shape[1:], lambda s, rb, *_: (s, 0, 0, 0, 0)),
        ],
        out_specs=pl.BlockSpec((1, BLOCK_ROWS, total), lambda s, rb, *_: (s, rb, 0)),
        scratch_shapes=[pltpu.VMEM((2, (span + BLOCK_ROWS) * BLOCK_ROWS, LANES), jnp.float32)],
    )
    return pl.pallas_call(
        assemble_kernel,
        grid_spec=grid_spec,
        out_shape=jax.ShapeDtypeStruct((2, rows, total), jnp.float32),
        compiler_params=pltpu.CompilerParams(dimension_semantics=("arbitrary", "arbitrary")),
    )(index, tables)


def line_sum(partial_value, my_index, devices):
    core = my_index % 2
    pairs = [(i, i ^ 1) for i in range(devices)]
    half_shape = partial_value.shape[1:]
    dense = (-1, LANES) if math.prod(half_shape) % LANES == 0 else half_shape
    keep = jnp.where(core == 0, partial_value[0], partial_value[1]).reshape(dense)
    give = jnp.where(core == 0, partial_value[1], partial_value[0]).reshape(dense)
    mine = keep + lax.ppermute(give, "slab", pairs)
    chips = devices // 2
    if chips & (chips - 1) == 0 and chips > 1 and len(dense) == 2:
        rows = mine.shape[0]
        padded = -(-rows // 16) * 16
        grown = jnp.pad(mine, ((0, padded - rows), (0, 0)))
        upper = (my_index // 2) % 2
        halves = (grown[: padded // 2], grown[padded // 2 :])
        pair = [(i, i ^ 2) for i in range(devices)]
        kept = jnp.where(upper == 0, halves[0], halves[1])
        sent = jnp.where(upper == 0, halves[1], halves[0])
        kept = kept + lax.ppermute(sent, "slab", pair)
        bit = 4
        while bit < devices:
            kept = kept + lax.ppermute(kept, "slab", [(i, i ^ bit) for i in range(devices)])
            bit *= 2
        back = lax.ppermute(kept, "slab", pair)
        total = jnp.where(
            upper == 0, jnp.concatenate([kept, back]), jnp.concatenate([back, kept])
        )[:rows]
    else:
        right = [(i, i + 2) for i in range(devices - 2)]
        left = [(i + 2, i) for i in range(devices - 2)]
        from_left = jnp.zeros_like(mine)
        from_right = jnp.zeros_like(mine)
        for step in range(chips - 1):
            from_left, from_right = (
                lax.ppermute(mine + from_left, "slab", right),
                lax.ppermute(mine + from_right, "slab", left),
            )
        total = mine + from_left + from_right
    other = lax.ppermute(total, "slab", pairs).reshape(half_shape)
    total = total.reshape(half_shape)
    return jnp.where(core == 0, jnp.stack([total, other]), jnp.stack([other, total]))


def shards(labels):
    slab_rows = labels.shape[0]
    map_width = labels.shape[1]
    devices = lax.axis_size("slab")
    my_index = lax.axis_index("slab")
    permit = permittivity(labels)
    padded_keep = -(-KEEP // devices) * devices
    half_keep = -(-HARM // devices) * devices
    frequency = (HARM - 1) - jnp.arange(padded_keep, dtype=jnp.int32)
    col_frequency = (HARM - 1) - jnp.arange(half_keep, dtype=jnp.int32)
    fine_count = 64 if map_width % 64 == 0 else 1
    coarse = jnp.arange(map_width // fine_count, dtype=jnp.int32) * fine_count
    fine = jnp.arange(fine_count, dtype=jnp.int32)
    coarse_angles = (coarse[:, None] * col_frequency[None, :] % map_width).astype(jnp.float32) * (
        2.0 * math.pi / map_width
    )
    fine_angles = (fine[:, None] * col_frequency[None, :] % map_width).astype(jnp.float32) * (
        2.0 * math.pi / map_width
    )
    c_cos = jnp.cos(coarse_angles)[:, None, :]
    c_sin = jnp.sin(coarse_angles)[:, None, :]
    f_cos = jnp.cos(fine_angles)[None, :, :]
    f_sin = jnp.sin(fine_angles)[None, :, :]
    col_cos = (c_cos * f_cos - c_sin * f_sin).reshape(map_width, -1)
    col_sin = (c_sin * f_cos + c_cos * f_sin).reshape(map_width, -1)
    col_table = jnp.stack([col_cos, -col_sin], axis=1)
    col_table, permit = lax.optimization_barrier((col_table, permit))
    smooth = extended_2(permit, (("slab", 0),), 4)
    for sweep_index in range(3):
        smooth = smooth_once(smooth)
    grad_x, grad_y = gradient(smooth)
    scale = jnp.sqrt(grad_x * grad_x + grad_y * grad_y + 1.0)
    normal_x = grad_x / scale
    normal_y = grad_y / scale
    inverse = 1.0 / permit
    contrast = permit - inverse
    fields = jnp.stack(
        [
            permit,
            contrast * normal_x * normal_x,
            contrast * normal_x * normal_y,
            contrast * normal_y * normal_y,
        ]
    )
    half_spectra = jnp.einsum("kxy,ycn->kxcn", fields, col_table, precision=lax.Precision.HIGH)
    my_positions = my_index * slab_rows + jnp.arange(slab_rows, dtype=jnp.int32)
    partial_value = row_transform(half_spectra, my_positions, frequency, map_width)
    summed = line_sum(partial_value, my_index, devices)
    coef = summed / float(map_width * map_width)
    a_in = jnp.arange(padded_keep, dtype=jnp.int32)
    c_in = jnp.arange(half_keep, dtype=jnp.int32)
    b_out = jnp.arange(2 * LANES, dtype=jnp.int32)
    flip_rows = (a_in[None, :] == (KEEP - 1) - a_in[:, None]).astype(jnp.float32)
    keep_cols = ((c_in[:, None] == b_out[None, :]) & (b_out[None, :] < HARM)).astype(jnp.float32)
    mirror_cols = (
        (c_in[:, None] == (KEEP - 1) - b_out[None, :]) & (b_out[None, :] >= HARM)
    ).astype(jnp.float32)
    sign = jnp.array([1.0, -1.0], jnp.float32)[:, None, None, None]
    direct = jnp.einsum("skac,cb->skab", coef, keep_cols, precision=lax.Precision.HIGHEST)
    mirrored = jnp.einsum(
        "ad,skdc,cb->skab", flip_rows, coef, mirror_cols, precision=lax.Precision.HIGHEST
    )
    full = direct + sign * mirrored
    tables = jnp.stack(
        [full[:, 2], full[:, 0] - full[:, 3], full[:, 1] - full[:, 0], -full[:, 2]], axis=1
    )
    tables = jnp.stack(
        [tables[..., COPY_STEP * c : COPY_STEP * c + LANES] for c in range(COPIES)], axis=1
    )
    index = jnp.stack([my_index, devices]).astype(jnp.int32)
    return assemble(index, tables, ROWS_DEV)


def solution(mesh):
    placed = (P(("layer", "slab"), None),)
    return jax.shard_map(
        shards,
        mesh=mesh,
        in_specs=placed,
        out_specs=P(None, ("layer", "slab"), None),
        check_vma=False,
    )
```

```python
import functools
import math

import jax
import jax.numpy as jnp
from jax import lax
from jax.experimental import pallas as pl
from jax.experimental.pallas import tpu as pltpu
from jax.sharding import PartitionSpec as P

HARM = 101
ROWS_DEV = 64
KEEP = 201
ORDERS = 10201
BLOCK_ROWS = 8
STEP_ROWS = 16
COPIES = 4
COPY_STEP = 28
LANES = 128


PERMITS = (1.0, 2.1, 4.0, 12.1)


def extended_2(block, sides, width):
    for axis, dim in sides:
        count = lax.axis_size(axis)
        forward = [(i, i + 1) for i in range(count - 1)]
        forward.append((count - 1, 0))
        backward = [(target, source) for source, target in forward]
        low = lax.ppermute(
            lax.slice_in_dim(block, block.shape[dim] - width, None, axis=dim), axis, forward
        )
        high = lax.ppermute(lax.slice_in_dim(block, 0, width, axis=dim), axis, backward)
        block = jnp.concatenate([low, block, high], axis=dim)
    return block


def permittivity(labels):
    total = jnp.zeros(labels.shape, jnp.float32)
    for index_value in range(4):
        total = total + jnp.where(
            labels == index_value, jnp.float32(PERMITS[index_value]), jnp.float32(0.0)
        )
    return total


def smooth_once(extended):
    middle = extended[1:-1]
    return (
        4.0 * middle
        + extended[:-2]
        + extended[2:]
        + jnp.roll(middle, 1, 1)
        + jnp.roll(middle, -1, 1)
    ) / 8.0


def gradient(extended):
    middle = extended[1:-1]
    grad_x = (extended[2:] - extended[:-2]) / 2.0
    grad_y = (jnp.roll(middle, -1, 1) - jnp.roll(middle, 1, 1)) / 2.0
    return (grad_x, grad_y)


def rim_rows(field_in):
    return extended_2(field_in, (("slab", 0),), 1)


def row_transform(spectra_in, positions, frequency, map_width):
    phases = frequency[:, None] * positions[None, :] % map_width
    angles = phases.astype(jnp.float32) * (2.0 * math.pi / map_width)
    table = jnp.stack([jnp.cos(angles), jnp.sin(angles)])
    products = jnp.einsum("smx,kxcn->skmcn", table, spectra_in, precision=lax.Precision.HIGH)
    real_part = products[0, :, :, 0] + products[1, :, :, 1]
    imag_part = products[0, :, :, 1] - products[1, :, :, 0]
    return jnp.stack([real_part, imag_part])


def chunk_segments(total, half):
    chunks = []
    for start in range(0, total, LANES):
        width = min(LANES, total - start)
        runs = []
        for lane in range(width):
            flat = start + lane
            h, j = divmod(flat, half)
            u, v = divmod(j, HARM)
            if not runs or runs[-1][0] != h or runs[-1][1] != u:
                runs.append((h, u, lane, v))
        chunks.append((start, width, runs))
    return chunks


def assemble_kernel(index_ref, fl_ref, o_ref, z_ref):
    s = pl.program_id(0)
    rb = pl.program_id(1)
    rows = o_ref.shape[1] * pl.num_programs(1)
    spacing = ORDERS // (rows * index_ref[1] // 2)
    centre = (HARM - 1) // 2
    span = z_ref.shape[2] // BLOCK_ROWS - BLOCK_ROWS
    lane_iota = lax.broadcasted_iota(jnp.int32, (span, LANES), 1)
    sub = lax.broadcasted_iota(jnp.int32, (BLOCK_ROWS, LANES), 0)
    lane = lax.broadcasted_iota(jnp.int32, (BLOCK_ROWS, LANES), 1)
    for part in range(o_ref.shape[1] // BLOCK_ROWS):
        z_part = z_ref.at[part]
        for rr in range(BLOCK_ROWS):
            row = rb * o_ref.shape[1] + part * BLOCK_ROWS + rr
            order_index = (index_ref[0] * rows + row) // 2 * spacing
            first = order_index // HARM
            second = order_index % HARM
            a0 = (HARM - 1) - first
            b0 = (HARM - 1) - second
            kx = 0.3 + 0.02 * (first - centre).astype(jnp.float32)
            ky = 0.2 + 0.02 * (second - centre).astype(jnp.float32)
            if rr % 2:
                diagonal = (ky * ky, -(kx * ky))
            else:
                diagonal = (kx * ky, -(kx * kx))
            copy = jnp.minimum(b0 // COPY_STEP, COPIES - 1)
            shift = (LANES - (b0 - COPY_STEP * copy)) % LANES
            base = pl.multiple_of(a0 // BLOCK_ROWS * BLOCK_ROWS, BLOCK_ROWS)
            off = a0 % BLOCK_ROWS
            dest = pl.multiple_of((BLOCK_ROWS - off) * BLOCK_ROWS, BLOCK_ROWS) + rr
            spot_tile = pl.multiple_of((first + BLOCK_ROWS) * BLOCK_ROWS, BLOCK_ROWS)
            spot = (sub == rr) & (lane == second)
            for h in range(2):
                combo = 2 * (rr % 2) + h
                x = fl_ref[0, copy, combo, pl.ds(base, span), :]
                x = pltpu.roll(x, shift, 1)
                z_part[h, pl.ds(dest, span, stride=BLOCK_ROWS), :] = x
                d = jnp.where(s == 0, diagonal[h], jnp.float32(0.0))
                tile = z_part[h, pl.ds(spot_tile, BLOCK_ROWS), :]
                z_part[h, pl.ds(spot_tile, BLOCK_ROWS), :] = tile + jnp.where(spot, d, jnp.float32(0.0))
        placed = {}
        for start, width, runs in chunk_segments(o_ref.shape[2], o_ref.shape[2] // 2):
            acc = None
            for h, u, l0, v0 in runs:
                if (h, u) not in placed:
                    src = z_part[h, pl.ds((u + BLOCK_ROWS) * BLOCK_ROWS, BLOCK_ROWS), :]
                    sh = (l0 - v0) % LANES
                    placed[(h, u)] = pltpu.roll(src, sh, 1) if sh else src
                src = placed[(h, u)]
                acc = src if acc is None else jnp.where(lane >= l0, src, acc)
            if width < LANES:
                acc = acc[:, :width]
            o_ref[0, pl.ds(part * BLOCK_ROWS, BLOCK_ROWS), pl.ds(start, width)] = acc


def assemble(index, tables, rows):
    span = 112
    n_blocks = rows // STEP_ROWS
    total = 2 * ORDERS
    grid_spec = pltpu.PrefetchScalarGridSpec(
        num_scalar_prefetch=1,
        grid=(2, n_blocks),
        in_specs=[
            pl.BlockSpec((1,) + tables.shape[1:], lambda s, rb, *_: (s, 0, 0, 0, 0)),
        ],
        out_specs=pl.BlockSpec((1, STEP_ROWS, total), lambda s, rb, *_: (s, rb, 0)),
        scratch_shapes=[
            pltpu.VMEM(
                (STEP_ROWS // BLOCK_ROWS, 2, (span + BLOCK_ROWS) * BLOCK_ROWS, LANES), jnp.float32
            )
        ],
    )
    return pl.pallas_call(
        assemble_kernel,
        grid_spec=grid_spec,
        out_shape=jax.ShapeDtypeStruct((2, rows, total), jnp.float32),
        compiler_params=pltpu.CompilerParams(dimension_semantics=("arbitrary", "arbitrary")),
    )(index, tables)


def line_sum(partial_value, my_index, devices):
    core = my_index % 2
    pairs = [(i, i ^ 1) for i in range(devices)]
    half_shape = partial_value.shape[1:]
    dense = (-1, LANES) if math.prod(half_shape) % LANES == 0 else half_shape
    keep = jnp.where(core == 0, partial_value[0], partial_value[1]).reshape(dense)
    give = jnp.where(core == 0, partial_value[1], partial_value[0]).reshape(dense)
    mine = keep + lax.ppermute(give, "slab", pairs)
    chips = devices // 2
    if chips & (chips - 1) == 0 and chips > 1 and len(dense) == 2:
        rows = mine.shape[0]
        padded = -(-rows // 16) * 16
        grown = jnp.pad(mine, ((0, padded - rows), (0, 0)))
        upper = (my_index // 2) % 2
        halves = (grown[: padded // 2], grown[padded // 2 :])
        pair = [(i, i ^ 2) for i in range(devices)]
        kept = jnp.where(upper == 0, halves[0], halves[1])
        sent = jnp.where(upper == 0, halves[1], halves[0])
        kept = kept + lax.ppermute(sent, "slab", pair)
        bit = 4
        while bit < devices:
            kept = kept + lax.ppermute(kept, "slab", [(i, i ^ bit) for i in range(devices)])
            bit *= 2
        back = lax.ppermute(kept, "slab", pair)
        total = jnp.where(
            upper == 0, jnp.concatenate([kept, back]), jnp.concatenate([back, kept])
        )[:rows]
    else:
        right = [(i, i + 2) for i in range(devices - 2)]
        left = [(i + 2, i) for i in range(devices - 2)]
        from_left = jnp.zeros_like(mine)
        from_right = jnp.zeros_like(mine)
        for step in range(chips - 1):
            from_left, from_right = (
                lax.ppermute(mine + from_left, "slab", right),
                lax.ppermute(mine + from_right, "slab", left),
            )
        total = mine + from_left + from_right
    other = lax.ppermute(total, "slab", pairs).reshape(half_shape)
    total = total.reshape(half_shape)
    return jnp.where(core == 0, jnp.stack([total, other]), jnp.stack([other, total]))


def shards(labels):
    slab_rows = labels.shape[0]
    map_width = labels.shape[1]
    devices = lax.axis_size("slab")
    my_index = lax.axis_index("slab")
    permit = permittivity(labels)
    padded_keep = -(-KEEP // devices) * devices
    half_keep = -(-HARM // devices) * devices
    frequency = (HARM - 1) - jnp.arange(padded_keep, dtype=jnp.int32)
    col_frequency = (HARM - 1) - jnp.arange(half_keep, dtype=jnp.int32)
    fine_count = 64 if map_width % 64 == 0 else 1
    coarse = jnp.arange(map_width // fine_count, dtype=jnp.int32) * fine_count
    fine = jnp.arange(fine_count, dtype=jnp.int32)
    coarse_angles = (coarse[:, None] * col_frequency[None, :] % map_width).astype(jnp.float32) * (
        2.0 * math.pi / map_width
    )
    fine_angles = (fine[:, None] * col_frequency[None, :] % map_width).astype(jnp.float32) * (
        2.0 * math.pi / map_width
    )
    c_cos = jnp.cos(coarse_angles)[:, None, :]
    c_sin = jnp.sin(coarse_angles)[:, None, :]
    f_cos = jnp.cos(fine_angles)[None, :, :]
    f_sin = jnp.sin(fine_angles)[None, :, :]
    col_cos = (c_cos * f_cos - c_sin * f_sin).reshape(map_width, -1)
    col_sin = (c_sin * f_cos + c_cos * f_sin).reshape(map_width, -1)
    col_table = jnp.stack([col_cos, -col_sin], axis=1)
    col_table, permit = lax.optimization_barrier((col_table, permit))
    smooth = extended_2(permit, (("slab", 0),), 4)
    for sweep_index in range(3):
        smooth = smooth_once(smooth)
    grad_x, grad_y = gradient(smooth)
    scale = jnp.sqrt(grad_x * grad_x + grad_y * grad_y + 1.0)
    normal_x = grad_x / scale
    normal_y = grad_y / scale
    inverse = 1.0 / permit
    contrast = permit - inverse
    fields = jnp.stack(
        [
            permit,
            contrast * normal_x * normal_x,
            contrast * normal_x * normal_y,
            contrast * normal_y * normal_y,
        ]
    )
    half_spectra = jnp.einsum("kxy,ycn->kxcn", fields, col_table, precision=lax.Precision.HIGH)
    my_positions = my_index * slab_rows + jnp.arange(slab_rows, dtype=jnp.int32)
    partial_value = row_transform(half_spectra, my_positions, frequency, map_width)
    summed = line_sum(partial_value, my_index, devices)
    coef = summed / float(map_width * map_width)
    a_in = jnp.arange(padded_keep, dtype=jnp.int32)
    c_in = jnp.arange(half_keep, dtype=jnp.int32)
    b_out = jnp.arange(2 * LANES, dtype=jnp.int32)
    flip_rows = (a_in[None, :] == (KEEP - 1) - a_in[:, None]).astype(jnp.float32)
    keep_cols = ((c_in[:, None] == b_out[None, :]) & (b_out[None, :] < HARM)).astype(jnp.float32)
    mirror_cols = (
        (c_in[:, None] == (KEEP - 1) - b_out[None, :]) & (b_out[None, :] >= HARM)
    ).astype(jnp.float32)
    sign = jnp.array([1.0, -1.0], jnp.float32)[:, None, None, None]
    direct = jnp.einsum("skac,cb->skab", coef, keep_cols, precision=lax.Precision.HIGHEST)
    mirrored = jnp.einsum(
        "ad,skdc,cb->skab", flip_rows, coef, mirror_cols, precision=lax.Precision.HIGHEST
    )
    full = direct + sign * mirrored
    tables = jnp.stack(
        [full[:, 2], full[:, 0] - full[:, 3], full[:, 1] - full[:, 0], -full[:, 2]], axis=1
    )
    tables = jnp.stack(
        [tables[..., COPY_STEP * c : COPY_STEP * c + LANES] for c in range(COPIES)], axis=1
    )
    index = jnp.stack([my_index, devices]).astype(jnp.int32)
    return assemble(index, tables, ROWS_DEV)


def solution(mesh):
    placed = (P(("layer", "slab"), None),)
    return jax.shard_map(
        shards,
        mesh=mesh,
        in_specs=placed,
        out_specs=P(None, ("layer", "slab"), None),
        check_vma=False,
    )
```

```python
import functools
import math

import jax
import jax.numpy as jnp
from jax import lax
from jax.experimental import pallas as pl
from jax.experimental.pallas import tpu as pltpu
from jax.sharding import PartitionSpec as P

HARM = 101
ROWS_DEV = 64
KEEP = 201
ORDERS = 10201
BLOCK_ROWS = 8
STEP_ROWS = 32
COPIES = 4
COPY_STEP = 28
LANES = 128


PERMITS = (1.0, 2.1, 4.0, 12.1)


def extended_2(block, sides, width):
    for axis, dim in sides:
        count = lax.axis_size(axis)
        forward = [(i, i + 1) for i in range(count - 1)]
        forward.append((count - 1, 0))
        backward = [(target, source) for source, target in forward]
        low = lax.ppermute(
            lax.slice_in_dim(block, block.shape[dim] - width, None, axis=dim), axis, forward
        )
        high = lax.ppermute(lax.slice_in_dim(block, 0, width, axis=dim), axis, backward)
        block = jnp.concatenate([low, block, high], axis=dim)
    return block


def permittivity(labels):
    total = jnp.zeros(labels.shape, jnp.float32)
    for index_value in range(4):
        total = total + jnp.where(
            labels == index_value, jnp.float32(PERMITS[index_value]), jnp.float32(0.0)
        )
    return total


def smooth_once(extended):
    middle = extended[1:-1]
    return (
        4.0 * middle
        + extended[:-2]
        + extended[2:]
        + jnp.roll(middle, 1, 1)
        + jnp.roll(middle, -1, 1)
    ) / 8.0


def gradient(extended):
    middle = extended[1:-1]
    grad_x = (extended[2:] - extended[:-2]) / 2.0
    grad_y = (jnp.roll(middle, -1, 1) - jnp.roll(middle, 1, 1)) / 2.0
    return (grad_x, grad_y)


def rim_rows(field_in):
    return extended_2(field_in, (("slab", 0),), 1)


def row_transform(spectra_in, positions, frequency, map_width):
    phases = frequency[:, None] * positions[None, :] % map_width
    angles = phases.astype(jnp.float32) * (2.0 * math.pi / map_width)
    table = jnp.stack([jnp.cos(angles), jnp.sin(angles)])
    products = jnp.einsum("smx,kxcn->skmcn", table, spectra_in, precision=lax.Precision.HIGH)
    real_part = products[0, :, :, 0] + products[1, :, :, 1]
    imag_part = products[0, :, :, 1] - products[1, :, :, 0]
    return jnp.stack([real_part, imag_part])


def chunk_segments(total, half):
    chunks = []
    for start in range(0, total, LANES):
        width = min(LANES, total - start)
        runs = []
        for lane in range(width):
            flat = start + lane
            h, j = divmod(flat, half)
            u, v = divmod(j, HARM)
            if not runs or runs[-1][0] != h or runs[-1][1] != u:
                runs.append((h, u, lane, v))
        chunks.append((start, width, runs))
    return chunks


def assemble_kernel(index_ref, fl_ref, o_ref, z_ref):
    s = pl.program_id(0)
    rb = pl.program_id(1)
    rows = o_ref.shape[1] * pl.num_programs(1)
    spacing = ORDERS // (rows * index_ref[1] // 2)
    centre = (HARM - 1) // 2
    span = z_ref.shape[2] // BLOCK_ROWS - BLOCK_ROWS
    lane_iota = lax.broadcasted_iota(jnp.int32, (span, LANES), 1)
    sub = lax.broadcasted_iota(jnp.int32, (BLOCK_ROWS, LANES), 0)
    lane = lax.broadcasted_iota(jnp.int32, (BLOCK_ROWS, LANES), 1)
    for part in range(o_ref.shape[1] // BLOCK_ROWS):
        z_part = z_ref.at[part]
        for rr in range(BLOCK_ROWS):
            row = rb * o_ref.shape[1] + part * BLOCK_ROWS + rr
            order_index = (index_ref[0] * rows + row) // 2 * spacing
            first = order_index // HARM
            second = order_index % HARM
            a0 = (HARM - 1) - first
            b0 = (HARM - 1) - second
            kx = 0.3 + 0.02 * (first - centre).astype(jnp.float32)
            ky = 0.2 + 0.02 * (second - centre).astype(jnp.float32)
            if rr % 2:
                diagonal = (ky * ky, -(kx * ky))
            else:
                diagonal = (kx * ky, -(kx * kx))
            copy = jnp.minimum(b0 // COPY_STEP, COPIES - 1)
            shift = (LANES - (b0 - COPY_STEP * copy)) % LANES
            base = pl.multiple_of(a0 // BLOCK_ROWS * BLOCK_ROWS, BLOCK_ROWS)
            off = a0 % BLOCK_ROWS
            dest = pl.multiple_of((BLOCK_ROWS - off) * BLOCK_ROWS, BLOCK_ROWS) + rr
            spot_tile = pl.multiple_of((first + BLOCK_ROWS) * BLOCK_ROWS, BLOCK_ROWS)
            spot = (sub == rr) & (lane == second)
            for h in range(2):
                combo = 2 * (rr % 2) + h
                x = fl_ref[0, copy, combo, pl.ds(base, span), :]
                x = pltpu.roll(x, shift, 1)
                z_part[h, pl.ds(dest, span, stride=BLOCK_ROWS), :] = x
                d = jnp.where(s == 0, diagonal[h], jnp.float32(0.0))
                tile = z_part[h, pl.ds(spot_tile, BLOCK_ROWS), :]
                z_part[h, pl.ds(spot_tile, BLOCK_ROWS), :] = tile + jnp.where(spot, d, jnp.float32(0.0))
        placed = {}
        for start, width, runs in chunk_segments(o_ref.shape[2], o_ref.shape[2] // 2):
            acc = None
            for h, u, l0, v0 in runs:
                if (h, u) not in placed:
                    src = z_part[h, pl.ds((u + BLOCK_ROWS) * BLOCK_ROWS, BLOCK_ROWS), :]
                    sh = (l0 - v0) % LANES
                    placed[(h, u)] = pltpu.roll(src, sh, 1) if sh else src
                src = placed[(h, u)]
                acc = src if acc is None else jnp.where(lane >= l0, src, acc)
            if width < LANES:
                acc = acc[:, :width]
            o_ref[0, pl.ds(part * BLOCK_ROWS, BLOCK_ROWS), pl.ds(start, width)] = acc


def assemble(index, tables, rows):
    span = 112
    n_blocks = rows // STEP_ROWS
    total = 2 * ORDERS
    grid_spec = pltpu.PrefetchScalarGridSpec(
        num_scalar_prefetch=1,
        grid=(2, n_blocks),
        in_specs=[
            pl.BlockSpec((1,) + tables.shape[1:], lambda s, rb, *_: (s, 0, 0, 0, 0)),
        ],
        out_specs=pl.BlockSpec((1, STEP_ROWS, total), lambda s, rb, *_: (s, rb, 0)),
        scratch_shapes=[
            pltpu.VMEM(
                (STEP_ROWS // BLOCK_ROWS, 2, (span + BLOCK_ROWS) * BLOCK_ROWS, LANES), jnp.float32
            )
        ],
    )
    return pl.pallas_call(
        assemble_kernel,
        grid_spec=grid_spec,
        out_shape=jax.ShapeDtypeStruct((2, rows, total), jnp.float32),
        compiler_params=pltpu.CompilerParams(dimension_semantics=("arbitrary", "arbitrary")),
    )(index, tables)


def line_sum(partial_value, my_index, devices):
    core = my_index % 2
    pairs = [(i, i ^ 1) for i in range(devices)]
    half_shape = partial_value.shape[1:]
    dense = (-1, LANES) if math.prod(half_shape) % LANES == 0 else half_shape
    keep = jnp.where(core == 0, partial_value[0], partial_value[1]).reshape(dense)
    give = jnp.where(core == 0, partial_value[1], partial_value[0]).reshape(dense)
    mine = keep + lax.ppermute(give, "slab", pairs)
    chips = devices // 2
    if chips & (chips - 1) == 0 and chips > 1 and len(dense) == 2:
        rows = mine.shape[0]
        padded = -(-rows // 16) * 16
        grown = jnp.pad(mine, ((0, padded - rows), (0, 0)))
        upper = (my_index // 2) % 2
        halves = (grown[: padded // 2], grown[padded // 2 :])
        pair = [(i, i ^ 2) for i in range(devices)]
        kept = jnp.where(upper == 0, halves[0], halves[1])
        sent = jnp.where(upper == 0, halves[1], halves[0])
        kept = kept + lax.ppermute(sent, "slab", pair)
        bit = 4
        while bit < devices:
            kept = kept + lax.ppermute(kept, "slab", [(i, i ^ bit) for i in range(devices)])
            bit *= 2
        back = lax.ppermute(kept, "slab", pair)
        total = jnp.where(
            upper == 0, jnp.concatenate([kept, back]), jnp.concatenate([back, kept])
        )[:rows]
    else:
        right = [(i, i + 2) for i in range(devices - 2)]
        left = [(i + 2, i) for i in range(devices - 2)]
        from_left = jnp.zeros_like(mine)
        from_right = jnp.zeros_like(mine)
        for step in range(chips - 1):
            from_left, from_right = (
                lax.ppermute(mine + from_left, "slab", right),
                lax.ppermute(mine + from_right, "slab", left),
            )
        total = mine + from_left + from_right
    other = lax.ppermute(total, "slab", pairs).reshape(half_shape)
    total = total.reshape(half_shape)
    return jnp.where(core == 0, jnp.stack([total, other]), jnp.stack([other, total]))


def shards(labels):
    slab_rows = labels.shape[0]
    map_width = labels.shape[1]
    devices = lax.axis_size("slab")
    my_index = lax.axis_index("slab")
    permit = permittivity(labels)
    padded_keep = -(-KEEP // devices) * devices
    half_keep = -(-HARM // devices) * devices
    frequency = (HARM - 1) - jnp.arange(padded_keep, dtype=jnp.int32)
    col_frequency = (HARM - 1) - jnp.arange(half_keep, dtype=jnp.int32)
    fine_count = 64 if map_width % 64 == 0 else 1
    coarse = jnp.arange(map_width // fine_count, dtype=jnp.int32) * fine_count
    fine = jnp.arange(fine_count, dtype=jnp.int32)
    coarse_angles = (coarse[:, None] * col_frequency[None, :] % map_width).astype(jnp.float32) * (
        2.0 * math.pi / map_width
    )
    fine_angles = (fine[:, None] * col_frequency[None, :] % map_width).astype(jnp.float32) * (
        2.0 * math.pi / map_width
    )
    c_cos = jnp.cos(coarse_angles)[:, None, :]
    c_sin = jnp.sin(coarse_angles)[:, None, :]
    f_cos = jnp.cos(fine_angles)[None, :, :]
    f_sin = jnp.sin(fine_angles)[None, :, :]
    col_cos = (c_cos * f_cos - c_sin * f_sin).reshape(map_width, -1)
    col_sin = (c_sin * f_cos + c_cos * f_sin).reshape(map_width, -1)
    col_table = jnp.stack([col_cos, -col_sin], axis=1)
    col_table, permit = lax.optimization_barrier((col_table, permit))
    smooth = extended_2(permit, (("slab", 0),), 4)
    for sweep_index in range(3):
        smooth = smooth_once(smooth)
    grad_x, grad_y = gradient(smooth)
    scale = jnp.sqrt(grad_x * grad_x + grad_y * grad_y + 1.0)
    normal_x = grad_x / scale
    normal_y = grad_y / scale
    inverse = 1.0 / permit
    contrast = permit - inverse
    fields = jnp.stack(
        [
            permit,
            contrast * normal_x * normal_x,
            contrast * normal_x * normal_y,
            contrast * normal_y * normal_y,
        ]
    )
    half_spectra = jnp.einsum("kxy,ycn->kxcn", fields, col_table, precision=lax.Precision.HIGH)
    my_positions = my_index * slab_rows + jnp.arange(slab_rows, dtype=jnp.int32)
    partial_value = row_transform(half_spectra, my_positions, frequency, map_width)
    summed = line_sum(partial_value, my_index, devices)
    coef = summed / float(map_width * map_width)
    a_in = jnp.arange(padded_keep, dtype=jnp.int32)
    c_in = jnp.arange(half_keep, dtype=jnp.int32)
    b_out = jnp.arange(2 * LANES, dtype=jnp.int32)
    flip_rows = (a_in[None, :] == (KEEP - 1) - a_in[:, None]).astype(jnp.float32)
    keep_cols = ((c_in[:, None] == b_out[None, :]) & (b_out[None, :] < HARM)).astype(jnp.float32)
    mirror_cols = (
        (c_in[:, None] == (KEEP - 1) - b_out[None, :]) & (b_out[None, :] >= HARM)
    ).astype(jnp.float32)
    sign = jnp.array([1.0, -1.0], jnp.float32)[:, None, None, None]
    direct = jnp.einsum("skac,cb->skab", coef, keep_cols, precision=lax.Precision.HIGHEST)
    mirrored = jnp.einsum(
        "ad,skdc,cb->skab", flip_rows, coef, mirror_cols, precision=lax.Precision.HIGHEST
    )
    full = direct + sign * mirrored
    tables = jnp.stack(
        [full[:, 2], full[:, 0] - full[:, 3], full[:, 1] - full[:, 0], -full[:, 2]], axis=1
    )
    tables = jnp.stack(
        [tables[..., COPY_STEP * c : COPY_STEP * c + LANES] for c in range(COPIES)], axis=1
    )
    index = jnp.stack([my_index, devices]).astype(jnp.int32)
    return assemble(index, tables, ROWS_DEV)


def solution(mesh):
    placed = (P(("layer", "slab"), None),)
    return jax.shard_map(
        shards,
        mesh=mesh,
        in_specs=placed,
        out_specs=P(None, ("layer", "slab"), None),
        check_vma=False,
    )
```

```python
import functools
import itertools
import math

import jax
import jax.numpy as jnp
from jax import lax
from jax.experimental import pallas as pl
from jax.experimental.pallas import tpu as pltpu
from jax.sharding import PartitionSpec as P

HARM = 101
ROWS_DEV = 64
KEEP = 201
ORDERS = 10201
BLOCK_ROWS = 8
STEP_ROWS = 16
COPIES = 4
COPY_STEP = 28
LANES = 128


PERMITS = (1.0, 2.1, 4.0, 12.1)


def extended_2(block, sides, width):
    for axis, dim in sides:
        count = lax.axis_size(axis)
        forward = [(i, i + 1) for i in range(count - 1)]
        forward.append((count - 1, 0))
        backward = [(target, source) for source, target in forward]
        low = lax.ppermute(
            lax.slice_in_dim(block, block.shape[dim] - width, None, axis=dim), axis, forward
        )
        high = lax.ppermute(lax.slice_in_dim(block, 0, width, axis=dim), axis, backward)
        block = jnp.concatenate([low, block, high], axis=dim)
    return block


def permittivity(labels):
    total = jnp.zeros(labels.shape, jnp.float32)
    for index_value in range(4):
        total = total + jnp.where(
            labels == index_value, jnp.float32(PERMITS[index_value]), jnp.float32(0.0)
        )
    return total


def smooth_once(extended):
    middle = extended[1:-1]
    return (
        4.0 * middle
        + extended[:-2]
        + extended[2:]
        + jnp.roll(middle, 1, 1)
        + jnp.roll(middle, -1, 1)
    ) / 8.0


def gradient(extended):
    middle = extended[1:-1]
    grad_x = (extended[2:] - extended[:-2]) / 2.0
    grad_y = (jnp.roll(middle, -1, 1) - jnp.roll(middle, 1, 1)) / 2.0
    return (grad_x, grad_y)


def rim_rows(field_in):
    return extended_2(field_in, (("slab", 0),), 1)


def row_transform(spectra_in, positions, frequency, map_width):
    phases = frequency[:, None] * positions[None, :] % map_width
    angles = phases.astype(jnp.float32) * (2.0 * math.pi / map_width)
    table = jnp.stack([jnp.cos(angles), jnp.sin(angles)])
    products = jnp.einsum("smx,kxcn->skmcn", table, spectra_in, precision=lax.Precision.HIGH)
    real_part = products[0, :, :, 0] + products[1, :, :, 1]
    imag_part = products[0, :, :, 1] - products[1, :, :, 0]
    return jnp.stack([real_part, imag_part])


def chunk_segments(total, half):
    chunks = []
    for start in range(0, total, LANES):
        width = min(LANES, total - start)
        runs = []
        for lane in range(width):
            flat = start + lane
            h, j = divmod(flat, half)
            u, v = divmod(j, HARM)
            if not runs or runs[-1][0] != h or runs[-1][1] != u:
                runs.append((h, u, lane, v))
        chunks.append((start, width, runs))
    return chunks


def assemble_kernel(index_ref, fl_ref, o_ref, z_ref):
    rb = pl.program_id(0)
    rows = o_ref.shape[1] * pl.num_programs(0)
    spacing = ORDERS // (rows * index_ref[1] // 2)
    centre = (HARM - 1) // 2
    span = z_ref.shape[-2] // BLOCK_ROWS - BLOCK_ROWS
    lane_iota = lax.broadcasted_iota(jnp.int32, (span, LANES), 1)
    sub = lax.broadcasted_iota(jnp.int32, (BLOCK_ROWS, LANES), 0)
    lane = lax.broadcasted_iota(jnp.int32, (BLOCK_ROWS, LANES), 1)
    for part, s in itertools.product(range(o_ref.shape[1] // BLOCK_ROWS), range(2)):
        z_part = z_ref.at[part, s]
        for rr in range(BLOCK_ROWS):
            row = rb * o_ref.shape[1] + part * BLOCK_ROWS + rr
            order_index = (index_ref[0] * rows + row) // 2 * spacing
            first = order_index // HARM
            second = order_index % HARM
            a0 = (HARM - 1) - first
            b0 = (HARM - 1) - second
            kx = 0.3 + 0.02 * (first - centre).astype(jnp.float32)
            ky = 0.2 + 0.02 * (second - centre).astype(jnp.float32)
            if rr % 2:
                diagonal = (ky * ky, -(kx * ky))
            else:
                diagonal = (kx * ky, -(kx * kx))
            copy = jnp.minimum(b0 // COPY_STEP, COPIES - 1)
            shift = (LANES - (b0 - COPY_STEP * copy)) % LANES
            base = pl.multiple_of(a0 // BLOCK_ROWS * BLOCK_ROWS, BLOCK_ROWS)
            off = a0 % BLOCK_ROWS
            dest = pl.multiple_of((BLOCK_ROWS - off) * BLOCK_ROWS, BLOCK_ROWS) + rr
            spot_tile = pl.multiple_of((first + BLOCK_ROWS) * BLOCK_ROWS, BLOCK_ROWS)
            spot = (sub == rr) & (lane == second)
            for h in range(2):
                combo = 2 * (rr % 2) + h
                x = fl_ref[s, copy, combo, pl.ds(base, span), :]
                x = pltpu.roll(x, shift, 1)
                z_part[h, pl.ds(dest, span, stride=BLOCK_ROWS), :] = x
                if s:
                    continue
                d = diagonal[h]
                tile = z_part[h, pl.ds(spot_tile, BLOCK_ROWS), :]
                z_part[h, pl.ds(spot_tile, BLOCK_ROWS), :] = tile + jnp.where(spot, d, jnp.float32(0.0))
        placed = {}
        for start, width, runs in chunk_segments(o_ref.shape[2], o_ref.shape[2] // 2):
            acc = None
            for h, u, l0, v0 in runs:
                if (h, u) not in placed:
                    src = z_part[h, pl.ds((u + BLOCK_ROWS) * BLOCK_ROWS, BLOCK_ROWS), :]
                    sh = (l0 - v0) % LANES
                    placed[(h, u)] = pltpu.roll(src, sh, 1) if sh else src
                src = placed[(h, u)]
                acc = src if acc is None else jnp.where(lane >= l0, src, acc)
            if width < LANES:
                acc = acc[:, :width]
            o_ref[s, pl.ds(part * BLOCK_ROWS, BLOCK_ROWS), pl.ds(start, width)] = acc


def assemble(index, tables, rows):
    span = 112
    n_blocks = rows // STEP_ROWS
    total = 2 * ORDERS
    grid_spec = pltpu.PrefetchScalarGridSpec(
        num_scalar_prefetch=1,
        grid=(n_blocks,),
        in_specs=[
            pl.BlockSpec(tables.shape, lambda rb, *_: (0, 0, 0, 0, 0)),
        ],
        out_specs=pl.BlockSpec((2, STEP_ROWS, total), lambda rb, *_: (0, rb, 0)),
        scratch_shapes=[
            pltpu.VMEM(
                (STEP_ROWS // BLOCK_ROWS, 2, 2, (span + BLOCK_ROWS) * BLOCK_ROWS, LANES), jnp.float32
            )
        ],
    )
    return pl.pallas_call(
        assemble_kernel,
        grid_spec=grid_spec,
        out_shape=jax.ShapeDtypeStruct((2, rows, total), jnp.float32),
        compiler_params=pltpu.CompilerParams(dimension_semantics=("arbitrary",)),
    )(index, tables)


def line_sum(partial_value, my_index, devices):
    core = my_index % 2
    pairs = [(i, i ^ 1) for i in range(devices)]
    half_shape = partial_value.shape[1:]
    dense = (-1, LANES) if math.prod(half_shape) % LANES == 0 else half_shape
    keep = jnp.where(core == 0, partial_value[0], partial_value[1]).reshape(dense)
    give = jnp.where(core == 0, partial_value[1], partial_value[0]).reshape(dense)
    mine = keep + lax.ppermute(give, "slab", pairs)
    chips = devices // 2
    if chips & (chips - 1) == 0 and chips > 1 and len(dense) == 2:
        rows = mine.shape[0]
        padded = -(-rows // 16) * 16
        grown = jnp.pad(mine, ((0, padded - rows), (0, 0)))
        upper = (my_index // 2) % 2
        halves = (grown[: padded // 2], grown[padded // 2 :])
        pair = [(i, i ^ 2) for i in range(devices)]
        kept = jnp.where(upper == 0, halves[0], halves[1])
        sent = jnp.where(upper == 0, halves[1], halves[0])
        kept = kept + lax.ppermute(sent, "slab", pair)
        bit = 4
        while bit < devices:
            kept = kept + lax.ppermute(kept, "slab", [(i, i ^ bit) for i in range(devices)])
            bit *= 2
        back = lax.ppermute(kept, "slab", pair)
        total = jnp.where(
            upper == 0, jnp.concatenate([kept, back]), jnp.concatenate([back, kept])
        )[:rows]
    else:
        right = [(i, i + 2) for i in range(devices - 2)]
        left = [(i + 2, i) for i in range(devices - 2)]
        from_left = jnp.zeros_like(mine)
        from_right = jnp.zeros_like(mine)
        for step in range(chips - 1):
            from_left, from_right = (
                lax.ppermute(mine + from_left, "slab", right),
                lax.ppermute(mine + from_right, "slab", left),
            )
        total = mine + from_left + from_right
    other = lax.ppermute(total, "slab", pairs).reshape(half_shape)
    total = total.reshape(half_shape)
    return jnp.where(core == 0, jnp.stack([total, other]), jnp.stack([other, total]))


def shards(labels):
    slab_rows = labels.shape[0]
    map_width = labels.shape[1]
    devices = lax.axis_size("slab")
    my_index = lax.axis_index("slab")
    permit = permittivity(labels)
    padded_keep = -(-KEEP // devices) * devices
    half_keep = -(-HARM // devices) * devices
    frequency = (HARM - 1) - jnp.arange(padded_keep, dtype=jnp.int32)
    col_frequency = (HARM - 1) - jnp.arange(half_keep, dtype=jnp.int32)
    fine_count = 64 if map_width % 64 == 0 else 1
    coarse = jnp.arange(map_width // fine_count, dtype=jnp.int32) * fine_count
    fine = jnp.arange(fine_count, dtype=jnp.int32)
    coarse_angles = (coarse[:, None] * col_frequency[None, :] % map_width).astype(jnp.float32) * (
        2.0 * math.pi / map_width
    )
    fine_angles = (fine[:, None] * col_frequency[None, :] % map_width).astype(jnp.float32) * (
        2.0 * math.pi / map_width
    )
    c_cos = jnp.cos(coarse_angles)[:, None, :]
    c_sin = jnp.sin(coarse_angles)[:, None, :]
    f_cos = jnp.cos(fine_angles)[None, :, :]
    f_sin = jnp.sin(fine_angles)[None, :, :]
    col_cos = (c_cos * f_cos - c_sin * f_sin).reshape(map_width, -1)
    col_sin = (c_sin * f_cos + c_cos * f_sin).reshape(map_width, -1)
    col_table = jnp.stack([col_cos, -col_sin], axis=1)
    col_table, permit = lax.optimization_barrier((col_table, permit))
    smooth = extended_2(permit, (("slab", 0),), 4)
    for sweep_index in range(3):
        smooth = smooth_once(smooth)
    grad_x, grad_y = gradient(smooth)
    scale = jnp.sqrt(grad_x * grad_x + grad_y * grad_y + 1.0)
    normal_x = grad_x / scale
    normal_y = grad_y / scale
    inverse = 1.0 / permit
    contrast = permit - inverse
    fields = jnp.stack(
        [
            permit,
            contrast * normal_x * normal_x,
            contrast * normal_x * normal_y,
            contrast * normal_y * normal_y,
        ]
    )
    half_spectra = jnp.einsum("kxy,ycn->kxcn", fields, col_table, precision=lax.Precision.HIGH)
    my_positions = my_index * slab_rows + jnp.arange(slab_rows, dtype=jnp.int32)
    partial_value = row_transform(half_spectra, my_positions, frequency, map_width)
    summed = line_sum(partial_value, my_index, devices)
    coef = summed / float(map_width * map_width)
    a_in = jnp.arange(padded_keep, dtype=jnp.int32)
    c_in = jnp.arange(half_keep, dtype=jnp.int32)
    b_out = jnp.arange(2 * LANES, dtype=jnp.int32)
    flip_rows = (a_in[None, :] == (KEEP - 1) - a_in[:, None]).astype(jnp.float32)
    keep_cols = ((c_in[:, None] == b_out[None, :]) & (b_out[None, :] < HARM)).astype(jnp.float32)
    mirror_cols = (
        (c_in[:, None] == (KEEP - 1) - b_out[None, :]) & (b_out[None, :] >= HARM)
    ).astype(jnp.float32)
    sign = jnp.array([1.0, -1.0], jnp.float32)[:, None, None, None]
    direct = jnp.einsum("skac,cb->skab", coef, keep_cols, precision=lax.Precision.HIGHEST)
    mirrored = jnp.einsum(
        "ad,skdc,cb->skab", flip_rows, coef, mirror_cols, precision=lax.Precision.HIGHEST
    )
    full = direct + sign * mirrored
    tables = jnp.stack(
        [full[:, 2], full[:, 0] - full[:, 3], full[:, 1] - full[:, 0], -full[:, 2]], axis=1
    )
    tables = jnp.stack(
        [tables[..., COPY_STEP * c : COPY_STEP * c + LANES] for c in range(COPIES)], axis=1
    )
    index = jnp.stack([my_index, devices]).astype(jnp.int32)
    return assemble(index, tables, ROWS_DEV)


def solution(mesh):
    placed = (P(("layer", "slab"), None),)
    return jax.shard_map(
        shards,
        mesh=mesh,
        in_specs=placed,
        out_specs=P(None, ("layer", "slab"), None),
        check_vma=False,
    )
```

```python
import functools
import itertools
import math

import jax
import jax.numpy as jnp
from jax import lax
from jax.experimental import pallas as pl
from jax.experimental.pallas import tpu as pltpu
from jax.sharding import PartitionSpec as P

HARM = 101
ROWS_DEV = 64
KEEP = 201
ORDERS = 10201
BLOCK_ROWS = 8
STEP_ROWS = 16
COPIES = 4
COPY_STEP = 28
LANES = 128


PERMITS = (1.0, 2.1, 4.0, 12.1)


def extended_2(block, sides, width):
    for axis, dim in sides:
        count = lax.axis_size(axis)
        forward = [(i, i + 1) for i in range(count - 1)]
        forward.append((count - 1, 0))
        backward = [(target, source) for source, target in forward]
        low = lax.ppermute(
            lax.slice_in_dim(block, block.shape[dim] - width, None, axis=dim), axis, forward
        )
        high = lax.ppermute(lax.slice_in_dim(block, 0, width, axis=dim), axis, backward)
        block = jnp.concatenate([low, block, high], axis=dim)
    return block


def permittivity(labels):
    total = jnp.zeros(labels.shape, jnp.float32)
    for index_value in range(4):
        total = total + jnp.where(
            labels == index_value, jnp.float32(PERMITS[index_value]), jnp.float32(0.0)
        )
    return total


def smooth_once(extended):
    middle = extended[1:-1]
    return (
        4.0 * middle
        + extended[:-2]
        + extended[2:]
        + jnp.roll(middle, 1, 1)
        + jnp.roll(middle, -1, 1)
    ) / 8.0


def gradient(extended):
    middle = extended[1:-1]
    grad_x = (extended[2:] - extended[:-2]) / 2.0
    grad_y = (jnp.roll(middle, -1, 1) - jnp.roll(middle, 1, 1)) / 2.0
    return (grad_x, grad_y)


def rim_rows(field_in):
    return extended_2(field_in, (("slab", 0),), 1)


def row_transform(spectra_in, start, count, frequency, map_width):
    fine_count = 16 if count % 16 == 0 else 1
    coarse = start + jnp.arange(count // fine_count, dtype=jnp.int32) * fine_count
    fine = jnp.arange(fine_count, dtype=jnp.int32)
    scale = 2.0 * math.pi / map_width
    c_angles = (frequency[:, None] * coarse[None, :] % map_width).astype(jnp.float32) * scale
    f_angles = (frequency[:, None] * fine[None, :] % map_width).astype(jnp.float32) * scale
    c_cos = jnp.cos(c_angles)[:, :, None]
    c_sin = jnp.sin(c_angles)[:, :, None]
    f_cos = jnp.cos(f_angles)[:, None, :]
    f_sin = jnp.sin(f_angles)[:, None, :]
    table_cos = (c_cos * f_cos - c_sin * f_sin).reshape(frequency.shape[0], count)
    table_sin = (c_sin * f_cos + c_cos * f_sin).reshape(frequency.shape[0], count)
    table = jnp.stack([table_cos, table_sin])
    products = jnp.einsum("smx,kxcn->skmcn", table, spectra_in, precision=lax.Precision.HIGH)
    real_part = products[0, :, :, 0] + products[1, :, :, 1]
    imag_part = products[0, :, :, 1] - products[1, :, :, 0]
    return jnp.stack([real_part, imag_part])


def chunk_segments(total, half):
    chunks = []
    for start in range(0, total, LANES):
        width = min(LANES, total - start)
        runs = []
        for lane in range(width):
            flat = start + lane
            h, j = divmod(flat, half)
            u, v = divmod(j, HARM)
            if not runs or runs[-1][0] != h or runs[-1][1] != u:
                runs.append((h, u, lane, v))
        chunks.append((start, width, runs))
    return chunks


def assemble_kernel(index_ref, fl_ref, o_ref, z_ref):
    rb = pl.program_id(0)
    rows = o_ref.shape[1] * pl.num_programs(0)
    spacing = ORDERS // (rows * index_ref[1] // 2)
    centre = (HARM - 1) // 2
    span = z_ref.shape[-2] // BLOCK_ROWS - BLOCK_ROWS
    lane_iota = lax.broadcasted_iota(jnp.int32, (span, LANES), 1)
    sub = lax.broadcasted_iota(jnp.int32, (BLOCK_ROWS, LANES), 0)
    lane = lax.broadcasted_iota(jnp.int32, (BLOCK_ROWS, LANES), 1)
    for part, s in itertools.product(range(o_ref.shape[1] // BLOCK_ROWS), range(2)):
        z_part = z_ref.at[part, s]
        for rr in range(BLOCK_ROWS):
            row = rb * o_ref.shape[1] + part * BLOCK_ROWS + rr
            order_index = (index_ref[0] * rows + row) // 2 * spacing
            first = order_index // HARM
            second = order_index % HARM
            a0 = (HARM - 1) - first
            b0 = (HARM - 1) - second
            kx = 0.3 + 0.02 * (first - centre).astype(jnp.float32)
            ky = 0.2 + 0.02 * (second - centre).astype(jnp.float32)
            if rr % 2:
                diagonal = (ky * ky, -(kx * ky))
            else:
                diagonal = (kx * ky, -(kx * kx))
            copy = jnp.minimum(b0 // COPY_STEP, COPIES - 1)
            shift = (LANES - (b0 - COPY_STEP * copy)) % LANES
            base = pl.multiple_of(a0 // BLOCK_ROWS * BLOCK_ROWS, BLOCK_ROWS)
            off = a0 % BLOCK_ROWS
            dest = pl.multiple_of((BLOCK_ROWS - off) * BLOCK_ROWS, BLOCK_ROWS) + rr
            spot_tile = pl.multiple_of((first + BLOCK_ROWS) * BLOCK_ROWS, BLOCK_ROWS)
            spot = (sub == rr) & (lane == second)
            for h in range(2):
                combo = 2 * (rr % 2) + h
                x = fl_ref[s, copy, combo, pl.ds(base, span), :]
                x = pltpu.roll(x, shift, 1)
                z_part[h, pl.ds(dest, span, stride=BLOCK_ROWS), :] = x
                if s:
                    continue
                d = diagonal[h]
                tile = z_part[h, pl.ds(spot_tile, BLOCK_ROWS), :]
                z_part[h, pl.ds(spot_tile, BLOCK_ROWS), :] = tile + jnp.where(spot, d, jnp.float32(0.0))
        placed = {}
        for start, width, runs in chunk_segments(o_ref.shape[2], o_ref.shape[2] // 2):
            acc = None
            for h, u, l0, v0 in runs:
                if (h, u) not in placed:
                    src = z_part[h, pl.ds((u + BLOCK_ROWS) * BLOCK_ROWS, BLOCK_ROWS), :]
                    sh = (l0 - v0) % LANES
                    placed[(h, u)] = pltpu.roll(src, sh, 1) if sh else src
                src = placed[(h, u)]
                acc = src if acc is None else jnp.where(lane >= l0, src, acc)
            if width < LANES:
                acc = acc[:, :width]
            o_ref[s, pl.ds(part * BLOCK_ROWS, BLOCK_ROWS), pl.ds(start, width)] = acc


def assemble(index, tables, rows):
    span = 112
    n_blocks = rows // STEP_ROWS
    total = 2 * ORDERS
    grid_spec = pltpu.PrefetchScalarGridSpec(
        num_scalar_prefetch=1,
        grid=(n_blocks,),
        in_specs=[
            pl.BlockSpec(tables.shape, lambda rb, *_: (0, 0, 0, 0, 0)),
        ],
        out_specs=pl.BlockSpec((2, STEP_ROWS, total), lambda rb, *_: (0, rb, 0)),
        scratch_shapes=[
            pltpu.VMEM(
                (STEP_ROWS // BLOCK_ROWS, 2, 2, (span + BLOCK_ROWS) * BLOCK_ROWS, LANES), jnp.float32
            )
        ],
    )
    return pl.pallas_call(
        assemble_kernel,
        grid_spec=grid_spec,
        out_shape=jax.ShapeDtypeStruct((2, rows, total), jnp.float32),
        compiler_params=pltpu.CompilerParams(dimension_semantics=("arbitrary",)),
    )(index, tables)


def line_sum(partial_value, my_index, devices):
    core = my_index % 2
    pairs = [(i, i ^ 1) for i in range(devices)]
    half_shape = partial_value.shape[1:]
    dense = (-1, LANES) if math.prod(half_shape) % LANES == 0 else half_shape
    keep = jnp.where(core == 0, partial_value[0], partial_value[1]).reshape(dense)
    give = jnp.where(core == 0, partial_value[1], partial_value[0]).reshape(dense)
    mine = keep + lax.ppermute(give, "slab", pairs)
    chips = devices // 2
    if chips & (chips - 1) == 0 and chips > 1 and len(dense) == 2:
        rows = mine.shape[0]
        padded = -(-rows // 16) * 16
        grown = jnp.pad(mine, ((0, padded - rows), (0, 0)))
        upper = (my_index // 2) % 2
        halves = (grown[: padded // 2], grown[padded // 2 :])
        pair = [(i, i ^ 2) for i in range(devices)]
        kept = jnp.where(upper == 0, halves[0], halves[1])
        sent = jnp.where(upper == 0, halves[1], halves[0])
        kept = kept + lax.ppermute(sent, "slab", pair)
        bit = 4
        while bit < devices:
            kept = kept + lax.ppermute(kept, "slab", [(i, i ^ bit) for i in range(devices)])
            bit *= 2
        back = lax.ppermute(kept, "slab", pair)
        total = jnp.where(
            upper == 0, jnp.concatenate([kept, back]), jnp.concatenate([back, kept])
        )[:rows]
    else:
        right = [(i, i + 2) for i in range(devices - 2)]
        left = [(i + 2, i) for i in range(devices - 2)]
        from_left = jnp.zeros_like(mine)
        from_right = jnp.zeros_like(mine)
        for step in range(chips - 1):
            from_left, from_right = (
                lax.ppermute(mine + from_left, "slab", right),
                lax.ppermute(mine + from_right, "slab", left),
            )
        total = mine + from_left + from_right
    other = lax.ppermute(total, "slab", pairs).reshape(half_shape)
    total = total.reshape(half_shape)
    return jnp.where(core == 0, jnp.stack([total, other]), jnp.stack([other, total]))


def shards(labels):
    slab_rows = labels.shape[0]
    map_width = labels.shape[1]
    devices = lax.axis_size("slab")
    my_index = lax.axis_index("slab")
    permit = permittivity(labels)
    padded_keep = -(-KEEP // devices) * devices
    half_keep = -(-HARM // devices) * devices
    frequency = (HARM - 1) - jnp.arange(padded_keep, dtype=jnp.int32)
    col_frequency = (HARM - 1) - jnp.arange(half_keep, dtype=jnp.int32)
    fine_count = 64 if map_width % 64 == 0 else 1
    coarse = jnp.arange(map_width // fine_count, dtype=jnp.int32) * fine_count
    fine = jnp.arange(fine_count, dtype=jnp.int32)
    coarse_angles = (coarse[:, None] * col_frequency[None, :] % map_width).astype(jnp.float32) * (
        2.0 * math.pi / map_width
    )
    fine_angles = (fine[:, None] * col_frequency[None, :] % map_width).astype(jnp.float32) * (
        2.0 * math.pi / map_width
    )
    c_cos = jnp.cos(coarse_angles)[:, None, :]
    c_sin = jnp.sin(coarse_angles)[:, None, :]
    f_cos = jnp.cos(fine_angles)[None, :, :]
    f_sin = jnp.sin(fine_angles)[None, :, :]
    col_cos = (c_cos * f_cos - c_sin * f_sin).reshape(map_width, -1)
    col_sin = (c_sin * f_cos + c_cos * f_sin).reshape(map_width, -1)
    col_table = jnp.stack([col_cos, -col_sin], axis=1)
    col_table, permit = lax.optimization_barrier((col_table, permit))
    smooth = extended_2(permit, (("slab", 0),), 4)
    for sweep_index in range(3):
        smooth = smooth_once(smooth)
    grad_x, grad_y = gradient(smooth)
    scale = jnp.sqrt(grad_x * grad_x + grad_y * grad_y + 1.0)
    normal_x = grad_x / scale
    normal_y = grad_y / scale
    inverse = 1.0 / permit
    contrast = permit - inverse
    fields = jnp.stack(
        [
            permit,
            contrast * normal_x * normal_x,
            contrast * normal_x * normal_y,
            contrast * normal_y * normal_y,
        ]
    )
    half_spectra = jnp.einsum("kxy,ycn->kxcn", fields, col_table, precision=lax.Precision.HIGH)
    partial_value = row_transform(half_spectra, my_index * slab_rows, slab_rows, frequency, map_width)
    summed = line_sum(partial_value, my_index, devices)
    coef = summed / float(map_width * map_width)
    a_in = jnp.arange(padded_keep, dtype=jnp.int32)
    c_in = jnp.arange(half_keep, dtype=jnp.int32)
    b_out = jnp.arange(2 * LANES, dtype=jnp.int32)
    flip_rows = (a_in[None, :] == (KEEP - 1) - a_in[:, None]).astype(jnp.float32)
    keep_cols = ((c_in[:, None] == b_out[None, :]) & (b_out[None, :] < HARM)).astype(jnp.float32)
    mirror_cols = (
        (c_in[:, None] == (KEEP - 1) - b_out[None, :]) & (b_out[None, :] >= HARM)
    ).astype(jnp.float32)
    sign = jnp.array([1.0, -1.0], jnp.float32)[:, None, None, None]
    direct = jnp.einsum("skac,cb->skab", coef, keep_cols, precision=lax.Precision.HIGHEST)
    mirrored = jnp.einsum(
        "ad,skdc,cb->skab", flip_rows, coef, mirror_cols, precision=lax.Precision.HIGHEST
    )
    full = direct + sign * mirrored
    tables = jnp.stack(
        [full[:, 2], full[:, 0] - full[:, 3], full[:, 1] - full[:, 0], -full[:, 2]], axis=1
    )
    tables = jnp.stack(
        [tables[..., COPY_STEP * c : COPY_STEP * c + LANES] for c in range(COPIES)], axis=1
    )
    index = jnp.stack([my_index, devices]).astype(jnp.int32)
    return assemble(index, tables, ROWS_DEV)


def solution(mesh):
    placed = (P(("layer", "slab"), None),)
    return jax.shard_map(
        shards,
        mesh=mesh,
        in_specs=placed,
        out_specs=P(None, ("layer", "slab"), None),
        check_vma=False,
    )
```

```python
import functools
import itertools
import math

import jax
import jax.numpy as jnp
from jax import lax
from jax.experimental import pallas as pl
from jax.experimental.pallas import tpu as pltpu
from jax.sharding import PartitionSpec as P

HARM = 101
ROWS_DEV = 64
KEEP = 201
ORDERS = 10201
BLOCK_ROWS = 8
STEP_ROWS = 16
COPIES = 4
COPY_STEP = 28
LANES = 128


PERMITS = (1.0, 2.1, 4.0, 12.1)


def extended_2(block, sides, width):
    for axis, dim in sides:
        count = lax.axis_size(axis)
        forward = [(i, i + 1) for i in range(count - 1)]
        forward.append((count - 1, 0))
        backward = [(target, source) for source, target in forward]
        low = lax.ppermute(
            lax.slice_in_dim(block, block.shape[dim] - width, None, axis=dim), axis, forward
        )
        high = lax.ppermute(lax.slice_in_dim(block, 0, width, axis=dim), axis, backward)
        block = jnp.concatenate([low, block, high], axis=dim)
    return block


def permittivity(labels):
    total = jnp.zeros(labels.shape, jnp.float32)
    for index_value in range(4):
        total = total + jnp.where(
            labels == index_value, jnp.float32(PERMITS[index_value]), jnp.float32(0.0)
        )
    return total


def smooth_once(extended):
    middle = extended[1:-1]
    return (
        4.0 * middle
        + extended[:-2]
        + extended[2:]
        + jnp.roll(middle, 1, 1)
        + jnp.roll(middle, -1, 1)
    ) / 8.0


def gradient(extended):
    middle = extended[1:-1]
    grad_x = (extended[2:] - extended[:-2]) / 2.0
    grad_y = (jnp.roll(middle, -1, 1) - jnp.roll(middle, 1, 1)) / 2.0
    return (grad_x, grad_y)


def rim_rows(field_in):
    return extended_2(field_in, (("slab", 0),), 1)


def row_transform(spectra_in, start, count, frequency, map_width):
    fine_count = 16 if count % 16 == 0 else 1
    coarse = start + jnp.arange(count // fine_count, dtype=jnp.int32) * fine_count
    fine = jnp.arange(fine_count, dtype=jnp.int32)
    scale = 2.0 * math.pi / map_width
    c_angles = (frequency[:, None] * coarse[None, :] % map_width).astype(jnp.float32) * scale
    f_angles = (frequency[:, None] * fine[None, :] % map_width).astype(jnp.float32) * scale
    c_cos = jnp.cos(c_angles)[:, :, None]
    c_sin = jnp.sin(c_angles)[:, :, None]
    f_cos = jnp.cos(f_angles)[:, None, :]
    f_sin = jnp.sin(f_angles)[:, None, :]
    table_cos = (c_cos * f_cos - c_sin * f_sin).reshape(frequency.shape[0], count)
    table_sin = (c_sin * f_cos + c_cos * f_sin).reshape(frequency.shape[0], count)
    table = jnp.stack([table_cos, table_sin])
    products = jnp.einsum("smx,kxcn->skmcn", table, spectra_in, precision=lax.Precision.HIGH)
    real_part = products[0, :, :, 0] + products[1, :, :, 1]
    imag_part = products[0, :, :, 1] - products[1, :, :, 0]
    return jnp.stack([real_part, imag_part])


def chunk_segments(total, half):
    chunks = []
    for start in range(0, total, LANES):
        width = min(LANES, total - start)
        runs = []
        for lane in range(width):
            flat = start + lane
            h, j = divmod(flat, half)
            u, v = divmod(j, HARM)
            if not runs or runs[-1][0] != h or runs[-1][1] != u:
                runs.append((h, u, lane, v))
        chunks.append((start, width, runs))
    return chunks


def assemble_kernel(index_ref, fl_ref, o_ref, z_ref):
    rb = pl.program_id(0)
    rows = o_ref.shape[1] * pl.num_programs(0)
    spacing = ORDERS // (rows * index_ref[1] // 2)
    centre = (HARM - 1) // 2
    span = z_ref.shape[-2] // BLOCK_ROWS - BLOCK_ROWS
    lane_iota = lax.broadcasted_iota(jnp.int32, (span, LANES), 1)
    sub = lax.broadcasted_iota(jnp.int32, (BLOCK_ROWS, LANES), 0)
    lane = lax.broadcasted_iota(jnp.int32, (BLOCK_ROWS, LANES), 1)
    for part, s in itertools.product(range(o_ref.shape[1] // BLOCK_ROWS), range(2)):
        z_part = z_ref.at[part, s]
        for rr in range(BLOCK_ROWS):
            row = rb * o_ref.shape[1] + part * BLOCK_ROWS + rr
            order_index = (index_ref[0] * rows + row) // 2 * spacing
            first = order_index // HARM
            second = order_index % HARM
            a0 = (HARM - 1) - first
            b0 = (HARM - 1) - second
            kx = 0.3 + 0.02 * (first - centre).astype(jnp.float32)
            ky = 0.2 + 0.02 * (second - centre).astype(jnp.float32)
            if rr % 2:
                diagonal = (ky * ky, -(kx * ky))
            else:
                diagonal = (kx * ky, -(kx * kx))
            copy = jnp.minimum(b0 // COPY_STEP, COPIES - 1)
            shift = (LANES - (b0 - COPY_STEP * copy)) % LANES
            base = pl.multiple_of(a0 // BLOCK_ROWS * BLOCK_ROWS, BLOCK_ROWS)
            off = a0 % BLOCK_ROWS
            dest = pl.multiple_of((BLOCK_ROWS - off) * BLOCK_ROWS, BLOCK_ROWS) + rr
            spot_tile = pl.multiple_of((first + BLOCK_ROWS) * BLOCK_ROWS, BLOCK_ROWS)
            spot = (sub == rr) & (lane == second)
            for h in range(2):
                combo = 2 * (rr % 2) + h
                x = fl_ref[s, copy, combo, pl.ds(base, span), :]
                x = pltpu.roll(x, shift, 1)
                z_part[h, pl.ds(dest, span, stride=BLOCK_ROWS), :] = x
                if s:
                    continue
                d = diagonal[h]
                tile = z_part[h, pl.ds(spot_tile, BLOCK_ROWS), :]
                z_part[h, pl.ds(spot_tile, BLOCK_ROWS), :] = tile + jnp.where(spot, d, jnp.float32(0.0))
        placed = {}
        for start, width, runs in chunk_segments(o_ref.shape[2], o_ref.shape[2] // 2):
            acc = None
            for h, u, l0, v0 in runs:
                if (h, u) not in placed:
                    src = z_part[h, pl.ds((u + BLOCK_ROWS) * BLOCK_ROWS, BLOCK_ROWS), :]
                    sh = (l0 - v0) % LANES
                    placed[(h, u)] = pltpu.roll(src, sh, 1) if sh else src
                src = placed[(h, u)]
                acc = src if acc is None else jnp.where(lane >= l0, src, acc)
            if width < LANES:
                acc = acc[:, :width]
            o_ref[s, pl.ds(part * BLOCK_ROWS, BLOCK_ROWS), pl.ds(start, width)] = acc


def assemble(index, tables, rows):
    span = 112
    n_blocks = rows // STEP_ROWS
    total = 2 * ORDERS
    grid_spec = pltpu.PrefetchScalarGridSpec(
        num_scalar_prefetch=1,
        grid=(n_blocks,),
        in_specs=[
            pl.BlockSpec(tables.shape, lambda rb, *_: (0, 0, 0, 0, 0)),
        ],
        out_specs=pl.BlockSpec((2, STEP_ROWS, total), lambda rb, *_: (0, rb, 0)),
        scratch_shapes=[
            pltpu.VMEM(
                (STEP_ROWS // BLOCK_ROWS, 2, 2, (span + BLOCK_ROWS) * BLOCK_ROWS, LANES), jnp.float32
            )
        ],
    )
    return pl.pallas_call(
        assemble_kernel,
        grid_spec=grid_spec,
        out_shape=jax.ShapeDtypeStruct((2, rows, total), jnp.float32),
        compiler_params=pltpu.CompilerParams(dimension_semantics=("arbitrary",)),
    )(index, tables)


def line_sum(partial_value, my_index, devices):
    core = my_index % 2
    pairs = [(i, i ^ 1) for i in range(devices)]
    half_shape = partial_value.shape[1:]
    dense = (-1, LANES) if math.prod(half_shape) % LANES == 0 else half_shape
    keep = jnp.where(core == 0, partial_value[0], partial_value[1]).reshape(dense)
    give = jnp.where(core == 0, partial_value[1], partial_value[0]).reshape(dense)
    mine = keep + lax.ppermute(give, "slab", pairs)
    chips = devices // 2
    if chips & (chips - 1) == 0 and chips > 1 and len(dense) == 2:
        rows = mine.shape[0]
        padded = -(-rows // 16) * 16
        grown = jnp.pad(mine, ((0, padded - rows), (0, 0)))
        upper = (my_index // 2) % 2
        halves = (grown[: padded // 2], grown[padded // 2 :])
        pair = [(i, i ^ 2) for i in range(devices)]
        kept = jnp.where(upper == 0, halves[0], halves[1])
        sent = jnp.where(upper == 0, halves[1], halves[0])
        kept = kept + lax.ppermute(sent, "slab", pair)
        bit = 4
        while bit < devices:
            kept = kept + lax.ppermute(kept, "slab", [(i, i ^ bit) for i in range(devices)])
            bit *= 2
        back = lax.ppermute(kept, "slab", pair)
        total = jnp.where(
            upper == 0, jnp.concatenate([kept, back]), jnp.concatenate([back, kept])
        )[:rows]
    else:
        right = [(i, i + 2) for i in range(devices - 2)]
        left = [(i + 2, i) for i in range(devices - 2)]
        from_left = jnp.zeros_like(mine)
        from_right = jnp.zeros_like(mine)
        for step in range(chips - 1):
            from_left, from_right = (
                lax.ppermute(mine + from_left, "slab", right),
                lax.ppermute(mine + from_right, "slab", left),
            )
        total = mine + from_left + from_right
    other = lax.ppermute(total, "slab", pairs).reshape(half_shape)
    total = total.reshape(half_shape)
    return jnp.where(core == 0, jnp.stack([total, other]), jnp.stack([other, total]))


def shards(labels):
    slab_rows = labels.shape[0]
    map_width = labels.shape[1]
    devices = lax.axis_size("slab")
    my_index = lax.axis_index("slab")
    permit = permittivity(labels)
    padded_keep = -(-KEEP // devices) * devices
    half_keep = -(-HARM // devices) * devices
    frequency = (HARM - 1) - jnp.arange(padded_keep, dtype=jnp.int32)
    col_frequency = (HARM - 1) - jnp.arange(half_keep, dtype=jnp.int32)
    fine_count = 64 if map_width % 64 == 0 else 1
    coarse = jnp.arange(map_width // fine_count, dtype=jnp.int32) * fine_count
    fine = jnp.arange(fine_count, dtype=jnp.int32)
    coarse_angles = (coarse[:, None] * col_frequency[None, :] % map_width).astype(jnp.float32) * (
        2.0 * math.pi / map_width
    )
    fine_angles = (fine[:, None] * col_frequency[None, :] % map_width).astype(jnp.float32) * (
        2.0 * math.pi / map_width
    )
    c_cos = jnp.cos(coarse_angles)[:, None, :]
    c_sin = jnp.sin(coarse_angles)[:, None, :]
    f_cos = jnp.cos(fine_angles)[None, :, :]
    f_sin = jnp.sin(fine_angles)[None, :, :]
    col_cos = (c_cos * f_cos - c_sin * f_sin).reshape(map_width, -1)
    col_sin = (c_sin * f_cos + c_cos * f_sin).reshape(map_width, -1)
    col_table = jnp.stack([col_cos, -col_sin], axis=1)
    col_table, permit = lax.optimization_barrier((col_table, permit))
    smooth = extended_2(permit, (("slab", 0),), 4)
    for sweep_index in range(3):
        smooth = smooth_once(smooth)
    grad_x, grad_y = gradient(smooth)
    scale = jnp.sqrt(grad_x * grad_x + grad_y * grad_y + 1.0)
    normal_x = grad_x / scale
    normal_y = grad_y / scale
    inverse = 1.0 / permit
    contrast = permit - inverse
    fields = jnp.stack(
        [
            permit,
            contrast * normal_x * normal_x,
            contrast * normal_x * normal_y,
            contrast * normal_y * normal_y,
        ]
    )
    half_spectra = jnp.einsum("kxy,ycn->kxcn", fields, col_table, precision=lax.Precision.HIGH)
    partial_value = row_transform(half_spectra, my_index * slab_rows, slab_rows, frequency, map_width)
    summed = line_sum(partial_value, my_index, devices)
    coef = summed / float(map_width * map_width)
    a_in = jnp.arange(padded_keep, dtype=jnp.int32)
    c_in = jnp.arange(half_keep, dtype=jnp.int32)
    b_out = jnp.arange(2 * LANES, dtype=jnp.int32)
    flip_rows = (a_in[None, :] == (KEEP - 1) - a_in[:, None]).astype(jnp.float32)
    keep_cols = ((c_in[:, None] == b_out[None, :]) & (b_out[None, :] < HARM)).astype(jnp.float32)
    mirror_cols = (
        (c_in[:, None] == (KEEP - 1) - b_out[None, :]) & (b_out[None, :] >= HARM)
    ).astype(jnp.float32)
    sign = jnp.array([1.0, -1.0], jnp.float32)[:, None, None, None]
    blocks = jnp.stack(
        [coef[:, 2], coef[:, 0] - coef[:, 3], coef[:, 1] - coef[:, 0], -coef[:, 2]], axis=1
    )
    direct = jnp.einsum("skac,cb->skab", blocks, keep_cols, precision=lax.Precision.HIGHEST)
    mirrored = jnp.einsum(
        "ad,skdc,cb->skab", flip_rows, blocks, mirror_cols, precision=lax.Precision.HIGHEST
    )
    tables = direct + sign * mirrored
    tables = jnp.stack(
        [tables[..., COPY_STEP * c : COPY_STEP * c + LANES] for c in range(COPIES)], axis=1
    )
    index = jnp.stack([my_index, devices]).astype(jnp.int32)
    return assemble(index, tables, ROWS_DEV)


def solution(mesh):
    placed = (P(("layer", "slab"), None),)
    return jax.shard_map(
        shards,
        mesh=mesh,
        in_specs=placed,
        out_specs=P(None, ("layer", "slab"), None),
        check_vma=False,
    )
```

```python
import functools
import itertools
import math

import jax
import jax.numpy as jnp
from jax import lax
from jax.experimental import pallas as pl
from jax.experimental.pallas import tpu as pltpu
from jax.sharding import PartitionSpec as P

HARM = 101
ROWS_DEV = 64
KEEP = 201
ORDERS = 10201
BLOCK_ROWS = 8
STEP_ROWS = 16
COPIES = 4
COPY_STEP = 28
LANES = 128


PERMITS = (1.0, 2.1, 4.0, 12.1)


def extended_2(block, sides, width):
    for axis, dim in sides:
        count = lax.axis_size(axis)
        forward = [(i, i + 1) for i in range(count - 1)]
        forward.append((count - 1, 0))
        backward = [(target, source) for source, target in forward]
        low = lax.ppermute(
            lax.slice_in_dim(block, block.shape[dim] - width, None, axis=dim), axis, forward
        )
        high = lax.ppermute(lax.slice_in_dim(block, 0, width, axis=dim), axis, backward)
        block = jnp.concatenate([low, block, high], axis=dim)
    return block


def permittivity(labels):
    total = jnp.zeros(labels.shape, jnp.float32)
    for index_value in range(4):
        total = total + jnp.where(
            labels == index_value, jnp.float32(PERMITS[index_value]), jnp.float32(0.0)
        )
    return total


def smooth_once(extended):
    middle = extended[1:-1]
    return (
        4.0 * middle
        + extended[:-2]
        + extended[2:]
        + jnp.roll(middle, 1, 1)
        + jnp.roll(middle, -1, 1)
    ) / 8.0


def gradient(extended):
    middle = extended[1:-1]
    grad_x = (extended[2:] - extended[:-2]) / 2.0
    grad_y = (jnp.roll(middle, -1, 1) - jnp.roll(middle, 1, 1)) / 2.0
    return (grad_x, grad_y)


def rim_rows(field_in):
    return extended_2(field_in, (("slab", 0),), 1)


def row_transform(spectra_in, start, count, frequency, map_width):
    fine_count = 16 if count % 16 == 0 else 1
    coarse = start + jnp.arange(count // fine_count, dtype=jnp.int32) * fine_count
    fine = jnp.arange(fine_count, dtype=jnp.int32)
    scale = 2.0 * math.pi / map_width
    c_angles = (frequency[:, None] * coarse[None, :] % map_width).astype(jnp.float32) * scale
    f_angles = (frequency[:, None] * fine[None, :] % map_width).astype(jnp.float32) * scale
    c_cos = jnp.cos(c_angles)[:, :, None]
    c_sin = jnp.sin(c_angles)[:, :, None]
    f_cos = jnp.cos(f_angles)[:, None, :]
    f_sin = jnp.sin(f_angles)[:, None, :]
    table_cos = (c_cos * f_cos - c_sin * f_sin).reshape(frequency.shape[0], count)
    table_sin = (c_sin * f_cos + c_cos * f_sin).reshape(frequency.shape[0], count)
    table = jnp.stack([table_cos, table_sin])
    products = jnp.einsum("smx,kxcn->skmcn", table, spectra_in, precision=lax.Precision.HIGH)
    real_part = products[0, :, :, 0] + products[1, :, :, 1]
    imag_part = products[0, :, :, 1] - products[1, :, :, 0]
    return jnp.stack([real_part, imag_part])


def chunk_segments(total, half):
    chunks = []
    for start in range(0, total, LANES):
        width = min(LANES, total - start)
        runs = []
        for lane in range(width):
            flat = start + lane
            h, j = divmod(flat, half)
            u, v = divmod(j, HARM)
            if not runs or runs[-1][0] != h or runs[-1][1] != u:
                runs.append((h, u, lane, v))
        chunks.append((start, width, runs))
    return chunks


def assemble_kernel(devices, fl_ref, o_ref, z_ref):
    rb = pl.program_id(0)
    rows = o_ref.shape[1] * pl.num_programs(0)
    spacing = ORDERS // (rows * devices // 2)
    my_index = lax.axis_index("slab")
    centre = (HARM - 1) // 2
    span = z_ref.shape[-2] // BLOCK_ROWS - BLOCK_ROWS
    lane_iota = lax.broadcasted_iota(jnp.int32, (span, LANES), 1)
    sub = lax.broadcasted_iota(jnp.int32, (BLOCK_ROWS, LANES), 0)
    lane = lax.broadcasted_iota(jnp.int32, (BLOCK_ROWS, LANES), 1)
    for part, s in itertools.product(range(o_ref.shape[1] // BLOCK_ROWS), range(2)):
        z_part = z_ref.at[part, s]
        for rr in range(BLOCK_ROWS):
            row = rb * o_ref.shape[1] + part * BLOCK_ROWS + rr
            order_index = (my_index * rows + row) // 2 * spacing
            first = order_index // HARM
            second = order_index % HARM
            a0 = (HARM - 1) - first
            b0 = (HARM - 1) - second
            kx = 0.3 + 0.02 * (first - centre).astype(jnp.float32)
            ky = 0.2 + 0.02 * (second - centre).astype(jnp.float32)
            if rr % 2:
                diagonal = (ky * ky, -(kx * ky))
            else:
                diagonal = (kx * ky, -(kx * kx))
            copy = jnp.minimum(b0 // COPY_STEP, COPIES - 1)
            shift = (LANES - (b0 - COPY_STEP * copy)) % LANES
            base = pl.multiple_of(a0 // BLOCK_ROWS * BLOCK_ROWS, BLOCK_ROWS)
            off = a0 % BLOCK_ROWS
            dest = pl.multiple_of((BLOCK_ROWS - off) * BLOCK_ROWS, BLOCK_ROWS) + rr
            spot_tile = pl.multiple_of((first + BLOCK_ROWS) * BLOCK_ROWS, BLOCK_ROWS)
            spot = (sub == rr) & (lane == second)
            for h in range(2):
                combo = 2 * (rr % 2) + h
                x = fl_ref[s, copy, combo, pl.ds(base, span), :]
                x = pltpu.roll(x, shift, 1)
                z_part[h, pl.ds(dest, span, stride=BLOCK_ROWS), :] = x
                if s:
                    continue
                d = diagonal[h]
                tile = z_part[h, pl.ds(spot_tile, BLOCK_ROWS), :]
                z_part[h, pl.ds(spot_tile, BLOCK_ROWS), :] = tile + jnp.where(spot, d, jnp.float32(0.0))
        placed = {}
        for start, width, runs in chunk_segments(o_ref.shape[2], o_ref.shape[2] // 2):
            acc = None
            for h, u, l0, v0 in runs:
                if (h, u) not in placed:
                    src = z_part[h, pl.ds((u + BLOCK_ROWS) * BLOCK_ROWS, BLOCK_ROWS), :]
                    sh = (l0 - v0) % LANES
                    placed[(h, u)] = pltpu.roll(src, sh, 1) if sh else src
                src = placed[(h, u)]
                acc = src if acc is None else jnp.where(lane >= l0, src, acc)
            if width < LANES:
                acc = acc[:, :width]
            o_ref[s, pl.ds(part * BLOCK_ROWS, BLOCK_ROWS), pl.ds(start, width)] = acc


def assemble(devices, tables, rows):
    span = 112
    n_blocks = rows // STEP_ROWS
    total = 2 * ORDERS
    grid_spec = pl.GridSpec(
        grid=(n_blocks,),
        in_specs=[
            pl.BlockSpec(tables.shape, lambda rb: (0, 0, 0, 0, 0)),
        ],
        out_specs=pl.BlockSpec((2, STEP_ROWS, total), lambda rb: (0, rb, 0)),
        scratch_shapes=[
            pltpu.VMEM(
                (STEP_ROWS // BLOCK_ROWS, 2, 2, (span + BLOCK_ROWS) * BLOCK_ROWS, LANES), jnp.float32
            )
        ],
    )
    return pl.pallas_call(
        functools.partial(assemble_kernel, devices),
        grid_spec=grid_spec,
        out_shape=jax.ShapeDtypeStruct((2, rows, total), jnp.float32),
        compiler_params=pltpu.CompilerParams(dimension_semantics=("arbitrary",)),
    )(tables)


def line_sum(partial_value, my_index, devices):
    core = my_index % 2
    pairs = [(i, i ^ 1) for i in range(devices)]
    half_shape = partial_value.shape[1:]
    dense = (-1, LANES) if math.prod(half_shape) % LANES == 0 else half_shape
    keep = jnp.where(core == 0, partial_value[0], partial_value[1]).reshape(dense)
    give = jnp.where(core == 0, partial_value[1], partial_value[0]).reshape(dense)
    mine = keep + lax.ppermute(give, "slab", pairs)
    chips = devices // 2
    if chips & (chips - 1) == 0 and chips > 1 and len(dense) == 2:
        rows = mine.shape[0]
        padded = -(-rows // 16) * 16
        grown = jnp.pad(mine, ((0, padded - rows), (0, 0)))
        upper = (my_index // 2) % 2
        halves = (grown[: padded // 2], grown[padded // 2 :])
        pair = [(i, i ^ 2) for i in range(devices)]
        kept = jnp.where(upper == 0, halves[0], halves[1])
        sent = jnp.where(upper == 0, halves[1], halves[0])
        kept = kept + lax.ppermute(sent, "slab", pair)
        bit = 4
        while bit < devices:
            kept = kept + lax.ppermute(kept, "slab", [(i, i ^ bit) for i in range(devices)])
            bit *= 2
        back = lax.ppermute(kept, "slab", pair)
        total = jnp.where(
            upper == 0, jnp.concatenate([kept, back]), jnp.concatenate([back, kept])
        )[:rows]
    else:
        right = [(i, i + 2) for i in range(devices - 2)]
        left = [(i + 2, i) for i in range(devices - 2)]
        from_left = jnp.zeros_like(mine)
        from_right = jnp.zeros_like(mine)
        for step in range(chips - 1):
            from_left, from_right = (
                lax.ppermute(mine + from_left, "slab", right),
                lax.ppermute(mine + from_right, "slab", left),
            )
        total = mine + from_left + from_right
    other = lax.ppermute(total, "slab", pairs).reshape(half_shape)
    total = total.reshape(half_shape)
    return jnp.where(core == 0, jnp.stack([total, other]), jnp.stack([other, total]))


def shards(labels):
    slab_rows = labels.shape[0]
    map_width = labels.shape[1]
    devices = lax.axis_size("slab")
    my_index = lax.axis_index("slab")
    permit = permittivity(labels)
    padded_keep = -(-KEEP // devices) * devices
    half_keep = -(-HARM // devices) * devices
    frequency = (HARM - 1) - jnp.arange(padded_keep, dtype=jnp.int32)
    col_frequency = (HARM - 1) - jnp.arange(half_keep, dtype=jnp.int32)
    fine_count = 64 if map_width % 64 == 0 else 1
    coarse = jnp.arange(map_width // fine_count, dtype=jnp.int32) * fine_count
    fine = jnp.arange(fine_count, dtype=jnp.int32)
    coarse_angles = (coarse[:, None] * col_frequency[None, :] % map_width).astype(jnp.float32) * (
        2.0 * math.pi / map_width
    )
    fine_angles = (fine[:, None] * col_frequency[None, :] % map_width).astype(jnp.float32) * (
        2.0 * math.pi / map_width
    )
    c_cos = jnp.cos(coarse_angles)[:, None, :]
    c_sin = jnp.sin(coarse_angles)[:, None, :]
    f_cos = jnp.cos(fine_angles)[None, :, :]
    f_sin = jnp.sin(fine_angles)[None, :, :]
    col_cos = (c_cos * f_cos - c_sin * f_sin).reshape(map_width, -1)
    col_sin = (c_sin * f_cos + c_cos * f_sin).reshape(map_width, -1)
    col_table = jnp.stack([col_cos, -col_sin], axis=1)
    col_table, permit = lax.optimization_barrier((col_table, permit))
    smooth = extended_2(permit, (("slab", 0),), 4)
    for sweep_index in range(3):
        smooth = smooth_once(smooth)
    grad_x, grad_y = gradient(smooth)
    scale = jnp.sqrt(grad_x * grad_x + grad_y * grad_y + 1.0)
    normal_x = grad_x / scale
    normal_y = grad_y / scale
    inverse = 1.0 / permit
    contrast = permit - inverse
    fields = jnp.stack(
        [
            permit,
            contrast * normal_x * normal_x,
            contrast * normal_x * normal_y,
            contrast * normal_y * normal_y,
        ]
    )
    half_spectra = jnp.einsum("kxy,ycn->kxcn", fields, col_table, precision=lax.Precision.HIGH)
    partial_value = row_transform(half_spectra, my_index * slab_rows, slab_rows, frequency, map_width)
    summed = line_sum(partial_value, my_index, devices)
    coef = summed / float(map_width * map_width)
    a_in = jnp.arange(padded_keep, dtype=jnp.int32)
    c_in = jnp.arange(half_keep, dtype=jnp.int32)
    b_out = jnp.arange(2 * LANES, dtype=jnp.int32)
    flip_rows = (a_in[None, :] == (KEEP - 1) - a_in[:, None]).astype(jnp.float32)
    keep_cols = ((c_in[:, None] == b_out[None, :]) & (b_out[None, :] < HARM)).astype(jnp.float32)
    mirror_cols = (
        (c_in[:, None] == (KEEP - 1) - b_out[None, :]) & (b_out[None, :] >= HARM)
    ).astype(jnp.float32)
    sign = jnp.array([1.0, -1.0], jnp.float32)[:, None, None, None]
    blocks = jnp.stack(
        [coef[:, 2], coef[:, 0] - coef[:, 3], coef[:, 1] - coef[:, 0], -coef[:, 2]], axis=1
    )
    direct = jnp.einsum("skac,cb->skab", blocks, keep_cols, precision=lax.Precision.HIGHEST)
    mirrored = jnp.einsum(
        "ad,skdc,cb->skab", flip_rows, blocks, mirror_cols, precision=lax.Precision.HIGHEST
    )
    tables = direct + sign * mirrored
    tables = jnp.stack(
        [tables[..., COPY_STEP * c : COPY_STEP * c + LANES] for c in range(COPIES)], axis=1
    )
    return assemble(devices, tables, ROWS_DEV)


def solution(mesh):
    placed = (P(("layer", "slab"), None),)
    return jax.shard_map(
        shards,
        mesh=mesh,
        in_specs=placed,
        out_specs=P(None, ("layer", "slab"), None),
        check_vma=False,
    )
```
